32 devices in a mesh: src: 8 (over z, y), vox: 4 (over x, core).
Axes of the slice: x: 2, y: 2, z: 4, core: 2. Of those that a mesh axis runs over, the one named last changes fastest.
Arguments:
- forward_voxel_field: bfloat16 [4096, 4096], P('src', 'vox'), may hold values from -0.09375 to 0.09375
- adjoint_voxel_field: bfloat16 [4096, 4096], P('src', 'vox'), may hold values from -6 to 6
- voxel_input_vector: float32 [4096], P('vox'), may hold values from -6 to 6
- measurement_weight: float32 [4096, 4096], P('src', 'vox'), may hold values from 0.00390625 to 0.0390625
Outputs:
- hess_vector: float32 [4096], P('vox')
The draws below stay inside these ranges and needn't reach their ends.
All inputs are finite; a program needn't handle non-finite values.
Results may differ from the reference program's by a relative error of at most 0.00056.
Values may be sent and summed in bfloat16 or wider, within the bound.
No kernel may reach another device: no remote copies, remote signals or barrier semaphores. Data moves between devices by JAX's collectives and lax.ppermute only.
A program may use at most 64 MiB of HBM per device.

```python
import math
import jax
import jax.numpy as jnp
from jax import lax

SOURCE_COUNT = 4096
DETECTOR_COUNT = 4096
V = 4096


def steps_of(own_key, shape, split, low, largest):
    factor_of = 1.0
    for dim, parts in split:
        heights = jax.random.uniform(jax.random.fold_in(jax.random.fold_in(own_key, 6), dim), (parts,), jnp.float32, low / len(split), largest / len(split))
        factor_of = factor_of * jnp.repeat(jnp.exp(heights), shape[dim] // parts).reshape((-1,) + (1,) * (len(shape) - 1 - dim))
    return factor_of


def centred(rng, dims, deviation, most, shards=(), held_as=jnp.bfloat16):
    loudness = steps_of(rng, dims, shards, -0.22, 0.18) if shards else 1.0
    entries = jax.random.normal(rng, dims, jnp.float32) * deviation * loudness
    return jnp.minimum(jnp.maximum(entries, -most), most).astype(held_as)


def setup_inputs(seed: int = 0) -> dict:
    streams_of = jax.random.split(jax.random.key(seed), 5)
    forward_voxel_field = centred(streams_of[0], (SOURCE_COUNT, V), V ** -0.5, 0.09375, ((0, 8), (1, 4)))
    adjoint_voxel_field = centred(streams_of[1], (DETECTOR_COUNT, V), 1.0, 6.0, ((0, 8), (1, 4)))
    voxel_input_vector = centred(streams_of[2], (V,), 1.0, 6.0, ((0, 4),), jnp.float32)
    measurement_weight = jnp.clip(jnp.exp(math.log(0.0390625) - 2.3025851 * jax.random.uniform(streams_of[3], (SOURCE_COUNT, DETECTOR_COUNT), jnp.float32) ** steps_of(streams_of[3], (SOURCE_COUNT, DETECTOR_COUNT), ((0, 8), (1, 4)), -0.2, 0.2)), 0.00390625, 0.0390625)
    return {"forward_voxel_field": forward_voxel_field, "adjoint_voxel_field": adjoint_voxel_field, "voxel_input_vector": voxel_input_vector, "measurement_weight": measurement_weight}


def reference(forward_voxel_field, adjoint_voxel_field, voxel_input_vector, measurement_weight):
    scaled = (forward_voxel_field.astype(jnp.float32) * voxel_input_vector[None, :]).astype(jnp.bfloat16)
    predicted_signal = lax.dot_general(scaled, adjoint_voxel_field, (((1,), (1,)), ((), ())), preferred_element_type=jnp.float32)
    weighted_signal = (measurement_weight * predicted_signal).astype(jnp.bfloat16)
    back = jnp.dot(weighted_signal, adjoint_voxel_field, preferred_element_type=jnp.float32)
    return jnp.sum(forward_voxel_field.astype(jnp.float32) * back, axis=0)
```

```python
import jax
import jax.numpy as jnp
from jax import lax
from jax.sharding import PartitionSpec as P


def _reduce_scatter_vox(part):
    vox = lax.axis_size("vox")
    me = lax.axis_index("vox")
    sl, d = part.shape
    db = d // vox
    m = vox // 2
    par = me % 2
    q = me // 2
    blocks = part.reshape(sl, m, 2, db)
    keep = lax.dynamic_index_in_dim(blocks, par, axis=2, keepdims=False)
    send = lax.dynamic_index_in_dim(blocks, 1 - par, axis=2, keepdims=False)
    pair = [(j, j ^ 1) for j in range(vox)]
    half = keep + lax.ppermute(send, "vox", pair)
    out = lax.dynamic_index_in_dim(half, q, axis=1, keepdims=False)
    for k in range(1, m):
        piece = lax.dynamic_index_in_dim(half, (q + k) % m, axis=1, keepdims=False)
        perm = [(g * 2 + p, ((g + k) % m) * 2 + p) for g in range(m) for p in range(2)]
        out = out + lax.ppermute(piece.astype(jnp.bfloat16), "vox", perm).astype(jnp.float32)
    return out


def _sum_over_src(v):
    n = lax.axis_size("src")
    if n & (n - 1):
        return lax.psum(v, "src")
    b = 1
    while b < n:
        v = v + lax.ppermute(v, "src", [(i, i ^ b) for i in range(n)])
        b *= 2
    return v


def per_device(forward_voxel_field, adjoint_voxel_field, voxel_input_vector, measurement_weight):
    scaled = (forward_voxel_field.astype(jnp.float32) * voxel_input_vector[None, :]).astype(
        jnp.bfloat16
    )
    adjoint_all = lax.all_gather(adjoint_voxel_field, "src", axis=0, tiled=True)
    predicted_part = lax.dot_general(
        scaled, adjoint_all, (((1,), (1,)), ((), ())), preferred_element_type=jnp.float32
    )
    pred_share = _reduce_scatter_vox(predicted_part)
    weighted_share = (measurement_weight * pred_share).astype(jnp.bfloat16)
    weighted_signal = lax.all_gather(weighted_share, "vox", axis=1, tiled=True)
    back = jnp.dot(weighted_signal, adjoint_all, preferred_element_type=jnp.float32)
    local_sum = jnp.sum(forward_voxel_field.astype(jnp.float32) * back, axis=0)
    return _sum_over_src(local_sum)


def solution(mesh):
    placed = (P("src", "vox"), P("src", "vox"), P("vox"), P("src", "vox"))
    return jax.shard_map(
        per_device, mesh=mesh, in_specs=placed, out_specs=P("vox"), check_vma=False
    )
```

```python
import jax
import jax.numpy as jnp
from jax import lax
from jax.sharding import PartitionSpec as P

CHUNKS = 4


def _rows(a, blk, n):
    return lax.dynamic_slice_in_dim(a, blk * n, n, axis=0)


def _sum_over_src(v):
    n = lax.axis_size("src")
    if n & (n - 1):
        return lax.psum(v, "src")
    b = 1
    while b < n:
        v = v + lax.ppermute(v, "src", [(i, i ^ b) for i in range(n)])
        b *= 2
    return v


def per_device(forward_voxel_field, adjoint_voxel_field, voxel_input_vector, measurement_weight):
    nsrc = lax.axis_size("src")
    vox = lax.axis_size("vox")
    me = lax.axis_index("vox")
    m = vox // 2
    par = me % 2
    q = me // 2
    t = nsrc // vox
    sl, vl = forward_voxel_field.shape
    ds = adjoint_voxel_field.shape[0]
    chunks = CHUNKS if ds % CHUNKS == 0 else 1
    r = ds // chunks
    n = t * r
    pair = [(j, j ^ 1) for j in range(vox)]

    def chip_perm(k):
        return [(g * 2 + p, ((g + k) % m) * 2 + p) for g in range(m) for p in range(2)]

    scaled = (forward_voxel_field.astype(jnp.float32) * voxel_input_vector[None, :]).astype(
        jnp.bfloat16
    )
    weight = measurement_weight.reshape(sl, t, ds)
    def gather(c):
        return lax.all_gather(adjoint_voxel_field[c * r:(c + 1) * r], "src", axis=0, tiled=True)

    back = jnp.zeros((sl, vl), jnp.float32)
    nxt = gather(0)
    for c in range(chunks):
        adj = nxt

        def pblock(blk):
            return lax.dot_general(
                scaled, _rows(adj, blk, n), (((1,), (1,)), ((), ())),
                preferred_element_type=jnp.float32,
            )

        halves = []
        for k in range(m):
            g = (q + k) % m
            keep = pblock(2 * g + par)
            send = pblock(2 * g + 1 - par)
            halves.append(keep + lax.ppermute(send, "vox", pair))
        share = halves[0]
        for k in range(1, m):
            share = share + lax.ppermute(
                halves[k].astype(jnp.bfloat16), "vox", chip_perm(k)
            ).astype(jnp.float32)

        w_c = weight[:, :, c * r:(c + 1) * r].reshape(sl, n)
        wt = (w_c * share).astype(jnp.bfloat16)

        got = [(me, wt)]
        for k in range(1, m):
            got.append((2 * ((q - k) % m) + par, lax.ppermute(wt, "vox", chip_perm(k))))
        got = got + [(blk ^ 1, lax.ppermute(w, "vox", pair)) for blk, w in got]
        if c + 1 < chunks:
            nxt, ws = lax.optimization_barrier((gather(c + 1), [w for _, w in got]))
            got = [(blk, w) for (blk, _), w in zip(got, ws)]
        for blk, w in got:
            back = back + jnp.dot(w, _rows(adj, blk, n), preferred_element_type=jnp.float32)

    local_sum = jnp.sum(forward_voxel_field.astype(jnp.float32) * back, axis=0)
    return _sum_over_src(local_sum)


def solution(mesh):
    placed = (P("src", "vox"), P("src", "vox"), P("vox"), P("src", "vox"))
    return jax.shard_map(
        per_device, mesh=mesh, in_specs=placed, out_specs=P("vox"), check_vma=False
    )
```

```python
import functools

import jax
import jax.numpy as jnp
from jax import lax
from jax.sharding import PartitionSpec as P

CHUNKS = 2


def _rows(a, blk, n):
    return lax.dynamic_slice_in_dim(a, blk * n, n, axis=0)


def _src_grid(mesh):
    devs = mesh.devices
    ax = mesh.axis_names.index("src")
    row = [devs[(i,) + (0,) * (devs.ndim - 1)] if ax == 0 else None for i in range(devs.shape[0])]
    if ax != 0 or any(not hasattr(d, "coords") for d in row):
        return None
    co = [tuple(d.coords) for d in row]
    n = len(co)
    diff = [k for k in range(len(co[0])) if n > 1 and co[1][k] != co[0][k]]
    if len(diff) != 1:
        return None
    nb = 1
    while nb < n and co[nb][diff[0]] != co[0][diff[0]]:
        nb += 1
    if n % nb:
        return None
    na = n // nb

    def near(i, j):
        return sum(abs(a - b) for a, b in zip(co[i], co[j])) == 1

    for i in range(n):
        ia, ib = divmod(i, nb)
        if ib + 1 < nb and not near(i, i + 1):
            return None
        if ia + 1 < na and not near(i, i + nb):
            return None
    return nb, na


def _line(block, pos, size, pairs_of):
    out = []
    for sign in (1, -1):
        cur = block
        for s in range(1, size):
            pairs = []
            for p in range(size):
                if 0 <= p + sign < size and 0 <= p - sign * (s - 1) < size:
                    pairs.extend(pairs_of(p, p + sign))
            cur = lax.ppermute(cur, "src", pairs)
            out.append((cur, pos - sign * s, sign, s))
    return out


def _valid(p, size, sign, s):
    return 0 <= p - sign * s < size


def _gather_src(block, grid):
    nsrc = lax.axis_size("src")
    if grid is None:
        return lax.all_gather(block, "src", axis=0, tiled=True)
    nb, na = grid
    me = lax.axis_index("src")
    ia, ib = me // nb, me % nb
    r = block.shape[0]
    if nb >= na:
        n1, p1, n2, p2 = nb, ib, na, ia

        def index(q1, q2):
            return q2 * nb + q1
    else:
        n1, p1, n2, p2 = na, ia, nb, ib

        def index(q1, q2):
            return q1 * nb + q2

    held = [(block, p1, None)] + [
        (arr, o1, (sign, s))
        for arr, o1, sign, s in _line(
            block, p1, n1, lambda p, d: [(index(p, o), index(d, o)) for o in range(n2)]
        )
    ]
    buf = jnp.zeros(((nsrc + 1) * r,) + block.shape[1:], block.dtype)
    for arr, o1, how in held:

        def ok1(q1, how=how):
            return how is None or _valid(q1, n1, *how)

        second = _line(
            arr, p2, n2,
            lambda p, d, ok1=ok1: [(index(o, p), index(o, d)) for o in range(n1) if ok1(o)],
        )
        for arr2, o2, how2 in [(arr, p2, None)] + [(a2, o, (sg, st)) for a2, o, sg, st in second]:
            good = (o1 >= 0) & (o1 < n1) & (o2 >= 0) & (o2 < n2)
            slot = jnp.where(good, index(o1, o2), nsrc)
            buf = lax.dynamic_update_slice_in_dim(buf, arr2, slot * r, axis=0)
    return buf[: nsrc * r]


def _sum_over_src(v):
    n = lax.axis_size("src")
    if n & (n - 1):
        return lax.psum(v, "src")
    b = 1
    while b < n:
        v = v + lax.ppermute(v, "src", [(i, i ^ b) for i in range(n)])
        b *= 2
    return v


def per_device(grid, forward_voxel_field, adjoint_voxel_field, voxel_input_vector, measurement_weight):
    nsrc = lax.axis_size("src")
    vox = lax.axis_size("vox")
    me = lax.axis_index("vox")
    m = vox // 2
    par = me % 2
    q = me // 2
    t = nsrc // vox
    sl, vl = forward_voxel_field.shape
    ds = adjoint_voxel_field.shape[0]
    chunks = CHUNKS if ds % CHUNKS == 0 else 1
    r = ds // chunks
    n = t * r
    pair = [(j, j ^ 1) for j in range(vox)]

    def chip_perm(k):
        return [(g * 2 + p, ((g + k) % m) * 2 + p) for g in range(m) for p in range(2)]

    scaled = (forward_voxel_field.astype(jnp.float32) * voxel_input_vector[None, :]).astype(
        jnp.bfloat16
    )
    weight = measurement_weight.reshape(sl, t, ds)
    def gather(c):
        return _gather_src(adjoint_voxel_field[c * r:(c + 1) * r], grid)

    back = jnp.zeros((sl, vl), jnp.float32)
    nxt = gather(0)
    for c in range(chunks):
        adj = nxt

        def pblock(blk):
            return lax.dot_general(
                scaled, _rows(adj, blk, n), (((1,), (1,)), ((), ())),
                preferred_element_type=jnp.float32,
            )

        halves = []
        for k in range(m):
            g = (q + k) % m
            keep = pblock(2 * g + par)
            send = pblock(2 * g + 1 - par)
            halves.append(keep + lax.ppermute(send, "vox", pair))
        share = halves[0]
        for k in range(1, m):
            share = share + lax.ppermute(
                halves[k].astype(jnp.bfloat16), "vox", chip_perm(k)
            ).astype(jnp.float32)

        w_c = weight[:, :, c * r:(c + 1) * r].reshape(sl, n)
        wt = (w_c * share).astype(jnp.bfloat16)

        got = [(me, wt)]
        for k in range(1, m):
            got.append((2 * ((q - k) % m) + par, lax.ppermute(wt, "vox", chip_perm(k))))
        got = got + [(blk ^ 1, lax.ppermute(w, "vox", pair)) for blk, w in got]
        if c + 1 < chunks:
            nxt, ws = lax.optimization_barrier((gather(c + 1), [w for _, w in got]))
            got = [(blk, w) for (blk, _), w in zip(got, ws)]
        for blk, w in got:
            back = back + jnp.dot(w, _rows(adj, blk, n), preferred_element_type=jnp.float32)

    local_sum = jnp.sum(forward_voxel_field.astype(jnp.float32) * back, axis=0)
    return _sum_over_src(local_sum)


def solution(mesh):
    placed = (P("src", "vox"), P("src", "vox"), P("vox"), P("src", "vox"))
    return jax.shard_map(
        functools.partial(per_device, _src_grid(mesh)), mesh=mesh, in_specs=placed, out_specs=P("vox"), check_vma=False
    )
```

```python
import functools

import jax
import jax.numpy as jnp
from jax import lax
from jax.sharding import PartitionSpec as P

CHUNKS = 2


def _rows(a, blk, n):
    return lax.dynamic_slice_in_dim(a, blk * n, n, axis=0)


def _src_grid(mesh):
    devs = mesh.devices
    ax = mesh.axis_names.index("src")
    row = [devs[(i,) + (0,) * (devs.ndim - 1)] if ax == 0 else None for i in range(devs.shape[0])]
    if ax != 0 or any(not hasattr(d, "coords") for d in row):
        return None
    co = [tuple(d.coords) for d in row]
    n = len(co)
    diff = [k for k in range(len(co[0])) if n > 1 and co[1][k] != co[0][k]]
    if len(diff) != 1:
        return None
    nb = 1
    while nb < n and co[nb][diff[0]] != co[0][diff[0]]:
        nb += 1
    if n % nb:
        return None
    na = n // nb

    def near(i, j):
        return sum(abs(a - b) for a, b in zip(co[i], co[j])) == 1

    for i in range(n):
        ia, ib = divmod(i, nb)
        if ib + 1 < nb and not near(i, i + 1):
            return None
        if ia + 1 < na and not near(i, i + nb):
            return None
    if nb != 2 or na < 2:
        return None
    return nb, na


def _gather_src(block, grid):
    if grid is None:
        return lax.all_gather(block, "src", axis=0, tiled=True)
    nb, na = grid
    me = lax.axis_index("src")
    ia, ib = me // nb, me % nb
    swap = [(i, i ^ 1) for i in range(na * nb)]

    def along(p, d):
        return [(p * nb + o, d * nb + o) for o in range(nb)]

    def cross(sign, s):
        return [(i, i ^ 1) for i in range(na * nb) if 0 <= i // nb - sign * s < na]

    got = {}
    for sign in (1, -1):
        cur = block
        for s in range(1, na):
            pairs = []
            for p in range(na):
                if 0 <= p + sign < na and 0 <= p - sign * (s - 1) < na:
                    pairs.extend(along(p, p + sign))
            cur = lax.ppermute(cur, "src", pairs)
            got[(sign, s)] = (cur, lax.ppermute(cur, "src", cross(sign, s)))
    planes = [(block, lax.ppermute(block, "src", swap))]
    for k in range(1, na):
        up, down = got[(-1, k)], got[(1, na - k)]
        ok = ia + k < na
        planes.append(tuple(jnp.where(ok, u, d) for u, d in zip(up, down)))
    return jnp.concatenate([x for pl in planes for x in pl], axis=0)


def _sum_over_src(v):
    n = lax.axis_size("src")
    if n & (n - 1):
        return lax.psum(v, "src")
    b = 1
    while b < n:
        v = v + lax.ppermute(v, "src", [(i, i ^ b) for i in range(n)])
        b *= 2
    return v


def per_device(grid, forward_voxel_field, adjoint_voxel_field, voxel_input_vector, measurement_weight):
    nsrc = lax.axis_size("src")
    vox = lax.axis_size("vox")
    me = lax.axis_index("vox")
    m = vox // 2
    par = me % 2
    q = me // 2
    t = nsrc // vox
    sl, vl = forward_voxel_field.shape
    ds = adjoint_voxel_field.shape[0]
    chunks = CHUNKS if ds % CHUNKS == 0 else 1
    r = ds // chunks
    n = t * r
    pair = [(j, j ^ 1) for j in range(vox)]

    def chip_perm(k):
        return [(g * 2 + p, ((g + k) % m) * 2 + p) for g in range(m) for p in range(2)]

    scaled = (forward_voxel_field.astype(jnp.float32) * voxel_input_vector[None, :]).astype(
        jnp.bfloat16
    )
    weight = measurement_weight.reshape(sl, t, ds)
    if grid is not None and grid[0] == t:
        na = grid[1]
        ia = lax.axis_index("src") // t
        flip = lax.axis_index("src") % t == 1

        def rel(blk):
            return (blk - ia) % na

        def order(w):
            return jnp.where(flip, w[:, ::-1], w)
    else:
        grid = None

        def rel(blk):
            return blk

        def order(w):
            return w
    def gather(c):
        return _gather_src(adjoint_voxel_field[c * r:(c + 1) * r], grid)

    back = jnp.zeros((sl, vl), jnp.float32)
    nxt = gather(0)
    for c in range(chunks):
        adj = nxt

        def pblock(blk):
            return lax.dot_general(
                scaled, _rows(adj, rel(blk), n), (((1,), (1,)), ((), ())),
                preferred_element_type=jnp.float32,
            )

        halves = []
        for k in range(m):
            g = (q + k) % m
            keep = pblock(2 * g + par)
            send = pblock(2 * g + 1 - par)
            halves.append(keep + lax.ppermute(send, "vox", pair))
        share = halves[0]
        for k in range(1, m):
            share = share + lax.ppermute(
                halves[k].astype(jnp.bfloat16), "vox", chip_perm(k)
            ).astype(jnp.float32)

        w_c = order(weight[:, :, c * r:(c + 1) * r]).reshape(sl, n)
        wt = (w_c * share).astype(jnp.bfloat16)

        got = [(me, wt)]
        for k in range(1, m):
            got.append((2 * ((q - k) % m) + par, lax.ppermute(wt, "vox", chip_perm(k))))
        got = got + [(blk ^ 1, lax.ppermute(w, "vox", pair)) for blk, w in got]
        if c + 1 < chunks:
            nxt, ws = lax.optimization_barrier((gather(c + 1), [w for _, w in got]))
            got = [(blk, w) for (blk, _), w in zip(got, ws)]
        for blk, w in got:
            back = back + jnp.dot(w, _rows(adj, rel(blk), n), preferred_element_type=jnp.float32)

    local_sum = jnp.sum(forward_voxel_field.astype(jnp.float32) * back, axis=0)
    return _sum_over_src(local_sum)


def solution(mesh):
    placed = (P("src", "vox"), P("src", "vox"), P("vox"), P("src", "vox"))
    return jax.shard_map(
        functools.partial(per_device, _src_grid(mesh)), mesh=mesh, in_specs=placed, out_specs=P("vox"), check_vma=False
    )
```

```python
import functools

import jax
import jax.numpy as jnp
from jax import lax
from jax.sharding import PartitionSpec as P

CHUNKS = 2


def _rows(a, blk, n):
    return lax.dynamic_slice_in_dim(a, blk * n, n, axis=0)


def _src_grid(mesh):
    devs = mesh.devices
    ax = mesh.axis_names.index("src")
    row = [devs[(i,) + (0,) * (devs.ndim - 1)] if ax == 0 else None for i in range(devs.shape[0])]
    if ax != 0 or any(not hasattr(d, "coords") for d in row):
        return None
    co = [tuple(d.coords) for d in row]
    n = len(co)
    diff = [k for k in range(len(co[0])) if n > 1 and co[1][k] != co[0][k]]
    if len(diff) != 1:
        return None
    nb = 1
    while nb < n and co[nb][diff[0]] != co[0][diff[0]]:
        nb += 1
    if n % nb:
        return None
    na = n // nb

    def near(i, j):
        return sum(abs(a - b) for a, b in zip(co[i], co[j])) == 1

    for i in range(n):
        ia, ib = divmod(i, nb)
        if ib + 1 < nb and not near(i, i + 1):
            return None
        if ia + 1 < na and not near(i, i + nb):
            return None
    if nb != 2 or na < 2:
        return None
    return nb, na


def _gather_src(block, grid):
    if grid is None:
        return lax.all_gather(block, "src", axis=0, tiled=True)
    nb, na = grid
    me = lax.axis_index("src")
    ia, ib = me // nb, me % nb
    swap = [(i, i ^ 1) for i in range(na * nb)]

    def along(p, d):
        return [(p * nb + o, d * nb + o) for o in range(nb)]

    def cross(sign, s):
        return [(i, i ^ 1) for i in range(na * nb) if 0 <= i // nb - sign * s < na]

    got = {}
    for sign in (1, -1):
        cur = block
        for s in range(1, na):
            pairs = []
            for p in range(na):
                if 0 <= p + sign < na and 0 <= p - sign * (s - 1) < na:
                    pairs.extend(along(p, p + sign))
            cur = lax.ppermute(cur, "src", pairs)
            got[(sign, s)] = (cur, lax.ppermute(cur, "src", cross(sign, s)))
    first = ib == 0
    planes = [(block, lax.ppermute(block, "src", swap))]
    for k in range(1, na):
        up, down = got[(-1, k)], got[(1, na - k)]
        ok = ia + k < na
        planes.append(tuple(jnp.where(ok, u, d) for u, d in zip(up, down)))
    return jnp.concatenate(
        [x for a, b in planes for x in (jnp.where(first, a, b), jnp.where(first, b, a))], axis=0
    )


def _sum_over_src(v):
    n = lax.axis_size("src")
    if n & (n - 1):
        return lax.psum(v, "src")
    b = 1
    while b < n:
        v = v + lax.ppermute(v, "src", [(i, i ^ b) for i in range(n)])
        b *= 2
    return v


def per_device(grid, forward_voxel_field, adjoint_voxel_field, voxel_input_vector, measurement_weight):
    nsrc = lax.axis_size("src")
    vox = lax.axis_size("vox")
    me = lax.axis_index("vox")
    m = vox // 2
    par = me % 2
    q = me // 2
    t = nsrc // vox
    sl, vl = forward_voxel_field.shape
    ds = adjoint_voxel_field.shape[0]
    chunks = CHUNKS if ds % CHUNKS == 0 else 1
    r = ds // chunks
    n = t * r
    pair = [(j, j ^ 1) for j in range(vox)]

    def chip_perm(k):
        return [(g * 2 + p, ((g + k) % m) * 2 + p) for g in range(m) for p in range(2)]

    scaled = (forward_voxel_field.astype(jnp.float32) * voxel_input_vector[None, :]).astype(
        jnp.bfloat16
    )
    weight = measurement_weight.reshape(sl, t, ds)
    if grid is not None and grid[0] == t:
        na = grid[1]
        ia = lax.axis_index("src") // t

        def rel(blk):
            return (blk - ia) % na
    else:
        grid = None

        def rel(blk):
            return blk
    def gather(c):
        return _gather_src(adjoint_voxel_field[c * r:(c + 1) * r], grid)

    back = jnp.zeros((sl, vl), jnp.float32)
    nxt = gather(0)
    for c in range(chunks):
        adj = nxt

        def pblock(blk):
            return lax.dot_general(
                scaled, _rows(adj, rel(blk), n), (((1,), (1,)), ((), ())),
                preferred_element_type=jnp.float32,
            )

        keeps = [pblock(2 * ((q + k) % m) + par) for k in range(m)]
        sends = [pblock(2 * ((q + k) % m) + 1 - par) for k in range(m)]
        halves = [a + b for a, b in zip(keeps, lax.ppermute(tuple(sends), "vox", pair))]
        share = halves[0]
        for k in range(1, m):
            share = share + lax.ppermute(
                halves[k].astype(jnp.bfloat16), "vox", chip_perm(k)
            ).astype(jnp.float32)

        w_c = weight[:, :, c * r:(c + 1) * r].reshape(sl, n)
        wt = (w_c * share).astype(jnp.bfloat16)

        got = [(me, wt)]
        for k in range(1, m):
            got.append((2 * ((q - k) % m) + par, lax.ppermute(wt, "vox", chip_perm(k))))
        mine = lax.ppermute(tuple(w for _, w in got), "vox", pair)
        got = got + [(blk ^ 1, w) for (blk, _), w in zip(got, mine)]
        if c + 1 < chunks:
            nxt, ws = lax.optimization_barrier((gather(c + 1), [w for _, w in got]))
            got = [(blk, w) for (blk, _), w in zip(got, ws)]
        for blk, w in got:
            back = back + jnp.dot(w, _rows(adj, rel(blk), n), preferred_element_type=jnp.float32)

    local_sum = jnp.sum(forward_voxel_field.astype(jnp.float32) * back, axis=0)
    return _sum_over_src(local_sum)


def solution(mesh):
    placed = (P("src", "vox"), P("src", "vox"), P("vox"), P("src", "vox"))
    return jax.shard_map(
        functools.partial(per_device, _src_grid(mesh)), mesh=mesh, in_specs=placed, out_specs=P("vox"), check_vma=False
    )
```

```python
import functools

import jax
import jax.numpy as jnp
from jax import lax
from jax.sharding import PartitionSpec as P

CHUNKS = 1


def _rows(a, blk, n):
    return lax.dynamic_slice_in_dim(a, blk * n, n, axis=0)


def _src_grid(mesh):
    devs = mesh.devices
    ax = mesh.axis_names.index("src")
    row = [devs[(i,) + (0,) * (devs.ndim - 1)] if ax == 0 else None for i in range(devs.shape[0])]
    if ax != 0 or any(not hasattr(d, "coords") for d in row):
        return None
    co = [tuple(d.coords) for d in row]
    n = len(co)
    diff = [k for k in range(len(co[0])) if n > 1 and co[1][k] != co[0][k]]
    if len(diff) != 1:
        return None
    nb = 1
    while nb < n and co[nb][diff[0]] != co[0][diff[0]]:
        nb += 1
    if n % nb:
        return None
    na = n // nb

    def near(i, j):
        return sum(abs(a - b) for a, b in zip(co[i], co[j])) == 1

    for i in range(n):
        ia, ib = divmod(i, nb)
        if ib + 1 < nb and not near(i, i + 1):
            return None
        if ia + 1 < na and not near(i, i + nb):
            return None
    if nb != 2 or na < 2:
        return None
    return nb, na


def _gather_src(block, grid):
    if grid is None:
        return lax.all_gather(block, "src", axis=0, tiled=True)
    nb, na = grid
    me = lax.axis_index("src")
    ia, ib = me // nb, me % nb
    swap = [(i, i ^ 1) for i in range(na * nb)]

    def along(p, d):
        return [(p * nb + o, d * nb + o) for o in range(nb)]

    def cross(sign, s):
        return [(i, i ^ 1) for i in range(na * nb) if 0 <= i // nb - sign * s < na]

    got = {}
    for sign in (1, -1):
        cur = block
        for s in range(1, na):
            pairs = []
            for p in range(na):
                if 0 <= p + sign < na and 0 <= p - sign * (s - 1) < na:
                    pairs.extend(along(p, p + sign))
            cur = lax.ppermute(cur, "src", pairs)
            got[(sign, s)] = (cur, lax.ppermute(cur, "src", cross(sign, s)))
    first = ib == 0
    planes = [(block, lax.ppermute(block, "src", swap))]
    for k in range(1, na):
        up, down = got[(-1, k)], got[(1, na - k)]
        ok = ia + k < na
        planes.append(tuple(jnp.where(ok, u, d) for u, d in zip(up, down)))
    return jnp.concatenate(
        [x for a, b in planes for x in (jnp.where(first, a, b), jnp.where(first, b, a))], axis=0
    )


def _sum_over_src(v):
    n = lax.axis_size("src")
    if n & (n - 1):
        return lax.psum(v, "src")
    b = 1
    while b < n:
        v = v + lax.ppermute(v, "src", [(i, i ^ b) for i in range(n)])
        b *= 2
    return v


def per_device(grid, forward_voxel_field, adjoint_voxel_field, voxel_input_vector, measurement_weight):
    nsrc = lax.axis_size("src")
    vox = lax.axis_size("vox")
    me = lax.axis_index("vox")
    m = vox // 2
    par = me % 2
    q = me // 2
    t = nsrc // vox
    sl, vl = forward_voxel_field.shape
    ds = adjoint_voxel_field.shape[0]
    chunks = CHUNKS if ds % CHUNKS == 0 else 1
    r = ds // chunks
    n = t * r
    pair = [(j, j ^ 1) for j in range(vox)]

    def chip_perm(k):
        return [(g * 2 + p, ((g + k) % m) * 2 + p) for g in range(m) for p in range(2)]

    scaled = (forward_voxel_field.astype(jnp.float32) * voxel_input_vector[None, :]).astype(
        jnp.bfloat16
    )
    weight = measurement_weight.reshape(sl, t, ds)
    if grid is not None and grid[0] == t:
        na = grid[1]
        ia = lax.axis_index("src") // t

        def rel(blk):
            return (blk - ia) % na
    else:
        grid = None

        def rel(blk):
            return blk
    def gather(c):
        return _gather_src(adjoint_voxel_field[c * r:(c + 1) * r], grid)

    back = jnp.zeros((sl, vl), jnp.float32)
    nxt = gather(0)
    for c in range(chunks):
        adj = nxt

        def pblock(blk):
            return lax.dot_general(
                scaled, _rows(adj, rel(blk), n), (((1,), (1,)), ((), ())),
                preferred_element_type=jnp.float32,
            )

        keeps = [pblock(2 * ((q + k) % m) + par) for k in range(m)]
        sends = [pblock(2 * ((q + k) % m) + 1 - par) for k in range(m)]
        halves = [a + b for a, b in zip(keeps, lax.ppermute(tuple(sends), "vox", pair))]
        share = halves[0]
        for k in range(1, m):
            share = share + lax.ppermute(
                halves[k].astype(jnp.bfloat16), "vox", chip_perm(k)
            ).astype(jnp.float32)

        w_c = weight[:, :, c * r:(c + 1) * r].reshape(sl, n)
        wt = (w_c * share).astype(jnp.bfloat16)

        got = [(me, wt)]
        for k in range(1, m):
            got.append((2 * ((q - k) % m) + par, lax.ppermute(wt, "vox", chip_perm(k))))
        mine = lax.ppermute(tuple(w for _, w in got), "vox", pair)
        got = got + [(blk ^ 1, w) for (blk, _), w in zip(got, mine)]
        if c + 1 < chunks:
            nxt, ws = lax.optimization_barrier((gather(c + 1), [w for _, w in got]))
            got = [(blk, w) for (blk, _), w in zip(got, ws)]
        for blk, w in got:
            back = back + jnp.dot(w, _rows(adj, rel(blk), n), preferred_element_type=jnp.float32)

    local_sum = jnp.sum(forward_voxel_field.astype(jnp.float32) * back, axis=0)
    return _sum_over_src(local_sum)


def solution(mesh):
    placed = (P("src", "vox"), P("src", "vox"), P("vox"), P("src", "vox"))
    return jax.shard_map(
        functools.partial(per_device, _src_grid(mesh)), mesh=mesh, in_specs=placed, out_specs=P("vox"), check_vma=False
    )
```

```python
import functools

import jax
import jax.numpy as jnp
from jax import lax
from jax.sharding import PartitionSpec as P

CHUNKS = 4


def _rows(a, blk, n):
    return lax.dynamic_slice_in_dim(a, blk * n, n, axis=0)


def _src_grid(mesh):
    devs = mesh.devices
    ax = mesh.axis_names.index("src")
    row = [devs[(i,) + (0,) * (devs.ndim - 1)] if ax == 0 else None for i in range(devs.shape[0])]
    if ax != 0 or any(not hasattr(d, "coords") for d in row):
        return None
    co = [tuple(d.coords) for d in row]
    n = len(co)
    diff = [k for k in range(len(co[0])) if n > 1 and co[1][k] != co[0][k]]
    if len(diff) != 1:
        return None
    nb = 1
    while nb < n and co[nb][diff[0]] != co[0][diff[0]]:
        nb += 1
    if n % nb:
        return None
    na = n // nb

    def near(i, j):
        return sum(abs(a - b) for a, b in zip(co[i], co[j])) == 1

    for i in range(n):
        ia, ib = divmod(i, nb)
        if ib + 1 < nb and not near(i, i + 1):
            return None
        if ia + 1 < na and not near(i, i + nb):
            return None
    if nb != 2 or na < 2:
        return None
    return nb, na


def _gather_src(block, grid):
    if grid is None:
        return lax.all_gather(block, "src", axis=0, tiled=True)
    nb, na = grid
    me = lax.axis_index("src")
    ia, ib = me // nb, me % nb
    swap = [(i, i ^ 1) for i in range(na * nb)]

    def along(p, d):
        return [(p * nb + o, d * nb + o) for o in range(nb)]

    def cross(sign, s):
        return [(i, i ^ 1) for i in range(na * nb) if 0 <= i // nb - sign * s < na]

    got = {}
    for sign in (1, -1):
        cur = block
        for s in range(1, na):
            pairs = []
            for p in range(na):
                if 0 <= p + sign < na and 0 <= p - sign * (s - 1) < na:
                    pairs.extend(along(p, p + sign))
            cur = lax.ppermute(cur, "src", pairs)
            got[(sign, s)] = (cur, lax.ppermute(cur, "src", cross(sign, s)))
    first = ib == 0
    planes = [(block, lax.ppermute(block, "src", swap))]
    for k in range(1, na):
        up, down = got[(-1, k)], got[(1, na - k)]
        ok = ia + k < na
        planes.append(tuple(jnp.where(ok, u, d) for u, d in zip(up, down)))
    return jnp.concatenate(
        [x for a, b in planes for x in (jnp.where(first, a, b), jnp.where(first, b, a))], axis=0
    )


def _sum_over_src(v):
    n = lax.axis_size("src")
    if n & (n - 1):
        return lax.psum(v, "src")
    b = 1
    while b < n:
        v = v + lax.ppermute(v, "src", [(i, i ^ b) for i in range(n)])
        b *= 2
    return v


def per_device(grid, forward_voxel_field, adjoint_voxel_field, voxel_input_vector, measurement_weight):
    nsrc = lax.axis_size("src")
    vox = lax.axis_size("vox")
    me = lax.axis_index("vox")
    m = vox // 2
    par = me % 2
    q = me // 2
    t = nsrc // vox
    sl, vl = forward_voxel_field.shape
    ds = adjoint_voxel_field.shape[0]
    chunks = CHUNKS if ds % CHUNKS == 0 else 1
    r = ds // chunks
    n = t * r
    pair = [(j, j ^ 1) for j in range(vox)]

    def chip_perm(k):
        return [(g * 2 + p, ((g + k) % m) * 2 + p) for g in range(m) for p in range(2)]

    scaled = (forward_voxel_field.astype(jnp.float32) * voxel_input_vector[None, :]).astype(
        jnp.bfloat16
    )
    weight = measurement_weight.reshape(sl, t, ds)
    if grid is not None and grid[0] == t:
        na = grid[1]
        ia = lax.axis_index("src") // t

        def rel(blk):
            return (blk - ia) % na
    else:
        grid = None

        def rel(blk):
            return blk
    def gather(c):
        return _gather_src(adjoint_voxel_field[c * r:(c + 1) * r], grid)

    back = jnp.zeros((sl, vl), jnp.float32)
    nxt = gather(0)
    for c in range(chunks):
        adj = nxt

        def pblock(blk):
            return lax.dot_general(
                scaled, _rows(adj, rel(blk), n), (((1,), (1,)), ((), ())),
                preferred_element_type=jnp.float32,
            )

        keeps = [pblock(2 * ((q + k) % m) + par) for k in range(m)]
        sends = [pblock(2 * ((q + k) % m) + 1 - par) for k in range(m)]
        halves = [a + b for a, b in zip(keeps, lax.ppermute(tuple(sends), "vox", pair))]
        share = halves[0]
        for k in range(1, m):
            share = share + lax.ppermute(
                halves[k].astype(jnp.bfloat16), "vox", chip_perm(k)
            ).astype(jnp.float32)

        w_c = weight[:, :, c * r:(c + 1) * r].reshape(sl, n)
        wt = (w_c * share).astype(jnp.bfloat16)

        got = [(me, wt)]
        for k in range(1, m):
            got.append((2 * ((q - k) % m) + par, lax.ppermute(wt, "vox", chip_perm(k))))
        mine = lax.ppermute(tuple(w for _, w in got), "vox", pair)
        got = got + [(blk ^ 1, w) for (blk, _), w in zip(got, mine)]
        if c + 1 < chunks:
            nxt, ws = lax.optimization_barrier((gather(c + 1), [w for _, w in got]))
            got = [(blk, w) for (blk, _), w in zip(got, ws)]
        for blk, w in got:
            back = back + jnp.dot(w, _rows(adj, rel(blk), n), preferred_element_type=jnp.float32)

    local_sum = jnp.sum(forward_voxel_field.astype(jnp.float32) * back, axis=0)
    return _sum_over_src(local_sum)


def solution(mesh):
    placed = (P("src", "vox"), P("src", "vox"), P("vox"), P("src", "vox"))
    return jax.shard_map(
        functools.partial(per_device, _src_grid(mesh)), mesh=mesh, in_specs=placed, out_specs=P("vox"), check_vma=False
    )
```

```python
import functools

import jax
import jax.numpy as jnp
from jax import lax
from jax.sharding import PartitionSpec as P

CHUNKS = 2


def _rows(a, blk, n):
    return lax.dynamic_slice_in_dim(a, blk * n, n, axis=0)


def _src_grid(mesh):
    devs = mesh.devices
    ax = mesh.axis_names.index("src")
    row = [devs[(i,) + (0,) * (devs.ndim - 1)] if ax == 0 else None for i in range(devs.shape[0])]
    if ax != 0 or any(not hasattr(d, "coords") for d in row):
        return None
    co = [tuple(d.coords) for d in row]
    n = len(co)
    diff = [k for k in range(len(co[0])) if n > 1 and co[1][k] != co[0][k]]
    if len(diff) != 1:
        return None
    nb = 1
    while nb < n and co[nb][diff[0]] != co[0][diff[0]]:
        nb += 1
    if n % nb:
        return None
    na = n // nb

    def near(i, j):
        return sum(abs(a - b) for a, b in zip(co[i], co[j])) == 1

    for i in range(n):
        ia, ib = divmod(i, nb)
        if ib + 1 < nb and not near(i, i + 1):
            return None
        if ia + 1 < na and not near(i, i + nb):
            return None
    if nb != 2 or na < 2:
        return None
    return nb, na


def _gather_src(block, grid):
    if grid is None:
        return lax.all_gather(block, "src", axis=0, tiled=True)
    nb, na = grid
    me = lax.axis_index("src")
    ia, ib = me // nb, me % nb
    swap = [(i, i ^ 1) for i in range(na * nb)]

    def along(p, d):
        return [(p * nb + o, d * nb + o) for o in range(nb)]

    got = {}
    for sign in (1, -1):
        cur = block
        for s in range(1, na):
            pairs = []
            for p in range(na):
                if 0 <= p + sign < na and 0 <= p - sign * (s - 1) < na:
                    pairs.extend(along(p, p + sign))
            cur = lax.ppermute(cur, "src", pairs)
            got[(sign, s)] = cur
    col = [block] + [
        jnp.where(ia + k < na, got[(-1, k)], got[(1, na - k)]) for k in range(1, na)
    ]
    col = jnp.stack(col)
    other = lax.ppermute(col, "src", swap)
    first = ib == 0
    planes = jnp.stack([jnp.where(first, col, other), jnp.where(first, other, col)], axis=1)
    return planes.reshape((-1,) + block.shape[1:])


def _sum_over_src(v):
    n = lax.axis_size("src")
    if n & (n - 1):
        return lax.psum(v, "src")
    b = 1
    while b < n:
        v = v + lax.ppermute(v, "src", [(i, i ^ b) for i in range(n)])
        b *= 2
    return v


def per_device(grid, forward_voxel_field, adjoint_voxel_field, voxel_input_vector, measurement_weight):
    nsrc = lax.axis_size("src")
    vox = lax.axis_size("vox")
    me = lax.axis_index("vox")
    m = vox // 2
    par = me % 2
    q = me // 2
    t = nsrc // vox
    sl, vl = forward_voxel_field.shape
    ds = adjoint_voxel_field.shape[0]
    chunks = CHUNKS if ds % CHUNKS == 0 else 1
    r = ds // chunks
    n = t * r
    pair = [(j, j ^ 1) for j in range(vox)]

    def chip_perm(k):
        return [(g * 2 + p, ((g + k) % m) * 2 + p) for g in range(m) for p in range(2)]

    scaled = (forward_voxel_field.astype(jnp.float32) * voxel_input_vector[None, :]).astype(
        jnp.bfloat16
    )
    weight = measurement_weight.reshape(sl, t, ds)
    if grid is not None and grid[0] == t:
        na = grid[1]
        ia = lax.axis_index("src") // t

        def rel(blk):
            return (blk - ia) % na
    else:
        grid = None

        def rel(blk):
            return blk
    def gather(c):
        return _gather_src(adjoint_voxel_field[c * r:(c + 1) * r], grid)

    back = jnp.zeros((sl, vl), jnp.float32)
    nxt = gather(0)
    for c in range(chunks):
        adj = nxt

        def pblock(blk):
            return lax.dot_general(
                scaled, _rows(adj, rel(blk), n), (((1,), (1,)), ((), ())),
                preferred_element_type=jnp.float32,
            )

        keeps = [pblock(2 * ((q + k) % m) + par) for k in range(m)]
        sends = [pblock(2 * ((q + k) % m) + 1 - par) for k in range(m)]
        halves = [a + b for a, b in zip(keeps, lax.ppermute(tuple(sends), "vox", pair))]
        share = halves[0]
        for k in range(1, m):
            share = share + lax.ppermute(
                halves[k].astype(jnp.bfloat16), "vox", chip_perm(k)
            ).astype(jnp.float32)

        w_c = weight[:, :, c * r:(c + 1) * r].reshape(sl, n)
        wt = (w_c * share).astype(jnp.bfloat16)

        got = [(me, wt)]
        for k in range(1, m):
            got.append((2 * ((q - k) % m) + par, lax.ppermute(wt, "vox", chip_perm(k))))
        mine = lax.ppermute(tuple(w for _, w in got), "vox", pair)
        got = got + [(blk ^ 1, w) for (blk, _), w in zip(got, mine)]
        if c + 1 < chunks:
            nxt, ws = lax.optimization_barrier((gather(c + 1), [w for _, w in got]))
            got = [(blk, w) for (blk, _), w in zip(got, ws)]
        for blk, w in got:
            back = back + jnp.dot(w, _rows(adj, rel(blk), n), preferred_element_type=jnp.float32)

    local_sum = jnp.sum(forward_voxel_field.astype(jnp.float32) * back, axis=0)
    return _sum_over_src(local_sum)


def solution(mesh):
    placed = (P("src", "vox"), P("src", "vox"), P("vox"), P("src", "vox"))
    return jax.shard_map(
        functools.partial(per_device, _src_grid(mesh)), mesh=mesh, in_specs=placed, out_specs=P("vox"), check_vma=False
    )
```

```python
import functools

import jax
import jax.numpy as jnp
from jax import lax
from jax.sharding import PartitionSpec as P

CHUNKS = 2


def _rows(a, blk, n):
    return lax.dynamic_slice_in_dim(a, blk * n, n, axis=0)


def _src_grid(mesh):
    devs = mesh.devices
    ax = mesh.axis_names.index("src")
    row = [devs[(i,) + (0,) * (devs.ndim - 1)] if ax == 0 else None for i in range(devs.shape[0])]
    if ax != 0 or any(not hasattr(d, "coords") for d in row):
        return None
    co = [tuple(d.coords) for d in row]
    n = len(co)
    diff = [k for k in range(len(co[0])) if n > 1 and co[1][k] != co[0][k]]
    if len(diff) != 1:
        return None
    nb = 1
    while nb < n and co[nb][diff[0]] != co[0][diff[0]]:
        nb += 1
    if n % nb:
        return None
    na = n // nb

    def near(i, j):
        return sum(abs(a - b) for a, b in zip(co[i], co[j])) == 1

    for i in range(n):
        ia, ib = divmod(i, nb)
        if ib + 1 < nb and not near(i, i + 1):
            return None
        if ia + 1 < na and not near(i, i + nb):
            return None
    if nb != 2 or na < 2:
        return None
    return nb, na


def _gather_src(block, grid):
    if grid is None:
        return lax.all_gather(block, "src", axis=0, tiled=True)
    nb, na = grid
    me = lax.axis_index("src")
    ia, ib = me // nb, me % nb
    swap = [(i, i ^ 1) for i in range(na * nb)]

    def along(p, d):
        return [(p * nb + o, d * nb + o) for o in range(nb)]

    mate = lax.ppermute(block, "src", swap)
    got = {}
    for sign in (1, -1):
        cur = block
        for s in range(1, na):
            pairs = []
            for p in range(na):
                if 0 <= p + sign < na and 0 <= p - sign * (s - 1) < na:
                    pairs.extend(along(p, p + sign))
            cur = lax.ppermute(cur, "src", pairs)
            got[(sign, s)] = cur
    far = jnp.stack(
        [jnp.where(ia + k < na, got[(-1, k)], got[(1, na - k)]) for k in range(1, na)]
    )
    col = jnp.concatenate([block[None], far])
    other = jnp.concatenate([mate[None], lax.ppermute(far, "src", swap)])
    first = ib == 0
    planes = jnp.stack([jnp.where(first, col, other), jnp.where(first, other, col)], axis=1)
    return planes.reshape((-1,) + block.shape[1:])


def _sum_over_src(v):
    n = lax.axis_size("src")
    if n & (n - 1):
        return lax.psum(v, "src")
    b = 1
    while b < n:
        v = v + lax.ppermute(v, "src", [(i, i ^ b) for i in range(n)])
        b *= 2
    return v


def per_device(grid, forward_voxel_field, adjoint_voxel_field, voxel_input_vector, measurement_weight):
    nsrc = lax.axis_size("src")
    vox = lax.axis_size("vox")
    me = lax.axis_index("vox")
    m = vox // 2
    par = me % 2
    q = me // 2
    t = nsrc // vox
    sl, vl = forward_voxel_field.shape
    ds = adjoint_voxel_field.shape[0]
    chunks = CHUNKS if ds % CHUNKS == 0 else 1
    r = ds // chunks
    n = t * r
    pair = [(j, j ^ 1) for j in range(vox)]

    def chip_perm(k):
        return [(g * 2 + p, ((g + k) % m) * 2 + p) for g in range(m) for p in range(2)]

    scaled = (forward_voxel_field.astype(jnp.float32) * voxel_input_vector[None, :]).astype(
        jnp.bfloat16
    )
    weight = measurement_weight.reshape(sl, t, ds)
    if grid is not None and grid[0] == t:
        na = grid[1]
        ia = lax.axis_index("src") // t

        def rel(blk):
            return (blk - ia) % na
    else:
        grid = None

        def rel(blk):
            return blk
    def gather(c):
        return _gather_src(adjoint_voxel_field[c * r:(c + 1) * r], grid)

    back = jnp.zeros((sl, vl), jnp.float32)
    nxt = gather(0)
    for c in range(chunks):
        adj = nxt

        def pblock(blk):
            return lax.dot_general(
                scaled, _rows(adj, rel(blk), n), (((1,), (1,)), ((), ())),
                preferred_element_type=jnp.float32,
            )

        keeps = [pblock(2 * ((q + k) % m) + par) for k in range(m)]
        sends = [pblock(2 * ((q + k) % m) + 1 - par) for k in range(m)]
        halves = [a + b for a, b in zip(keeps, lax.ppermute(tuple(sends), "vox", pair))]
        share = halves[0]
        for k in range(1, m):
            share = share + lax.ppermute(
                halves[k].astype(jnp.bfloat16), "vox", chip_perm(k)
            ).astype(jnp.float32)

        w_c = weight[:, :, c * r:(c + 1) * r].reshape(sl, n)
        wt = (w_c * share).astype(jnp.bfloat16)

        got = [(me, wt)]
        for k in range(1, m):
            got.append((2 * ((q - k) % m) + par, lax.ppermute(wt, "vox", chip_perm(k))))
        mine = lax.ppermute(tuple(w for _, w in got), "vox", pair)
        got = got + [(blk ^ 1, w) for (blk, _), w in zip(got, mine)]
        if c + 1 < chunks:
            nxt, ws = lax.optimization_barrier((gather(c + 1), [w for _, w in got]))
            got = [(blk, w) for (blk, _), w in zip(got, ws)]
        for blk, w in got:
            back = back + jnp.dot(w, _rows(adj, rel(blk), n), preferred_element_type=jnp.float32)

    local_sum = jnp.sum(forward_voxel_field.astype(jnp.float32) * back, axis=0)
    return _sum_over_src(local_sum)


def solution(mesh):
    placed = (P("src", "vox"), P("src", "vox"), P("vox"), P("src", "vox"))
    return jax.shard_map(
        functools.partial(per_device, _src_grid(mesh)), mesh=mesh, in_specs=placed, out_specs=P("vox"), check_vma=False
    )
```

```python
import functools

import jax
import jax.numpy as jnp
from jax import lax
from jax.sharding import PartitionSpec as P

SPLIT = (1, 2, 1)


def _rows(a, blk, n):
    return lax.dynamic_slice_in_dim(a, blk * n, n, axis=0)


def _src_grid(mesh):
    devs = mesh.devices
    ax = mesh.axis_names.index("src")
    row = [devs[(i,) + (0,) * (devs.ndim - 1)] if ax == 0 else None for i in range(devs.shape[0])]
    if ax != 0 or any(not hasattr(d, "coords") for d in row):
        return None
    co = [tuple(d.coords) for d in row]
    n = len(co)
    diff = [k for k in range(len(co[0])) if n > 1 and co[1][k] != co[0][k]]
    if len(diff) != 1:
        return None
    nb = 1
    while nb < n and co[nb][diff[0]] != co[0][diff[0]]:
        nb += 1
    if n % nb:
        return None
    na = n // nb

    def near(i, j):
        return sum(abs(a - b) for a, b in zip(co[i], co[j])) == 1

    for i in range(n):
        ia, ib = divmod(i, nb)
        if ib + 1 < nb and not near(i, i + 1):
            return None
        if ia + 1 < na and not near(i, i + nb):
            return None
    if nb != 2 or na < 2:
        return None
    return nb, na


def _gather_src(block, grid):
    if grid is None:
        return lax.all_gather(block, "src", axis=0, tiled=True)
    nb, na = grid
    me = lax.axis_index("src")
    ia, ib = me // nb, me % nb
    swap = [(i, i ^ 1) for i in range(na * nb)]

    def along(p, d):
        return [(p * nb + o, d * nb + o) for o in range(nb)]

    got = {}
    for sign in (1, -1):
        cur = block
        for s in range(1, na):
            pairs = []
            for p in range(na):
                if 0 <= p + sign < na and 0 <= p - sign * (s - 1) < na:
                    pairs.extend(along(p, p + sign))
            cur = lax.ppermute(cur, "src", pairs)
            got[(sign, s)] = cur
    col = [block] + [
        jnp.where(ia + k < na, got[(-1, k)], got[(1, na - k)]) for k in range(1, na)
    ]
    col = jnp.stack(col)
    other = lax.ppermute(col, "src", swap)
    first = ib == 0
    planes = jnp.stack([jnp.where(first, col, other), jnp.where(first, other, col)], axis=1)
    return planes.reshape((-1,) + block.shape[1:])


def _sum_over_src(v):
    n = lax.axis_size("src")
    if n & (n - 1):
        return lax.psum(v, "src")
    b = 1
    while b < n:
        v = v + lax.ppermute(v, "src", [(i, i ^ b) for i in range(n)])
        b *= 2
    return v


def per_device(grid, forward_voxel_field, adjoint_voxel_field, voxel_input_vector, measurement_weight):
    nsrc = lax.axis_size("src")
    vox = lax.axis_size("vox")
    me = lax.axis_index("vox")
    m = vox // 2
    par = me % 2
    q = me // 2
    t = nsrc // vox
    sl, vl = forward_voxel_field.shape
    ds = adjoint_voxel_field.shape[0]
    unit = ds // sum(SPLIT)
    if unit * sum(SPLIT) == ds and unit % 8 == 0:
        bounds = [unit * sum(SPLIT[:k]) for k in range(len(SPLIT) + 1)]
    else:
        bounds = [0, ds]
    chunks = len(bounds) - 1
    pair = [(j, j ^ 1) for j in range(vox)]

    def chip_perm(k):
        return [(g * 2 + p, ((g + k) % m) * 2 + p) for g in range(m) for p in range(2)]

    scaled = (forward_voxel_field.astype(jnp.float32) * voxel_input_vector[None, :]).astype(
        jnp.bfloat16
    )
    weight = measurement_weight.reshape(sl, t, ds)
    if grid is not None and grid[0] == t:
        na = grid[1]
        ia = lax.axis_index("src") // t

        def rel(blk):
            return (blk - ia) % na
    else:
        grid = None

        def rel(blk):
            return blk
    def gather(c):
        return _gather_src(adjoint_voxel_field[bounds[c]:bounds[c + 1]], grid)

    back = jnp.zeros((sl, vl), jnp.float32)
    nxt = gather(0)
    for c in range(chunks):
        adj = nxt
        n = t * (bounds[c + 1] - bounds[c])

        def pblock(blk):
            return lax.dot_general(
                scaled, _rows(adj, rel(blk), n), (((1,), (1,)), ((), ())),
                preferred_element_type=jnp.float32,
            )

        keeps = [pblock(2 * ((q + k) % m) + par) for k in range(m)]
        sends = [pblock(2 * ((q + k) % m) + 1 - par) for k in range(m)]
        halves = [a + b for a, b in zip(keeps, lax.ppermute(tuple(sends), "vox", pair))]
        share = halves[0]
        for k in range(1, m):
            share = share + lax.ppermute(
                halves[k].astype(jnp.bfloat16), "vox", chip_perm(k)
            ).astype(jnp.float32)

        w_c = weight[:, :, bounds[c]:bounds[c + 1]].reshape(sl, n)
        wt = (w_c * share).astype(jnp.bfloat16)

        got = [(me, wt)]
        for k in range(1, m):
            got.append((2 * ((q - k) % m) + par, lax.ppermute(wt, "vox", chip_perm(k))))
        mine = lax.ppermute(tuple(w for _, w in got), "vox", pair)
        got = got + [(blk ^ 1, w) for (blk, _), w in zip(got, mine)]
        if c + 1 < chunks:
            nxt, ws = lax.optimization_barrier((gather(c + 1), [w for _, w in got]))
            got = [(blk, w) for (blk, _), w in zip(got, ws)]
        for blk, w in got:
            back = back + jnp.dot(w, _rows(adj, rel(blk), n), preferred_element_type=jnp.float32)

    local_sum = jnp.sum(forward_voxel_field.astype(jnp.float32) * back, axis=0)
    return _sum_over_src(local_sum)


def solution(mesh):
    placed = (P("src", "vox"), P("src", "vox"), P("vox"), P("src", "vox"))
    return jax.shard_map(
        functools.partial(per_device, _src_grid(mesh)), mesh=mesh, in_specs=placed, out_specs=P("vox"), check_vma=False
    )
```

```python
import functools

import jax
import jax.numpy as jnp
from jax import lax
from jax.sharding import PartitionSpec as P

SPLIT = (1, 3)


def _rows(a, blk, n):
    return lax.dynamic_slice_in_dim(a, blk * n, n, axis=0)


def _src_grid(mesh):
    devs = mesh.devices
    ax = mesh.axis_names.index("src")
    row = [devs[(i,) + (0,) * (devs.ndim - 1)] if ax == 0 else None for i in range(devs.shape[0])]
    if ax != 0 or any(not hasattr(d, "coords") for d in row):
        return None
    co = [tuple(d.coords) for d in row]
    n = len(co)
    diff = [k for k in range(len(co[0])) if n > 1 and co[1][k] != co[0][k]]
    if len(diff) != 1:
        return None
    nb = 1
    while nb < n and co[nb][diff[0]] != co[0][diff[0]]:
        nb += 1
    if n % nb:
        return None
    na = n // nb

    def near(i, j):
        return sum(abs(a - b) for a, b in zip(co[i], co[j])) == 1

    for i in range(n):
        ia, ib = divmod(i, nb)
        if ib + 1 < nb and not near(i, i + 1):
            return None
        if ia + 1 < na and not near(i, i + nb):
            return None
    if nb != 2 or na < 2:
        return None
    return nb, na


def _gather_src(block, grid):
    if grid is None:
        return lax.all_gather(block, "src", axis=0, tiled=True)
    nb, na = grid
    me = lax.axis_index("src")
    ia, ib = me // nb, me % nb
    swap = [(i, i ^ 1) for i in range(na * nb)]

    def along(p, d):
        return [(p * nb + o, d * nb + o) for o in range(nb)]

    got = {}
    for sign in (1, -1):
        cur = block
        for s in range(1, na):
            pairs = []
            for p in range(na):
                if 0 <= p + sign < na and 0 <= p - sign * (s - 1) < na:
                    pairs.extend(along(p, p + sign))
            cur = lax.ppermute(cur, "src", pairs)
            got[(sign, s)] = cur
    col = [block] + [
        jnp.where(ia + k < na, got[(-1, k)], got[(1, na - k)]) for k in range(1, na)
    ]
    col = jnp.stack(col)
    other = lax.ppermute(col, "src", swap)
    first = ib == 0
    planes = jnp.stack([jnp.where(first, col, other), jnp.where(first, other, col)], axis=1)
    return planes.reshape((-1,) + block.shape[1:])


def _sum_over_src(v):
    n = lax.axis_size("src")
    if n & (n - 1):
        return lax.psum(v, "src")
    b = 1
    while b < n:
        v = v + lax.ppermute(v, "src", [(i, i ^ b) for i in range(n)])
        b *= 2
    return v


def per_device(grid, forward_voxel_field, adjoint_voxel_field, voxel_input_vector, measurement_weight):
    nsrc = lax.axis_size("src")
    vox = lax.axis_size("vox")
    me = lax.axis_index("vox")
    m = vox // 2
    par = me % 2
    q = me // 2
    t = nsrc // vox
    sl, vl = forward_voxel_field.shape
    ds = adjoint_voxel_field.shape[0]
    unit = ds // sum(SPLIT)
    if unit * sum(SPLIT) == ds and unit % 8 == 0:
        bounds = [unit * sum(SPLIT[:k]) for k in range(len(SPLIT) + 1)]
    else:
        bounds = [0, ds]
    chunks = len(bounds) - 1
    pair = [(j, j ^ 1) for j in range(vox)]

    def chip_perm(k):
        return [(g * 2 + p, ((g + k) % m) * 2 + p) for g in range(m) for p in range(2)]

    scaled = (forward_voxel_field.astype(jnp.float32) * voxel_input_vector[None, :]).astype(
        jnp.bfloat16
    )
    weight = measurement_weight.reshape(sl, t, ds)
    if grid is not None and grid[0] == t:
        na = grid[1]
        ia = lax.axis_index("src") // t

        def rel(blk):
            return (blk - ia) % na
    else:
        grid = None

        def rel(blk):
            return blk
    def gather(c):
        return _gather_src(adjoint_voxel_field[bounds[c]:bounds[c + 1]], grid)

    back = jnp.zeros((sl, vl), jnp.float32)
    nxt = gather(0)
    for c in range(chunks):
        adj = nxt
        n = t * (bounds[c + 1] - bounds[c])

        def pblock(blk):
            return lax.dot_general(
                scaled, _rows(adj, rel(blk), n), (((1,), (1,)), ((), ())),
                preferred_element_type=jnp.float32,
            )

        keeps = [pblock(2 * ((q + k) % m) + par) for k in range(m)]
        sends = [pblock(2 * ((q + k) % m) + 1 - par) for k in range(m)]
        halves = [a + b for a, b in zip(keeps, lax.ppermute(tuple(sends), "vox", pair))]
        share = halves[0]
        for k in range(1, m):
            share = share + lax.ppermute(
                halves[k].astype(jnp.bfloat16), "vox", chip_perm(k)
            ).astype(jnp.float32)

        w_c = weight[:, :, bounds[c]:bounds[c + 1]].reshape(sl, n)
        wt = (w_c * share).astype(jnp.bfloat16)

        got = [(me, wt)]
        for k in range(1, m):
            got.append((2 * ((q - k) % m) + par, lax.ppermute(wt, "vox", chip_perm(k))))
        mine = lax.ppermute(tuple(w for _, w in got), "vox", pair)
        got = got + [(blk ^ 1, w) for (blk, _), w in zip(got, mine)]
        if c + 1 < chunks:
            nxt, ws = lax.optimization_barrier((gather(c + 1), [w for _, w in got]))
            got = [(blk, w) for (blk, _), w in zip(got, ws)]
        for blk, w in got:
            back = back + jnp.dot(w, _rows(adj, rel(blk), n), preferred_element_type=jnp.float32)

    local_sum = jnp.sum(forward_voxel_field.astype(jnp.float32) * back, axis=0)
    return _sum_over_src(local_sum)


def solution(mesh):
    placed = (P("src", "vox"), P("src", "vox"), P("vox"), P("src", "vox"))
    return jax.shard_map(
        functools.partial(per_device, _src_grid(mesh)), mesh=mesh, in_specs=placed, out_specs=P("vox"), check_vma=False
    )
```

```python
import functools

import jax
import jax.numpy as jnp
from jax import lax
from jax.sharding import PartitionSpec as P

CHUNKS = 2


def _rows(a, blk, n):
    return lax.dynamic_slice_in_dim(a, blk * n, n, axis=0)


def _src_grid(mesh):
    devs = mesh.devices
    ax = mesh.axis_names.index("src")
    row = [devs[(i,) + (0,) * (devs.ndim - 1)] if ax == 0 else None for i in range(devs.shape[0])]
    if ax != 0 or any(not hasattr(d, "coords") for d in row):
        return None
    co = [tuple(d.coords) for d in row]
    n = len(co)
    diff = [k for k in range(len(co[0])) if n > 1 and co[1][k] != co[0][k]]
    if len(diff) != 1:
        return None
    nb = 1
    while nb < n and co[nb][diff[0]] != co[0][diff[0]]:
        nb += 1
    if n % nb:
        return None
    na = n // nb

    def near(i, j):
        return sum(abs(a - b) for a, b in zip(co[i], co[j])) == 1

    for i in range(n):
        ia, ib = divmod(i, nb)
        if ib + 1 < nb and not near(i, i + 1):
            return None
        if ia + 1 < na and not near(i, i + nb):
            return None
    if nb != 2 or na < 2:
        return None
    return nb, na


def _gather_src(block, grid):
    if grid is None:
        return lax.all_gather(block, "src", axis=0, tiled=True)
    nb, na = grid
    me = lax.axis_index("src")
    ib = me % nb
    swap = [(i, i ^ 1) for i in range(na * nb)]

    col = [block] + [
        lax.ppermute(
            block, "src", [(p * nb + o, ((p - k) % na) * nb + o) for p in range(na) for o in range(nb)]
        )
        for k in range(1, na)
    ]
    col = jnp.stack(col)
    other = lax.ppermute(col, "src", swap)
    first = ib == 0
    planes = jnp.stack([jnp.where(first, col, other), jnp.where(first, other, col)], axis=1)
    return planes.reshape((-1,) + block.shape[1:])


def _sum_over_src(v):
    n = lax.axis_size("src")
    if n & (n - 1):
        return lax.psum(v, "src")
    b = 1
    while b < n:
        v = v + lax.ppermute(v, "src", [(i, i ^ b) for i in range(n)])
        b *= 2
    return v


def per_device(grid, forward_voxel_field, adjoint_voxel_field, voxel_input_vector, measurement_weight):
    nsrc = lax.axis_size("src")
    vox = lax.axis_size("vox")
    me = lax.axis_index("vox")
    m = vox // 2
    par = me % 2
    q = me // 2
    t = nsrc // vox
    sl, vl = forward_voxel_field.shape
    ds = adjoint_voxel_field.shape[0]
    chunks = CHUNKS if ds % CHUNKS == 0 else 1
    r = ds // chunks
    n = t * r
    pair = [(j, j ^ 1) for j in range(vox)]

    def chip_perm(k):
        return [(g * 2 + p, ((g + k) % m) * 2 + p) for g in range(m) for p in range(2)]

    scaled = (forward_voxel_field.astype(jnp.float32) * voxel_input_vector[None, :]).astype(
        jnp.bfloat16
    )
    weight = measurement_weight.reshape(sl, t, ds)
    if grid is not None and grid[0] == t:
        na = grid[1]
        ia = lax.axis_index("src") // t

        def rel(blk):
            return (blk - ia) % na
    else:
        grid = None

        def rel(blk):
            return blk
    def gather(c):
        return _gather_src(adjoint_voxel_field[c * r:(c + 1) * r], grid)

    back = jnp.zeros((sl, vl), jnp.float32)
    nxt = gather(0)
    for c in range(chunks):
        adj = nxt

        def pblock(blk):
            return lax.dot_general(
                scaled, _rows(adj, rel(blk), n), (((1,), (1,)), ((), ())),
                preferred_element_type=jnp.float32,
            )

        keeps = [pblock(2 * ((q + k) % m) + par) for k in range(m)]
        sends = [pblock(2 * ((q + k) % m) + 1 - par) for k in range(m)]
        halves = [a + b for a, b in zip(keeps, lax.ppermute(tuple(sends), "vox", pair))]
        share = halves[0]
        for k in range(1, m):
            share = share + lax.ppermute(
                halves[k].astype(jnp.bfloat16), "vox", chip_perm(k)
            ).astype(jnp.float32)

        w_c = weight[:, :, c * r:(c + 1) * r].reshape(sl, n)
        wt = (w_c * share).astype(jnp.bfloat16)

        got = [(me, wt)]
        for k in range(1, m):
            got.append((2 * ((q - k) % m) + par, lax.ppermute(wt, "vox", chip_perm(k))))
        mine = lax.ppermute(tuple(w for _, w in got), "vox", pair)
        got = got + [(blk ^ 1, w) for (blk, _), w in zip(got, mine)]
        if c + 1 < chunks:
            nxt, ws = lax.optimization_barrier((gather(c + 1), [w for _, w in got]))
            got = [(blk, w) for (blk, _), w in zip(got, ws)]
        for blk, w in got:
            back = back + jnp.dot(w, _rows(adj, rel(blk), n), preferred_element_type=jnp.float32)

    local_sum = jnp.sum(forward_voxel_field.astype(jnp.float32) * back, axis=0)
    return _sum_over_src(local_sum)


def solution(mesh):
    placed = (P("src", "vox"), P("src", "vox"), P("vox"), P("src", "vox"))
    return jax.shard_map(
        functools.partial(per_device, _src_grid(mesh)), mesh=mesh, in_specs=placed, out_specs=P("vox"), check_vma=False
    )
```

```python
import functools

import jax
import jax.numpy as jnp
from jax import lax
from jax.sharding import PartitionSpec as P

CHUNKS = 2


def _rows(a, blk, n):
    return lax.dynamic_slice_in_dim(a, blk * n, n, axis=0)


def _src_grid(mesh):
    devs = mesh.devices
    ax = mesh.axis_names.index("src")
    row = [devs[(i,) + (0,) * (devs.ndim - 1)] if ax == 0 else None for i in range(devs.shape[0])]
    if ax != 0 or any(not hasattr(d, "coords") for d in row):
        return None
    co = [tuple(d.coords) for d in row]
    n = len(co)
    diff = [k for k in range(len(co[0])) if n > 1 and co[1][k] != co[0][k]]
    if len(diff) != 1:
        return None
    nb = 1
    while nb < n and co[nb][diff[0]] != co[0][diff[0]]:
        nb += 1
    if n % nb:
        return None
    na = n // nb

    def near(i, j):
        return sum(abs(a - b) for a, b in zip(co[i], co[j])) == 1

    for i in range(n):
        ia, ib = divmod(i, nb)
        if ib + 1 < nb and not near(i, i + 1):
            return None
        if ia + 1 < na and not near(i, i + nb):
            return None
    if nb != 2 or na < 2:
        return None
    return nb, na


def _gather_src(block, grid):
    if grid is None:
        return lax.all_gather(block, "src", axis=0, tiled=True)
    nb, na = grid
    me = lax.axis_index("src")
    ia, ib = me // nb, me % nb
    swap = [(i, i ^ 1) for i in range(na * nb)]

    def along(p, d):
        return [(p * nb + o, d * nb + o) for o in range(nb)]

    got = {}
    for sign in (1, -1):
        cur = block
        for s in range(1, na):
            pairs = []
            for p in range(na):
                if 0 <= p + sign < na and 0 <= p - sign * (s - 1) < na:
                    pairs.extend(along(p, p + sign))
            cur = lax.ppermute(cur, "src", pairs)
            got[(sign, s)] = cur
    col = [block] + [
        jnp.where(ia + k < na, got[(-1, k)], got[(1, na - k)]) for k in range(1, na)
    ]
    col = jnp.stack(col)
    other = lax.ppermute(col, "src", swap)
    first = ib == 0
    planes = jnp.stack([jnp.where(first, col, other), jnp.where(first, other, col)], axis=1)
    return planes.reshape((-1,) + block.shape[1:])


def _sum_over_src(v):
    n = lax.axis_size("src")
    me = lax.axis_index("src")
    got = [v] + [
        lax.ppermute(v, "src", [(i, (i - k) % n) for i in range(n)]) for k in range(1, n)
    ]
    ordered = jnp.roll(jnp.stack(got), me, axis=0)
    total = ordered[0]
    for a in range(1, n):
        total = total + ordered[a]
    return total


def per_device(grid, forward_voxel_field, adjoint_voxel_field, voxel_input_vector, measurement_weight):
    nsrc = lax.axis_size("src")
    vox = lax.axis_size("vox")
    me = lax.axis_index("vox")
    m = vox // 2
    par = me % 2
    q = me // 2
    t = nsrc // vox
    sl, vl = forward_voxel_field.shape
    ds = adjoint_voxel_field.shape[0]
    chunks = CHUNKS if ds % CHUNKS == 0 else 1
    r = ds // chunks
    n = t * r
    pair = [(j, j ^ 1) for j in range(vox)]

    def chip_perm(k):
        return [(g * 2 + p, ((g + k) % m) * 2 + p) for g in range(m) for p in range(2)]

    scaled = (forward_voxel_field.astype(jnp.float32) * voxel_input_vector[None, :]).astype(
        jnp.bfloat16
    )
    weight = measurement_weight.reshape(sl, t, ds)
    if grid is not None and grid[0] == t:
        na = grid[1]
        ia = lax.axis_index("src") // t

        def rel(blk):
            return (blk - ia) % na
    else:
        grid = None

        def rel(blk):
            return blk
    def gather(c):
        return _gather_src(adjoint_voxel_field[c * r:(c + 1) * r], grid)

    back = jnp.zeros((sl, vl), jnp.float32)
    nxt = gather(0)
    for c in range(chunks):
        adj = nxt

        def pblock(blk):
            return lax.dot_general(
                scaled, _rows(adj, rel(blk), n), (((1,), (1,)), ((), ())),
                preferred_element_type=jnp.float32,
            )

        keeps = [pblock(2 * ((q + k) % m) + par) for k in range(m)]
        sends = [pblock(2 * ((q + k) % m) + 1 - par) for k in range(m)]
        halves = [a + b for a, b in zip(keeps, lax.ppermute(tuple(sends), "vox", pair))]
        share = halves[0]
        for k in range(1, m):
            share = share + lax.ppermute(
                halves[k].astype(jnp.bfloat16), "vox", chip_perm(k)
            ).astype(jnp.float32)

        w_c = weight[:, :, c * r:(c + 1) * r].reshape(sl, n)
        wt = (w_c * share).astype(jnp.bfloat16)

        got = [(me, wt)]
        for k in range(1, m):
            got.append((2 * ((q - k) % m) + par, lax.ppermute(wt, "vox", chip_perm(k))))
        mine = lax.ppermute(tuple(w for _, w in got), "vox", pair)
        got = got + [(blk ^ 1, w) for (blk, _), w in zip(got, mine)]
        if c + 1 < chunks:
            nxt, ws = lax.optimization_barrier((gather(c + 1), [w for _, w in got]))
            got = [(blk, w) for (blk, _), w in zip(got, ws)]
        for blk, w in got:
            back = back + jnp.dot(w, _rows(adj, rel(blk), n), preferred_element_type=jnp.float32)

    local_sum = jnp.sum(forward_voxel_field.astype(jnp.float32) * back, axis=0)
    return _sum_over_src(local_sum)


def solution(mesh):
    placed = (P("src", "vox"), P("src", "vox"), P("vox"), P("src", "vox"))
    return jax.shard_map(
        functools.partial(per_device, _src_grid(mesh)), mesh=mesh, in_specs=placed, out_specs=P("vox"), check_vma=False
    )
```

```python
import functools

import jax
import jax.numpy as jnp
from jax import lax
from jax.sharding import PartitionSpec as P

CHUNKS = 2


def _rows(a, blk, n):
    return lax.dynamic_slice_in_dim(a, blk * n, n, axis=0)


def _src_grid(mesh):
    devs = mesh.devices
    ax = mesh.axis_names.index("src")
    row = [devs[(i,) + (0,) * (devs.ndim - 1)] if ax == 0 else None for i in range(devs.shape[0])]
    if ax != 0 or any(not hasattr(d, "coords") for d in row):
        return None
    co = [tuple(d.coords) for d in row]
    n = len(co)
    diff = [k for k in range(len(co[0])) if n > 1 and co[1][k] != co[0][k]]
    if len(diff) != 1:
        return None
    nb = 1
    while nb < n and co[nb][diff[0]] != co[0][diff[0]]:
        nb += 1
    if n % nb:
        return None
    na = n // nb

    def near(i, j):
        return sum(abs(a - b) for a, b in zip(co[i], co[j])) == 1

    for i in range(n):
        ia, ib = divmod(i, nb)
        if ib + 1 < nb and not near(i, i + 1):
            return None
        if ia + 1 < na and not near(i, i + nb):
            return None
    if nb != 2 or na < 2:
        return None
    return nb, na


def _gather_src(block, grid):
    if grid is None:
        return lax.all_gather(block, "src", axis=0, tiled=True)
    nb, na = grid
    me = lax.axis_index("src")
    ia, ib = me // nb, me % nb
    swap = [(i, i ^ 1) for i in range(na * nb)]

    def along(p, d):
        return [(p * nb + o, d * nb + o) for o in range(nb)]

    got = {}
    for sign in (1, -1):
        cur = block
        for s in range(1, na):
            pairs = []
            for p in range(na):
                if 0 <= p + sign < na and 0 <= p - sign * (s - 1) < na:
                    pairs.extend(along(p, p + sign))
            cur = lax.ppermute(cur, "src", pairs)
            got[(sign, s)] = cur
    col = [block] + [
        jnp.where(ia + k < na, got[(-1, k)], got[(1, na - k)]) for k in range(1, na)
    ]
    col = jnp.stack(col)
    other = lax.ppermute(col, "src", swap)
    first = ib == 0
    planes = jnp.stack([jnp.where(first, col, other), jnp.where(first, other, col)], axis=1)
    return planes.reshape((-1,) + block.shape[1:])


def _sum_over_src(v):
    n = lax.axis_size("src")
    if n & (n - 1):
        return lax.psum(v, "src")
    b = 1
    while b < n:
        v = v + lax.ppermute(v, "src", [(i, i ^ b) for i in range(n)])
        b *= 2
    return v


def _zline(block, na):
    me = lax.axis_index("src")
    ia = me // 2

    def along(p, d):
        return [(p * 2 + o, d * 2 + o) for o in range(2)]

    got = {}
    for sign in (1, -1):
        cur = block
        for s in range(1, na):
            pairs = []
            for p in range(na):
                if 0 <= p + sign < na and 0 <= p - sign * (s - 1) < na:
                    pairs.extend(along(p, p + sign))
            cur = lax.ppermute(cur, "src", pairs)
            got[(sign, s)] = cur
    col = [block] + [
        jnp.where(ia + k < na, got[(-1, k)], got[(1, na - k)]) for k in range(1, na)
    ]
    return jnp.concatenate(col, axis=0)


def _fast(na, forward_voxel_field, adjoint_voxel_field, voxel_input_vector, measurement_weight):
    vox = lax.axis_size("vox")
    me = lax.axis_index("vox")
    m = vox // 2
    par = me % 2
    q = me // 2
    si = lax.axis_index("src")
    ia = si // 2
    first = si % 2 == 0
    sl, vl = forward_voxel_field.shape
    ds = adjoint_voxel_field.shape[0]
    chunks = CHUNKS if ds % (CHUNKS * 8) == 0 else 1
    r = ds // chunks
    swap = [(i, i ^ 1) for i in range(2 * na)]
    pair = [(j, j ^ 1) for j in range(vox)]

    def chip_perm(k):
        return [(g * 2 + p, ((g + k) % m) * 2 + p) for g in range(m) for p in range(2)]

    def rows(col, blk):
        return lax.dynamic_slice_in_dim(col, ((blk - ia) % na) * r, r, axis=0)

    fwd = jnp.concatenate(
        [forward_voxel_field, lax.ppermute(forward_voxel_field, "src", swap)], axis=0
    )
    scaled = (fwd.astype(jnp.float32) * voxel_input_vector[None, :]).astype(jnp.bfloat16)
    weight = measurement_weight.reshape(sl, 2, ds)
    back = jnp.zeros((2 * sl, vl), jnp.float32)
    nxt = _zline(adjoint_voxel_field[:r], na)
    for c in range(chunks):
        col = nxt

        def pblock(blk):
            return lax.dot_general(
                scaled, rows(col, blk), (((1,), (1,)), ((), ())),
                preferred_element_type=jnp.float32,
            )

        keeps = [pblock(2 * ((q + k) % m) + par) for k in range(m)]
        sends = [pblock(2 * ((q + k) % m) + 1 - par) for k in range(m)]
        halves = [a + b for a, b in zip(keeps, lax.ppermute(tuple(sends), "vox", pair))]
        share = halves[0]
        for k in range(1, m):
            share = share + lax.ppermute(
                halves[k].astype(jnp.bfloat16), "vox", chip_perm(k)
            ).astype(jnp.float32)

        own, theirs = share[:sl], lax.ppermute(share[sl:], "src", swap)
        pred = jnp.stack([jnp.where(first, own, theirs), jnp.where(first, theirs, own)], axis=1)
        w_c = weight[:, :, c * r:(c + 1) * r]
        wt = (w_c * pred).astype(jnp.bfloat16)
        mine = jnp.where(first, wt[:, 0], wt[:, 1])
        other = jnp.where(first, wt[:, 1], wt[:, 0])
        piece = jnp.concatenate([mine, lax.ppermute(other, "src", swap)], axis=0)

        got = [(me, piece)]
        for k in range(1, m):
            got.append((2 * ((q - k) % m) + par, lax.ppermute(piece, "vox", chip_perm(k))))
        mates = lax.ppermute(tuple(w for _, w in got), "vox", pair)
        got = got + [(blk ^ 1, w) for (blk, _), w in zip(got, mates)]
        if c + 1 < chunks:
            nxt, ws = lax.optimization_barrier(
                (_zline(adjoint_voxel_field[(c + 1) * r:(c + 2) * r], na), [w for _, w in got])
            )
            got = [(blk, w) for (blk, _), w in zip(got, ws)]
        for blk, w in got:
            back = back + jnp.dot(w, rows(col, blk), preferred_element_type=jnp.float32)

    local_sum = jnp.sum(fwd.astype(jnp.float32) * back, axis=0)
    return _sum_over_src(local_sum)


def per_device(grid, forward_voxel_field, adjoint_voxel_field, voxel_input_vector, measurement_weight):
    nsrc = lax.axis_size("src")
    vox = lax.axis_size("vox")
    me = lax.axis_index("vox")
    m = vox // 2
    par = me % 2
    q = me // 2
    t = nsrc // vox
    sl, vl = forward_voxel_field.shape
    ds = adjoint_voxel_field.shape[0]
    chunks = CHUNKS if ds % CHUNKS == 0 else 1
    r = ds // chunks
    n = t * r
    pair = [(j, j ^ 1) for j in range(vox)]

    def chip_perm(k):
        return [(g * 2 + p, ((g + k) % m) * 2 + p) for g in range(m) for p in range(2)]

    scaled = (forward_voxel_field.astype(jnp.float32) * voxel_input_vector[None, :]).astype(
        jnp.bfloat16
    )
    weight = measurement_weight.reshape(sl, t, ds)
    if grid is not None and grid[0] == t:
        na = grid[1]
        ia = lax.axis_index("src") // t

        def rel(blk):
            return (blk - ia) % na
    else:
        grid = None

        def rel(blk):
            return blk
    def gather(c):
        return _gather_src(adjoint_voxel_field[c * r:(c + 1) * r], grid)

    back = jnp.zeros((sl, vl), jnp.float32)
    nxt = gather(0)
    for c in range(chunks):
        adj = nxt

        def pblock(blk):
            return lax.dot_general(
                scaled, _rows(adj, rel(blk), n), (((1,), (1,)), ((), ())),
                preferred_element_type=jnp.float32,
            )

        keeps = [pblock(2 * ((q + k) % m) + par) for k in range(m)]
        sends = [pblock(2 * ((q + k) % m) + 1 - par) for k in range(m)]
        halves = [a + b for a, b in zip(keeps, lax.ppermute(tuple(sends), "vox", pair))]
        share = halves[0]
        for k in range(1, m):
            share = share + lax.ppermute(
                halves[k].astype(jnp.bfloat16), "vox", chip_perm(k)
            ).astype(jnp.float32)

        w_c = weight[:, :, c * r:(c + 1) * r].reshape(sl, n)
        wt = (w_c * share).astype(jnp.bfloat16)

        got = [(me, wt)]
        for k in range(1, m):
            got.append((2 * ((q - k) % m) + par, lax.ppermute(wt, "vox", chip_perm(k))))
        mine = lax.ppermute(tuple(w for _, w in got), "vox", pair)
        got = got + [(blk ^ 1, w) for (blk, _), w in zip(got, mine)]
        if c + 1 < chunks:
            nxt, ws = lax.optimization_barrier((gather(c + 1), [w for _, w in got]))
            got = [(blk, w) for (blk, _), w in zip(got, ws)]
        for blk, w in got:
            back = back + jnp.dot(w, _rows(adj, rel(blk), n), preferred_element_type=jnp.float32)

    local_sum = jnp.sum(forward_voxel_field.astype(jnp.float32) * back, axis=0)
    return _sum_over_src(local_sum)


def solution(mesh):
    placed = (P("src", "vox"), P("src", "vox"), P("vox"), P("src", "vox"))
    grid = _src_grid(mesh)
    nsrc, vox = mesh.shape["src"], mesh.shape["vox"]
    if grid is not None and grid[0] == 2 and nsrc == 2 * vox and vox % 2 == 0 and grid[1] == vox:
        body = functools.partial(_fast, grid[1])
    else:
        body = functools.partial(per_device, None)
    return jax.shard_map(
        body, mesh=mesh, in_specs=placed, out_specs=P("vox"), check_vma=False
    )
```

```python
import functools

import jax
import jax.numpy as jnp
from jax import lax
from jax.sharding import PartitionSpec as P

CHUNKS = 1


def _rows(a, blk, n):
    return lax.dynamic_slice_in_dim(a, blk * n, n, axis=0)


def _src_grid(mesh):
    devs = mesh.devices
    ax = mesh.axis_names.index("src")
    row = [devs[(i,) + (0,) * (devs.ndim - 1)] if ax == 0 else None for i in range(devs.shape[0])]
    if ax != 0 or any(not hasattr(d, "coords") for d in row):
        return None
    co = [tuple(d.coords) for d in row]
    n = len(co)
    diff = [k for k in range(len(co[0])) if n > 1 and co[1][k] != co[0][k]]
    if len(diff) != 1:
        return None
    nb = 1
    while nb < n and co[nb][diff[0]] != co[0][diff[0]]:
        nb += 1
    if n % nb:
        return None
    na = n // nb

    def near(i, j):
        return sum(abs(a - b) for a, b in zip(co[i], co[j])) == 1

    for i in range(n):
        ia, ib = divmod(i, nb)
        if ib + 1 < nb and not near(i, i + 1):
            return None
        if ia + 1 < na and not near(i, i + nb):
            return None
    if nb != 2 or na < 2:
        return None
    return nb, na


def _gather_src(block, grid):
    if grid is None:
        return lax.all_gather(block, "src", axis=0, tiled=True)
    nb, na = grid
    me = lax.axis_index("src")
    ia, ib = me // nb, me % nb
    swap = [(i, i ^ 1) for i in range(na * nb)]

    def along(p, d):
        return [(p * nb + o, d * nb + o) for o in range(nb)]

    got = {}
    for sign in (1, -1):
        cur = block
        for s in range(1, na):
            pairs = []
            for p in range(na):
                if 0 <= p + sign < na and 0 <= p - sign * (s - 1) < na:
                    pairs.extend(along(p, p + sign))
            cur = lax.ppermute(cur, "src", pairs)
            got[(sign, s)] = cur
    col = [block] + [
        jnp.where(ia + k < na, got[(-1, k)], got[(1, na - k)]) for k in range(1, na)
    ]
    col = jnp.stack(col)
    other = lax.ppermute(col, "src", swap)
    first = ib == 0
    planes = jnp.stack([jnp.where(first, col, other), jnp.where(first, other, col)], axis=1)
    return planes.reshape((-1,) + block.shape[1:])


def _sum_over_src(v):
    n = lax.axis_size("src")
    if n & (n - 1):
        return lax.psum(v, "src")
    b = 1
    while b < n:
        v = v + lax.ppermute(v, "src", [(i, i ^ b) for i in range(n)])
        b *= 2
    return v


def _zline(block, na):
    me = lax.axis_index("src")
    ia = me // 2

    def along(p, d):
        return [(p * 2 + o, d * 2 + o) for o in range(2)]

    got = {}
    for sign in (1, -1):
        cur = block
        for s in range(1, na):
            pairs = []
            for p in range(na):
                if 0 <= p + sign < na and 0 <= p - sign * (s - 1) < na:
                    pairs.extend(along(p, p + sign))
            cur = lax.ppermute(cur, "src", pairs)
            got[(sign, s)] = cur
    col = [block] + [
        jnp.where(ia + k < na, got[(-1, k)], got[(1, na - k)]) for k in range(1, na)
    ]
    return jnp.concatenate(col, axis=0)


def _fast(na, forward_voxel_field, adjoint_voxel_field, voxel_input_vector, measurement_weight):
    vox = lax.axis_size("vox")
    me = lax.axis_index("vox")
    m = vox // 2
    par = me % 2
    q = me // 2
    si = lax.axis_index("src")
    ia = si // 2
    first = si % 2 == 0
    sl, vl = forward_voxel_field.shape
    ds = adjoint_voxel_field.shape[0]
    chunks = CHUNKS if ds % (CHUNKS * 8) == 0 else 1
    r = ds // chunks
    swap = [(i, i ^ 1) for i in range(2 * na)]
    pair = [(j, j ^ 1) for j in range(vox)]

    def chip_perm(k):
        return [(g * 2 + p, ((g + k) % m) * 2 + p) for g in range(m) for p in range(2)]

    def rows(col, blk):
        return lax.dynamic_slice_in_dim(col, ((blk - ia) % na) * r, r, axis=0)

    fwd = jnp.concatenate(
        [forward_voxel_field, lax.ppermute(forward_voxel_field, "src", swap)], axis=0
    )
    scaled = (fwd.astype(jnp.float32) * voxel_input_vector[None, :]).astype(jnp.bfloat16)
    weight = measurement_weight.reshape(sl, 2, ds)
    back = jnp.zeros((2 * sl, vl), jnp.float32)
    nxt = _zline(adjoint_voxel_field[:r], na)
    for c in range(chunks):
        col = nxt

        def pblock(blk):
            return lax.dot_general(
                scaled, rows(col, blk), (((1,), (1,)), ((), ())),
                preferred_element_type=jnp.float32,
            )

        keeps = [pblock(2 * ((q + k) % m) + par) for k in range(m)]
        sends = [pblock(2 * ((q + k) % m) + 1 - par) for k in range(m)]
        halves = [a + b for a, b in zip(keeps, lax.ppermute(tuple(sends), "vox", pair))]
        share = halves[0]
        for k in range(1, m):
            share = share + lax.ppermute(
                halves[k].astype(jnp.bfloat16), "vox", chip_perm(k)
            ).astype(jnp.float32)

        own, theirs = share[:sl], lax.ppermute(share[sl:], "src", swap)
        pred = jnp.stack([jnp.where(first, own, theirs), jnp.where(first, theirs, own)], axis=1)
        w_c = weight[:, :, c * r:(c + 1) * r]
        wt = (w_c * pred).astype(jnp.bfloat16)
        mine = jnp.where(first, wt[:, 0], wt[:, 1])
        other = jnp.where(first, wt[:, 1], wt[:, 0])
        piece = jnp.concatenate([mine, lax.ppermute(other, "src", swap)], axis=0)

        got = [(me, piece)]
        for k in range(1, m):
            got.append((2 * ((q - k) % m) + par, lax.ppermute(piece, "vox", chip_perm(k))))
        mates = lax.ppermute(tuple(w for _, w in got), "vox", pair)
        got = got + [(blk ^ 1, w) for (blk, _), w in zip(got, mates)]
        if c + 1 < chunks:
            nxt, ws = lax.optimization_barrier(
                (_zline(adjoint_voxel_field[(c + 1) * r:(c + 2) * r], na), [w for _, w in got])
            )
            got = [(blk, w) for (blk, _), w in zip(got, ws)]
        for blk, w in got:
            back = back + jnp.dot(w, rows(col, blk), preferred_element_type=jnp.float32)

    local_sum = jnp.sum(fwd.astype(jnp.float32) * back, axis=0)
    return _sum_over_src(local_sum)


def per_device(grid, forward_voxel_field, adjoint_voxel_field, voxel_input_vector, measurement_weight):
    nsrc = lax.axis_size("src")
    vox = lax.axis_size("vox")
    me = lax.axis_index("vox")
    m = vox // 2
    par = me % 2
    q = me // 2
    t = nsrc // vox
    sl, vl = forward_voxel_field.shape
    ds = adjoint_voxel_field.shape[0]
    chunks = CHUNKS if ds % CHUNKS == 0 else 1
    r = ds // chunks
    n = t * r
    pair = [(j, j ^ 1) for j in range(vox)]

    def chip_perm(k):
        return [(g * 2 + p, ((g + k) % m) * 2 + p) for g in range(m) for p in range(2)]

    scaled = (forward_voxel_field.astype(jnp.float32) * voxel_input_vector[None, :]).astype(
        jnp.bfloat16
    )
    weight = measurement_weight.reshape(sl, t, ds)
    if grid is not None and grid[0] == t:
        na = grid[1]
        ia = lax.axis_index("src") // t

        def rel(blk):
            return (blk - ia) % na
    else:
        grid = None

        def rel(blk):
            return blk
    def gather(c):
        return _gather_src(adjoint_voxel_field[c * r:(c + 1) * r], grid)

    back = jnp.zeros((sl, vl), jnp.float32)
    nxt = gather(0)
    for c in range(chunks):
        adj = nxt

        def pblock(blk):
            return lax.dot_general(
                scaled, _rows(adj, rel(blk), n), (((1,), (1,)), ((), ())),
                preferred_element_type=jnp.float32,
            )

        keeps = [pblock(2 * ((q + k) % m) + par) for k in range(m)]
        sends = [pblock(2 * ((q + k) % m) + 1 - par) for k in range(m)]
        halves = [a + b for a, b in zip(keeps, lax.ppermute(tuple(sends), "vox", pair))]
        share = halves[0]
        for k in range(1, m):
            share = share + lax.ppermute(
                halves[k].astype(jnp.bfloat16), "vox", chip_perm(k)
            ).astype(jnp.float32)

        w_c = weight[:, :, c * r:(c + 1) * r].reshape(sl, n)
        wt = (w_c * share).astype(jnp.bfloat16)

        got = [(me, wt)]
        for k in range(1, m):
            got.append((2 * ((q - k) % m) + par, lax.ppermute(wt, "vox", chip_perm(k))))
        mine = lax.ppermute(tuple(w for _, w in got), "vox", pair)
        got = got + [(blk ^ 1, w) for (blk, _), w in zip(got, mine)]
        if c + 1 < chunks:
            nxt, ws = lax.optimization_barrier((gather(c + 1), [w for _, w in got]))
            got = [(blk, w) for (blk, _), w in zip(got, ws)]
        for blk, w in got:
            back = back + jnp.dot(w, _rows(adj, rel(blk), n), preferred_element_type=jnp.float32)

    local_sum = jnp.sum(forward_voxel_field.astype(jnp.float32) * back, axis=0)
    return _sum_over_src(local_sum)


def solution(mesh):
    placed = (P("src", "vox"), P("src", "vox"), P("vox"), P("src", "vox"))
    grid = _src_grid(mesh)
    nsrc, vox = mesh.shape["src"], mesh.shape["vox"]
    if grid is not None and grid[0] == 2 and nsrc == 2 * vox and vox % 2 == 0 and grid[1] == vox:
        body = functools.partial(_fast, grid[1])
    else:
        body = functools.partial(per_device, None)
    return jax.shard_map(
        body, mesh=mesh, in_specs=placed, out_specs=P("vox"), check_vma=False
    )
```

```python
import functools

import jax
import jax.numpy as jnp
from jax import lax
from jax.sharding import PartitionSpec as P

CHUNKS = 2


def _rows(a, blk, n):
    return lax.dynamic_slice_in_dim(a, blk * n, n, axis=0)


def _src_grid(mesh):
    devs = mesh.devices
    ax = mesh.axis_names.index("src")
    row = [devs[(i,) + (0,) * (devs.ndim - 1)] if ax == 0 else None for i in range(devs.shape[0])]
    if ax != 0 or any(not hasattr(d, "coords") for d in row):
        return None
    co = [tuple(d.coords) for d in row]
    n = len(co)
    diff = [k for k in range(len(co[0])) if n > 1 and co[1][k] != co[0][k]]
    if len(diff) != 1:
        return None
    nb = 1
    while nb < n and co[nb][diff[0]] != co[0][diff[0]]:
        nb += 1
    if n % nb:
        return None
    na = n // nb

    def near(i, j):
        return sum(abs(a - b) for a, b in zip(co[i], co[j])) == 1

    for i in range(n):
        ia, ib = divmod(i, nb)
        if ib + 1 < nb and not near(i, i + 1):
            return None
        if ia + 1 < na and not near(i, i + nb):
            return None
    if nb != 2 or na < 2:
        return None
    return nb, na


def _gather_src(block, grid):
    if grid is None:
        return lax.all_gather(block, "src", axis=0, tiled=True)
    nb, na = grid
    me = lax.axis_index("src")
    ia, ib = me // nb, me % nb
    swap = [(i, i ^ 1) for i in range(na * nb)]

    def along(p, d):
        return [(p * nb + o, d * nb + o) for o in range(nb)]

    got = {}
    for sign in (1, -1):
        cur = block
        for s in range(1, na):
            pairs = []
            for p in range(na):
                if 0 <= p + sign < na and 0 <= p - sign * (s - 1) < na:
                    pairs.extend(along(p, p + sign))
            cur = lax.ppermute(cur, "src", pairs)
            got[(sign, s)] = cur
    col = [block] + [
        jnp.where(ia + k < na, got[(-1, k)], got[(1, na - k)]) for k in range(1, na)
    ]
    col = jnp.stack(col)
    other = lax.ppermute(col, "src", swap)
    first = ib == 0
    planes = jnp.stack([jnp.where(first, col, other), jnp.where(first, other, col)], axis=1)
    return planes.reshape((-1,) + block.shape[1:])


def _sum_over_src(v):
    n = lax.axis_size("src")
    if n & (n - 1):
        return lax.psum(v, "src")
    b = 1
    while b < n:
        v = v + lax.ppermute(v, "src", [(i, i ^ b) for i in range(n)])
        b *= 2
    return v


def per_device(grid, forward_voxel_field, adjoint_voxel_field, voxel_input_vector, measurement_weight):
    nsrc = lax.axis_size("src")
    vox = lax.axis_size("vox")
    me = lax.axis_index("vox")
    m = vox // 2
    par = me % 2
    q = me // 2
    t = nsrc // vox
    sl, vl = forward_voxel_field.shape
    ds = adjoint_voxel_field.shape[0]
    chunks = CHUNKS if ds % CHUNKS == 0 else 1
    r = ds // chunks
    n = t * r
    pair = [(j, j ^ 1) for j in range(vox)]

    def chip_perm(k):
        return [(g * 2 + p, ((g + k) % m) * 2 + p) for g in range(m) for p in range(2)]

    scaled = lax.optimization_barrier(
        (forward_voxel_field.astype(jnp.float32) * voxel_input_vector[None, :]).astype(jnp.bfloat16)
    )
    weight = measurement_weight.reshape(sl, t, ds)
    if grid is not None and grid[0] == t:
        na = grid[1]
        ia = lax.axis_index("src") // t

        def rel(blk):
            return (blk - ia) % na
    else:
        grid = None

        def rel(blk):
            return blk
    def gather(c):
        return _gather_src(adjoint_voxel_field[c * r:(c + 1) * r], grid)

    back = jnp.zeros((sl, vl), jnp.float32)
    nxt = gather(0)
    for c in range(chunks):
        adj = nxt

        def pblock(blk):
            return lax.dot_general(
                scaled, _rows(adj, rel(blk), n), (((1,), (1,)), ((), ())),
                preferred_element_type=jnp.float32,
            )

        keeps = [pblock(2 * ((q + k) % m) + par) for k in range(m)]
        sends = [pblock(2 * ((q + k) % m) + 1 - par) for k in range(m)]
        halves = [a + b for a, b in zip(keeps, lax.ppermute(tuple(sends), "vox", pair))]
        share = halves[0]
        for k in range(1, m):
            share = share + lax.ppermute(
                halves[k].astype(jnp.bfloat16), "vox", chip_perm(k)
            ).astype(jnp.float32)

        w_c = weight[:, :, c * r:(c + 1) * r].reshape(sl, n)
        wt = (w_c * share).astype(jnp.bfloat16)

        got = [(me, wt)]
        for k in range(1, m):
            got.append((2 * ((q - k) % m) + par, lax.ppermute(wt, "vox", chip_perm(k))))
        mine = lax.ppermute(tuple(w for _, w in got), "vox", pair)
        got = got + [(blk ^ 1, w) for (blk, _), w in zip(got, mine)]
        if c + 1 < chunks:
            nxt, ws = lax.optimization_barrier((gather(c + 1), [w for _, w in got]))
            got = [(blk, w) for (blk, _), w in zip(got, ws)]
        for blk, w in got:
            back = back + jnp.dot(w, _rows(adj, rel(blk), n), preferred_element_type=jnp.float32)

    local_sum = jnp.sum(forward_voxel_field.astype(jnp.float32) * back, axis=0)
    return _sum_over_src(local_sum)


def solution(mesh):
    placed = (P("src", "vox"), P("src", "vox"), P("vox"), P("src", "vox"))
    return jax.shard_map(
        functools.partial(per_device, _src_grid(mesh)), mesh=mesh, in_specs=placed, out_specs=P("vox"), check_vma=False
    )
```

```python
import functools

import jax
import jax.numpy as jnp
from jax import lax
from jax.sharding import PartitionSpec as P

CHUNKS = 2


def _rows(a, blk, n):
    return lax.dynamic_slice_in_dim(a, blk * n, n, axis=0)


def _src_grid(mesh):
    devs = mesh.devices
    ax = mesh.axis_names.index("src")
    row = [devs[(i,) + (0,) * (devs.ndim - 1)] if ax == 0 else None for i in range(devs.shape[0])]
    if ax != 0 or any(not hasattr(d, "coords") for d in row):
        return None
    co = [tuple(d.coords) for d in row]
    n = len(co)
    diff = [k for k in range(len(co[0])) if n > 1 and co[1][k] != co[0][k]]
    if len(diff) != 1:
        return None
    nb = 1
    while nb < n and co[nb][diff[0]] != co[0][diff[0]]:
        nb += 1
    if n % nb:
        return None
    na = n // nb

    def near(i, j):
        return sum(abs(a - b) for a, b in zip(co[i], co[j])) == 1

    for i in range(n):
        ia, ib = divmod(i, nb)
        if ib + 1 < nb and not near(i, i + 1):
            return None
        if ia + 1 < na and not near(i, i + nb):
            return None
    if nb != 2 or na < 2:
        return None
    return nb, na


def _gather_src(block, grid):
    if grid is None:
        return lax.all_gather(block, "src", axis=0, tiled=True)
    nb, na = grid
    me = lax.axis_index("src")
    ia, ib = me // nb, me % nb
    swap = [(i, i ^ 1) for i in range(na * nb)]

    def along(p, d):
        return [(p * nb + o, d * nb + o) for o in range(nb)]

    got = {}
    for sign in (1, -1):
        cur = block
        for s in range(1, na):
            pairs = []
            for p in range(na):
                if 0 <= p + sign < na and 0 <= p - sign * (s - 1) < na:
                    pairs.extend(along(p, p + sign))
            cur = lax.ppermute(cur, "src", pairs)
            got[(sign, s)] = cur
    col = [block] + [
        jnp.where(ia + k < na, got[(-1, k)], got[(1, na - k)]) for k in range(1, na)
    ]
    col = jnp.stack(col)
    other = lax.ppermute(col, "src", swap)
    first = ib == 0
    planes = jnp.stack([jnp.where(first, col, other), jnp.where(first, other, col)], axis=1)
    return planes.reshape((-1,) + block.shape[1:])


def _sum_over_src(v):
    n = lax.axis_size("src")
    if n & (n - 1):
        return lax.psum(v, "src")
    b = 1
    while b < n:
        v = v + lax.ppermute(v, "src", [(i, i ^ b) for i in range(n)])
        b *= 2
    return v


def _zline(block, na):
    me = lax.axis_index("src")
    ia = me // 2

    def along(p, d):
        return [(p * 2 + o, d * 2 + o) for o in range(2)]

    got = {}
    for sign in (1, -1):
        cur = block
        for s in range(1, na):
            pairs = []
            for p in range(na):
                if 0 <= p + sign < na and 0 <= p - sign * (s - 1) < na:
                    pairs.extend(along(p, p + sign))
            cur = lax.ppermute(cur, "src", pairs)
            got[(sign, s)] = cur
    col = [block] + [
        jnp.where(ia + k < na, got[(-1, k)], got[(1, na - k)]) for k in range(1, na)
    ]
    return jnp.concatenate(col, axis=0)


def _fast(na, forward_voxel_field, adjoint_voxel_field, voxel_input_vector, measurement_weight):
    vox = lax.axis_size("vox")
    me = lax.axis_index("vox")
    m = vox // 2
    par = me % 2
    q = me // 2
    si = lax.axis_index("src")
    ia = si // 2
    first = si % 2 == 0
    sl, vl = forward_voxel_field.shape
    ds = adjoint_voxel_field.shape[0]
    chunks = CHUNKS if ds % (CHUNKS * 8) == 0 else 1
    r = ds // chunks
    swap = [(i, i ^ 1) for i in range(2 * na)]
    pair = [(j, j ^ 1) for j in range(vox)]

    def chip_perm(k):
        return [(g * 2 + p, ((g + k) % m) * 2 + p) for g in range(m) for p in range(2)]

    def rows(col, blk):
        return lax.dynamic_slice_in_dim(col, ((blk - ia) % na) * r, r, axis=0)

    fwd = jnp.concatenate(
        [forward_voxel_field, lax.ppermute(forward_voxel_field, "src", swap)], axis=0
    )
    scaled = lax.optimization_barrier(
        (fwd.astype(jnp.float32) * voxel_input_vector[None, :]).astype(jnp.bfloat16)
    )
    weight = measurement_weight.reshape(sl, 2, ds)
    back = jnp.zeros((2 * sl, vl), jnp.float32)
    nxt = _zline(adjoint_voxel_field[:r], na)
    for c in range(chunks):
        col = nxt

        def pblock(blk):
            return lax.dot_general(
                scaled, rows(col, blk), (((1,), (1,)), ((), ())),
                preferred_element_type=jnp.float32,
            )

        keeps = [pblock(2 * ((q + k) % m) + par) for k in range(m)]
        sends = [pblock(2 * ((q + k) % m) + 1 - par) for k in range(m)]
        halves = [a + b for a, b in zip(keeps, lax.ppermute(tuple(sends), "vox", pair))]
        share = halves[0]
        for k in range(1, m):
            share = share + lax.ppermute(
                halves[k].astype(jnp.bfloat16), "vox", chip_perm(k)
            ).astype(jnp.float32)

        own, theirs = share[:sl], lax.ppermute(share[sl:], "src", swap)
        pred = jnp.stack([jnp.where(first, own, theirs), jnp.where(first, theirs, own)], axis=1)
        w_c = weight[:, :, c * r:(c + 1) * r]
        wt = (w_c * pred).astype(jnp.bfloat16)
        mine = jnp.where(first, wt[:, 0], wt[:, 1])
        other = jnp.where(first, wt[:, 1], wt[:, 0])
        piece = jnp.concatenate([mine, lax.ppermute(other, "src", swap)], axis=0)

        got = [(me, piece)]
        for k in range(1, m):
            got.append((2 * ((q - k) % m) + par, lax.ppermute(piece, "vox", chip_perm(k))))
        mates = lax.ppermute(tuple(w for _, w in got), "vox", pair)
        got = got + [(blk ^ 1, w) for (blk, _), w in zip(got, mates)]
        if c + 1 < chunks:
            nxt, ws = lax.optimization_barrier(
                (_zline(adjoint_voxel_field[(c + 1) * r:(c + 2) * r], na), [w for _, w in got])
            )
            got = [(blk, w) for (blk, _), w in zip(got, ws)]
        back = back + jnp.dot(
            jnp.concatenate([w for _, w in got], axis=1),
            jnp.concatenate([rows(col, blk) for blk, _ in got], axis=0),
            preferred_element_type=jnp.float32,
        )

    local_sum = jnp.sum(fwd.astype(jnp.float32) * back, axis=0)
    return _sum_over_src(local_sum)


def per_device(grid, forward_voxel_field, adjoint_voxel_field, voxel_input_vector, measurement_weight):
    nsrc = lax.axis_size("src")
    vox = lax.axis_size("vox")
    me = lax.axis_index("vox")
    m = vox // 2
    par = me % 2
    q = me // 2
    t = nsrc // vox
    sl, vl = forward_voxel_field.shape
    ds = adjoint_voxel_field.shape[0]
    chunks = CHUNKS if ds % CHUNKS == 0 else 1
    r = ds // chunks
    n = t * r
    pair = [(j, j ^ 1) for j in range(vox)]

    def chip_perm(k):
        return [(g * 2 + p, ((g + k) % m) * 2 + p) for g in range(m) for p in range(2)]

    scaled = (forward_voxel_field.astype(jnp.float32) * voxel_input_vector[None, :]).astype(
        jnp.bfloat16
    )
    weight = measurement_weight.reshape(sl, t, ds)
    if grid is not None and grid[0] == t:
        na = grid[1]
        ia = lax.axis_index("src") // t

        def rel(blk):
            return (blk - ia) % na
    else:
        grid = None

        def rel(blk):
            return blk
    def gather(c):
        return _gather_src(adjoint_voxel_field[c * r:(c + 1) * r], grid)

    back = jnp.zeros((sl, vl), jnp.float32)
    nxt = gather(0)
    for c in range(chunks):
        adj = nxt

        def pblock(blk):
            return lax.dot_general(
                scaled, _rows(adj, rel(blk), n), (((1,), (1,)), ((), ())),
                preferred_element_type=jnp.float32,
            )

        keeps = [pblock(2 * ((q + k) % m) + par) for k in range(m)]
        sends = [pblock(2 * ((q + k) % m) + 1 - par) for k in range(m)]
        halves = [a + b for a, b in zip(keeps, lax.ppermute(tuple(sends), "vox", pair))]
        share = halves[0]
        for k in range(1, m):
            share = share + lax.ppermute(
                halves[k].astype(jnp.bfloat16), "vox", chip_perm(k)
            ).astype(jnp.float32)

        w_c = weight[:, :, c * r:(c + 1) * r].reshape(sl, n)
        wt = (w_c * share).astype(jnp.bfloat16)

        got = [(me, wt)]
        for k in range(1, m):
            got.append((2 * ((q - k) % m) + par, lax.ppermute(wt, "vox", chip_perm(k))))
        mine = lax.ppermute(tuple(w for _, w in got), "vox", pair)
        got = got + [(blk ^ 1, w) for (blk, _), w in zip(got, mine)]
        if c + 1 < chunks:
            nxt, ws = lax.optimization_barrier((gather(c + 1), [w for _, w in got]))
            got = [(blk, w) for (blk, _), w in zip(got, ws)]
        for blk, w in got:
            back = back + jnp.dot(w, _rows(adj, rel(blk), n), preferred_element_type=jnp.float32)

    local_sum = jnp.sum(forward_voxel_field.astype(jnp.float32) * back, axis=0)
    return _sum_over_src(local_sum)


def solution(mesh):
    placed = (P("src", "vox"), P("src", "vox"), P("vox"), P("src", "vox"))
    grid = _src_grid(mesh)
    nsrc, vox = mesh.shape["src"], mesh.shape["vox"]
    if grid is not None and grid[0] == 2 and nsrc == 2 * vox and vox % 2 == 0 and grid[1] == vox:
        body = functools.partial(_fast, grid[1])
    else:
        body = functools.partial(per_device, None)
    return jax.shard_map(
        body, mesh=mesh, in_specs=placed, out_specs=P("vox"), check_vma=False
    )
```

```python
import functools

import jax
import jax.numpy as jnp
from jax import lax
from jax.sharding import PartitionSpec as P

CHUNKS = 2


def _rows(a, blk, n):
    return lax.dynamic_slice_in_dim(a, blk * n, n, axis=0)


def _src_grid(mesh):
    devs = mesh.devices
    ax = mesh.axis_names.index("src")
    row = [devs[(i,) + (0,) * (devs.ndim - 1)] if ax == 0 else None for i in range(devs.shape[0])]
    if ax != 0 or any(not hasattr(d, "coords") for d in row):
        return None
    co = [tuple(d.coords) for d in row]
    n = len(co)
    diff = [k for k in range(len(co[0])) if n > 1 and co[1][k] != co[0][k]]
    if len(diff) != 1:
        return None
    nb = 1
    while nb < n and co[nb][diff[0]] != co[0][diff[0]]:
        nb += 1
    if n % nb:
        return None
    na = n // nb

    def near(i, j):
        return sum(abs(a - b) for a, b in zip(co[i], co[j])) == 1

    for i in range(n):
        ia, ib = divmod(i, nb)
        if ib + 1 < nb and not near(i, i + 1):
            return None
        if ia + 1 < na and not near(i, i + nb):
            return None
    if nb != 2 or na < 2:
        return None
    return nb, na


def _gather_src(block, grid):
    if grid is None:
        return lax.all_gather(block, "src", axis=0, tiled=True)
    nb, na = grid
    me = lax.axis_index("src")
    ia, ib = me // nb, me % nb
    swap = [(i, i ^ 1) for i in range(na * nb)]

    def along(p, d):
        return [(p * nb + o, d * nb + o) for o in range(nb)]

    got = {}
    for sign in (1, -1):
        cur = block
        for s in range(1, na):
            pairs = []
            for p in range(na):
                if 0 <= p + sign < na and 0 <= p - sign * (s - 1) < na:
                    pairs.extend(along(p, p + sign))
            cur = lax.ppermute(cur, "src", pairs)
            got[(sign, s)] = cur
    col = [block] + [
        jnp.where(ia + k < na, got[(-1, k)], got[(1, na - k)]) for k in range(1, na)
    ]
    col = jnp.stack(col)
    other = lax.ppermute(col, "src", swap)
    first = ib == 0
    planes = jnp.stack([jnp.where(first, col, other), jnp.where(first, other, col)], axis=1)
    return planes.reshape((-1,) + block.shape[1:])


def _sum_over_src(v):
    n = lax.axis_size("src")
    if n & (n - 1):
        return lax.psum(v, "src")
    b = 1
    while b < n:
        v = v + lax.ppermute(v, "src", [(i, i ^ b) for i in range(n)])
        b *= 2
    return v


def _zline(block, na):
    me = lax.axis_index("src")
    ia = me // 2

    def along(p, d):
        return [(p * 2 + o, d * 2 + o) for o in range(2)]

    got = {}
    for sign in (1, -1):
        cur = block
        for s in range(1, na):
            pairs = []
            for p in range(na):
                if 0 <= p + sign < na and 0 <= p - sign * (s - 1) < na:
                    pairs.extend(along(p, p + sign))
            cur = lax.ppermute(cur, "src", pairs)
            got[(sign, s)] = cur
    col = [block] + [
        jnp.where(ia + k < na, got[(-1, k)], got[(1, na - k)]) for k in range(1, na)
    ]
    return jnp.concatenate(col, axis=0)


def _fast(na, forward_voxel_field, adjoint_voxel_field, voxel_input_vector, measurement_weight):
    vox = lax.axis_size("vox")
    me = lax.axis_index("vox")
    m = vox // 2
    par = me % 2
    q = me // 2
    si = lax.axis_index("src")
    ia = si // 2
    first = si % 2 == 0
    sl, vl = forward_voxel_field.shape
    ds = adjoint_voxel_field.shape[0]
    chunks = CHUNKS if ds % (CHUNKS * 8) == 0 else 1
    r = ds // chunks
    swap = [(i, i ^ 1) for i in range(2 * na)]
    pair = [(j, j ^ 1) for j in range(vox)]

    def chip_perm(k):
        return [(g * 2 + p, ((g + k) % m) * 2 + p) for g in range(m) for p in range(2)]

    def rows(col, blk):
        return lax.dynamic_slice_in_dim(col, ((blk - ia) % na) * r, r, axis=0)

    fwd = jnp.concatenate(
        [forward_voxel_field, lax.ppermute(forward_voxel_field, "src", swap)], axis=0
    )
    scaled = lax.optimization_barrier(
        (fwd.astype(jnp.float32) * voxel_input_vector[None, :]).astype(jnp.bfloat16)
    )
    weight = measurement_weight.reshape(sl, 2, ds)
    back = jnp.zeros((2 * sl, vl), jnp.float32)
    nxt = _zline(adjoint_voxel_field[:r], na)
    for c in range(chunks):
        col = nxt

        def pblock(blk):
            return lax.dot_general(
                scaled, rows(col, blk), (((1,), (1,)), ((), ())),
                preferred_element_type=jnp.float32,
            )

        keeps = [pblock(2 * ((q + k) % m) + par) for k in range(m)]
        sends = [pblock(2 * ((q + k) % m) + 1 - par) for k in range(m)]
        halves = [a + b for a, b in zip(keeps, lax.ppermute(tuple(sends), "vox", pair))]
        share = halves[0]
        for k in range(1, m):
            share = share + lax.ppermute(
                halves[k].astype(jnp.bfloat16), "vox", chip_perm(k)
            ).astype(jnp.float32)

        own = share[:sl]
        theirs = lax.ppermute(share[sl:].astype(jnp.bfloat16), "src", swap).astype(jnp.float32)
        pred = jnp.stack([jnp.where(first, own, theirs), jnp.where(first, theirs, own)], axis=1)
        w_c = weight[:, :, c * r:(c + 1) * r]
        wt = (w_c * pred).astype(jnp.bfloat16)
        mine = jnp.where(first, wt[:, 0], wt[:, 1])
        other = jnp.where(first, wt[:, 1], wt[:, 0])
        piece = jnp.concatenate([mine, lax.ppermute(other, "src", swap)], axis=0)

        got = [(me, piece)]
        for k in range(1, m):
            got.append((2 * ((q - k) % m) + par, lax.ppermute(piece, "vox", chip_perm(k))))
        mates = lax.ppermute(tuple(w for _, w in got), "vox", pair)
        got = got + [(blk ^ 1, w) for (blk, _), w in zip(got, mates)]
        if c + 1 < chunks:
            nxt, ws = lax.optimization_barrier(
                (_zline(adjoint_voxel_field[(c + 1) * r:(c + 2) * r], na), [w for _, w in got])
            )
            got = [(blk, w) for (blk, _), w in zip(got, ws)]
        back = back + jnp.dot(
            jnp.concatenate([w for _, w in got], axis=1),
            jnp.concatenate([rows(col, blk) for blk, _ in got], axis=0),
            preferred_element_type=jnp.float32,
        )

    local_sum = jnp.sum(fwd.astype(jnp.float32) * back, axis=0)
    return _sum_over_src(local_sum)


def per_device(grid, forward_voxel_field, adjoint_voxel_field, voxel_input_vector, measurement_weight):
    nsrc = lax.axis_size("src")
    vox = lax.axis_size("vox")
    me = lax.axis_index("vox")
    m = vox // 2
    par = me % 2
    q = me // 2
    t = nsrc // vox
    sl, vl = forward_voxel_field.shape
    ds = adjoint_voxel_field.shape[0]
    chunks = CHUNKS if ds % CHUNKS == 0 else 1
    r = ds // chunks
    n = t * r
    pair = [(j, j ^ 1) for j in range(vox)]

    def chip_perm(k):
        return [(g * 2 + p, ((g + k) % m) * 2 + p) for g in range(m) for p in range(2)]

    scaled = (forward_voxel_field.astype(jnp.float32) * voxel_input_vector[None, :]).astype(
        jnp.bfloat16
    )
    weight = measurement_weight.reshape(sl, t, ds)
    if grid is not None and grid[0] == t:
        na = grid[1]
        ia = lax.axis_index("src") // t

        def rel(blk):
            return (blk - ia) % na
    else:
        grid = None

        def rel(blk):
            return blk
    def gather(c):
        return _gather_src(adjoint_voxel_field[c * r:(c + 1) * r], grid)

    back = jnp.zeros((sl, vl), jnp.float32)
    nxt = gather(0)
    for c in range(chunks):
        adj = nxt

        def pblock(blk):
            return lax.dot_general(
                scaled, _rows(adj, rel(blk), n), (((1,), (1,)), ((), ())),
                preferred_element_type=jnp.float32,
            )

        keeps = [pblock(2 * ((q + k) % m) + par) for k in range(m)]
        sends = [pblock(2 * ((q + k) % m) + 1 - par) for k in range(m)]
        halves = [a + b for a, b in zip(keeps, lax.ppermute(tuple(sends), "vox", pair))]
        share = halves[0]
        for k in range(1, m):
            share = share + lax.ppermute(
                halves[k].astype(jnp.bfloat16), "vox", chip_perm(k)
            ).astype(jnp.float32)

        w_c = weight[:, :, c * r:(c + 1) * r].reshape(sl, n)
        wt = (w_c * share).astype(jnp.bfloat16)

        got = [(me, wt)]
        for k in range(1, m):
            got.append((2 * ((q - k) % m) + par, lax.ppermute(wt, "vox", chip_perm(k))))
        mine = lax.ppermute(tuple(w for _, w in got), "vox", pair)
        got = got + [(blk ^ 1, w) for (blk, _), w in zip(got, mine)]
        if c + 1 < chunks:
            nxt, ws = lax.optimization_barrier((gather(c + 1), [w for _, w in got]))
            got = [(blk, w) for (blk, _), w in zip(got, ws)]
        for blk, w in got:
            back = back + jnp.dot(w, _rows(adj, rel(blk), n), preferred_element_type=jnp.float32)

    local_sum = jnp.sum(forward_voxel_field.astype(jnp.float32) * back, axis=0)
    return _sum_over_src(local_sum)


def solution(mesh):
    placed = (P("src", "vox"), P("src", "vox"), P("vox"), P("src", "vox"))
    grid = _src_grid(mesh)
    nsrc, vox = mesh.shape["src"], mesh.shape["vox"]
    if grid is not None and grid[0] == 2 and nsrc == 2 * vox and vox % 2 == 0 and grid[1] == vox:
        body = functools.partial(_fast, grid[1])
    else:
        body = functools.partial(per_device, None)
    return jax.shard_map(
        body, mesh=mesh, in_specs=placed, out_specs=P("vox"), check_vma=False
    )
```

```python
import functools

import jax
import jax.numpy as jnp
from jax import lax
from jax.sharding import PartitionSpec as P

CHUNKS = 4


def _rows(a, blk, n):
    return lax.dynamic_slice_in_dim(a, blk * n, n, axis=0)


def _src_grid(mesh):
    devs = mesh.devices
    ax = mesh.axis_names.index("src")
    row = [devs[(i,) + (0,) * (devs.ndim - 1)] if ax == 0 else None for i in range(devs.shape[0])]
    if ax != 0 or any(not hasattr(d, "coords") for d in row):
        return None
    co = [tuple(d.coords) for d in row]
    n = len(co)
    diff = [k for k in range(len(co[0])) if n > 1 and co[1][k] != co[0][k]]
    if len(diff) != 1:
        return None
    nb = 1
    while nb < n and co[nb][diff[0]] != co[0][diff[0]]:
        nb += 1
    if n % nb:
        return None
    na = n // nb

    def near(i, j):
        return sum(abs(a - b) for a, b in zip(co[i], co[j])) == 1

    for i in range(n):
        ia, ib = divmod(i, nb)
        if ib + 1 < nb and not near(i, i + 1):
            return None
        if ia + 1 < na and not near(i, i + nb):
            return None
    if nb != 2 or na < 2:
        return None
    return nb, na


def _gather_src(block, grid):
    if grid is None:
        return lax.all_gather(block, "src", axis=0, tiled=True)
    nb, na = grid
    me = lax.axis_index("src")
    ia, ib = me // nb, me % nb
    swap = [(i, i ^ 1) for i in range(na * nb)]

    def along(p, d):
        return [(p * nb + o, d * nb + o) for o in range(nb)]

    got = {}
    for sign in (1, -1):
        cur = block
        for s in range(1, na):
            pairs = []
            for p in range(na):
                if 0 <= p + sign < na and 0 <= p - sign * (s - 1) < na:
                    pairs.extend(along(p, p + sign))
            cur = lax.ppermute(cur, "src", pairs)
            got[(sign, s)] = cur
    col = [block] + [
        jnp.where(ia + k < na, got[(-1, k)], got[(1, na - k)]) for k in range(1, na)
    ]
    col = jnp.stack(col)
    other = lax.ppermute(col, "src", swap)
    first = ib == 0
    planes = jnp.stack([jnp.where(first, col, other), jnp.where(first, other, col)], axis=1)
    return planes.reshape((-1,) + block.shape[1:])


def _sum_over_src(v):
    n = lax.axis_size("src")
    if n & (n - 1):
        return lax.psum(v, "src")
    b = 1
    while b < n:
        v = v + lax.ppermute(v, "src", [(i, i ^ b) for i in range(n)])
        b *= 2
    return v


def _zline(block, na):
    me = lax.axis_index("src")
    ia = me // 2

    def along(p, d):
        return [(p * 2 + o, d * 2 + o) for o in range(2)]

    got = {}
    for sign in (1, -1):
        cur = block
        for s in range(1, na):
            pairs = []
            for p in range(na):
                if 0 <= p + sign < na and 0 <= p - sign * (s - 1) < na:
                    pairs.extend(along(p, p + sign))
            cur = lax.ppermute(cur, "src", pairs)
            got[(sign, s)] = cur
    col = [block] + [
        jnp.where(ia + k < na, got[(-1, k)], got[(1, na - k)]) for k in range(1, na)
    ]
    return jnp.concatenate(col, axis=0)


def _fast(na, forward_voxel_field, adjoint_voxel_field, voxel_input_vector, measurement_weight):
    vox = lax.axis_size("vox")
    me = lax.axis_index("vox")
    m = vox // 2
    par = me % 2
    q = me // 2
    si = lax.axis_index("src")
    ia = si // 2
    first = si % 2 == 0
    sl, vl = forward_voxel_field.shape
    ds = adjoint_voxel_field.shape[0]
    chunks = CHUNKS if ds % (CHUNKS * 8) == 0 else 1
    r = ds // chunks
    swap = [(i, i ^ 1) for i in range(2 * na)]
    pair = [(j, j ^ 1) for j in range(vox)]

    def chip_perm(k):
        return [(g * 2 + p, ((g + k) % m) * 2 + p) for g in range(m) for p in range(2)]

    def rows(col, blk):
        return lax.dynamic_slice_in_dim(col, ((blk - ia) % na) * r, r, axis=0)

    fwd = jnp.concatenate(
        [forward_voxel_field, lax.ppermute(forward_voxel_field, "src", swap)], axis=0
    )
    scaled = lax.optimization_barrier(
        (fwd.astype(jnp.float32) * voxel_input_vector[None, :]).astype(jnp.bfloat16)
    )
    weight = measurement_weight.reshape(sl, 2, ds)
    back = jnp.zeros((2 * sl, vl), jnp.float32)
    nxt = _zline(adjoint_voxel_field[:r], na)
    for c in range(chunks):
        col = nxt

        def pblock(blk):
            return lax.dot_general(
                scaled, rows(col, blk), (((1,), (1,)), ((), ())),
                preferred_element_type=jnp.float32,
            )

        keeps = [pblock(2 * ((q + k) % m) + par) for k in range(m)]
        sends = [pblock(2 * ((q + k) % m) + 1 - par) for k in range(m)]
        halves = [a + b for a, b in zip(keeps, lax.ppermute(tuple(sends), "vox", pair))]
        share = halves[0]
        for k in range(1, m):
            share = share + lax.ppermute(
                halves[k].astype(jnp.bfloat16), "vox", chip_perm(k)
            ).astype(jnp.float32)

        own = share[:sl]
        theirs = lax.ppermute(share[sl:].astype(jnp.bfloat16), "src", swap).astype(jnp.float32)
        pred = jnp.stack([jnp.where(first, own, theirs), jnp.where(first, theirs, own)], axis=1)
        w_c = weight[:, :, c * r:(c + 1) * r]
        wt = (w_c * pred).astype(jnp.bfloat16)
        mine = jnp.where(first, wt[:, 0], wt[:, 1])
        other = jnp.where(first, wt[:, 1], wt[:, 0])
        piece = jnp.concatenate([mine, lax.ppermute(other, "src", swap)], axis=0)

        got = [(me, piece)]
        for k in range(1, m):
            got.append((2 * ((q - k) % m) + par, lax.ppermute(piece, "vox", chip_perm(k))))
        mates = lax.ppermute(tuple(w for _, w in got), "vox", pair)
        got = got + [(blk ^ 1, w) for (blk, _), w in zip(got, mates)]
        if c + 1 < chunks:
            nxt, ws = lax.optimization_barrier(
                (_zline(adjoint_voxel_field[(c + 1) * r:(c + 2) * r], na), [w for _, w in got])
            )
            got = [(blk, w) for (blk, _), w in zip(got, ws)]
        back = back + jnp.dot(
            jnp.concatenate([w for _, w in got], axis=1),
            jnp.concatenate([rows(col, blk) for blk, _ in got], axis=0),
            preferred_element_type=jnp.float32,
        )

    local_sum = jnp.sum(fwd.astype(jnp.float32) * back, axis=0)
    return _sum_over_src(local_sum)


def per_device(grid, forward_voxel_field, adjoint_voxel_field, voxel_input_vector, measurement_weight):
    nsrc = lax.axis_size("src")
    vox = lax.axis_size("vox")
    me = lax.axis_index("vox")
    m = vox // 2
    par = me % 2
    q = me // 2
    t = nsrc // vox
    sl, vl = forward_voxel_field.shape
    ds = adjoint_voxel_field.shape[0]
    chunks = CHUNKS if ds % CHUNKS == 0 else 1
    r = ds // chunks
    n = t * r
    pair = [(j, j ^ 1) for j in range(vox)]

    def chip_perm(k):
        return [(g * 2 + p, ((g + k) % m) * 2 + p) for g in range(m) for p in range(2)]

    scaled = (forward_voxel_field.astype(jnp.float32) * voxel_input_vector[None, :]).astype(
        jnp.bfloat16
    )
    weight = measurement_weight.reshape(sl, t, ds)
    if grid is not None and grid[0] == t:
        na = grid[1]
        ia = lax.axis_index("src") // t

        def rel(blk):
            return (blk - ia) % na
    else:
        grid = None

        def rel(blk):
            return blk
    def gather(c):
        return _gather_src(adjoint_voxel_field[c * r:(c + 1) * r], grid)

    back = jnp.zeros((sl, vl), jnp.float32)
    nxt = gather(0)
    for c in range(chunks):
        adj = nxt

        def pblock(blk):
            return lax.dot_general(
                scaled, _rows(adj, rel(blk), n), (((1,), (1,)), ((), ())),
                preferred_element_type=jnp.float32,
            )

        keeps = [pblock(2 * ((q + k) % m) + par) for k in range(m)]
        sends = [pblock(2 * ((q + k) % m) + 1 - par) for k in range(m)]
        halves = [a + b for a, b in zip(keeps, lax.ppermute(tuple(sends), "vox", pair))]
        share = halves[0]
        for k in range(1, m):
            share = share + lax.ppermute(
                halves[k].astype(jnp.bfloat16), "vox", chip_perm(k)
            ).astype(jnp.float32)

        w_c = weight[:, :, c * r:(c + 1) * r].reshape(sl, n)
        wt = (w_c * share).astype(jnp.bfloat16)

        got = [(me, wt)]
        for k in range(1, m):
            got.append((2 * ((q - k) % m) + par, lax.ppermute(wt, "vox", chip_perm(k))))
        mine = lax.ppermute(tuple(w for _, w in got), "vox", pair)
        got = got + [(blk ^ 1, w) for (blk, _), w in zip(got, mine)]
        if c + 1 < chunks:
            nxt, ws = lax.optimization_barrier((gather(c + 1), [w for _, w in got]))
            got = [(blk, w) for (blk, _), w in zip(got, ws)]
        for blk, w in got:
            back = back + jnp.dot(w, _rows(adj, rel(blk), n), preferred_element_type=jnp.float32)

    local_sum = jnp.sum(forward_voxel_field.astype(jnp.float32) * back, axis=0)
    return _sum_over_src(local_sum)


def solution(mesh):
    placed = (P("src", "vox"), P("src", "vox"), P("vox"), P("src", "vox"))
    grid = _src_grid(mesh)
    nsrc, vox = mesh.shape["src"], mesh.shape["vox"]
    if grid is not None and grid[0] == 2 and nsrc == 2 * vox and vox % 2 == 0 and grid[1] == vox:
        body = functools.partial(_fast, grid[1])
    else:
        body = functools.partial(per_device, None)
    return jax.shard_map(
        body, mesh=mesh, in_specs=placed, out_specs=P("vox"), check_vma=False
    )
```

```python
import functools

import jax
import jax.numpy as jnp
from jax import lax
from jax.sharding import PartitionSpec as P

CHUNKS = 2


def _rows(a, blk, n):
    return lax.dynamic_slice_in_dim(a, blk * n, n, axis=0)


def _src_grid(mesh):
    devs = mesh.devices
    ax = mesh.axis_names.index("src")
    row = [devs[(i,) + (0,) * (devs.ndim - 1)] if ax == 0 else None for i in range(devs.shape[0])]
    if ax != 0 or any(not hasattr(d, "coords") for d in row):
        return None
    co = [tuple(d.coords) for d in row]
    n = len(co)
    diff = [k for k in range(len(co[0])) if n > 1 and co[1][k] != co[0][k]]
    if len(diff) != 1:
        return None
    nb = 1
    while nb < n and co[nb][diff[0]] != co[0][diff[0]]:
        nb += 1
    if n % nb:
        return None
    na = n // nb

    def near(i, j):
        return sum(abs(a - b) for a, b in zip(co[i], co[j])) == 1

    for i in range(n):
        ia, ib = divmod(i, nb)
        if ib + 1 < nb and not near(i, i + 1):
            return None
        if ia + 1 < na and not near(i, i + nb):
            return None
    if nb != 2 or na < 2:
        return None
    return nb, na


def _gather_src(block, grid):
    if grid is None:
        return lax.all_gather(block, "src", axis=0, tiled=True)
    nb, na = grid
    me = lax.axis_index("src")
    ia, ib = me // nb, me % nb
    swap = [(i, i ^ 1) for i in range(na * nb)]

    def along(p, d):
        return [(p * nb + o, d * nb + o) for o in range(nb)]

    got = {}
    for sign in (1, -1):
        cur = block
        for s in range(1, na):
            pairs = []
            for p in range(na):
                if 0 <= p + sign < na and 0 <= p - sign * (s - 1) < na:
                    pairs.extend(along(p, p + sign))
            cur = lax.ppermute(cur, "src", pairs)
            got[(sign, s)] = cur
    col = [block] + [
        jnp.where(ia + k < na, got[(-1, k)], got[(1, na - k)]) for k in range(1, na)
    ]
    col = jnp.stack(col)
    other = lax.ppermute(col, "src", swap)
    first = ib == 0
    planes = jnp.stack([jnp.where(first, col, other), jnp.where(first, other, col)], axis=1)
    return planes.reshape((-1,) + block.shape[1:])


def _sum_over_src(v):
    n = lax.axis_size("src")
    if n & (n - 1):
        return lax.psum(v, "src")
    b = 1
    while b < n:
        v = v + lax.ppermute(v, "src", [(i, i ^ b) for i in range(n)])
        b *= 2
    return v


def _zline(block, na):
    me = lax.axis_index("src")
    ia = me // 2

    def along(p, d):
        return [(p * 2 + o, d * 2 + o) for o in range(2)]

    got = {}
    for sign in (1, -1):
        cur = block
        for s in range(1, na):
            pairs = []
            for p in range(na):
                if 0 <= p + sign < na and 0 <= p - sign * (s - 1) < na:
                    pairs.extend(along(p, p + sign))
            cur = lax.ppermute(cur, "src", pairs)
            got[(sign, s)] = cur
    col = [block] + [
        jnp.where(ia + k < na, got[(-1, k)], got[(1, na - k)]) for k in range(1, na)
    ]
    return jnp.concatenate(col, axis=0)


def _fast(na, forward_voxel_field, adjoint_voxel_field, voxel_input_vector, measurement_weight):
    vox = lax.axis_size("vox")
    me = lax.axis_index("vox")
    m = vox // 2
    par = me % 2
    q = me // 2
    si = lax.axis_index("src")
    ia = si // 2
    first = si % 2 == 0
    sl, vl = forward_voxel_field.shape
    ds = adjoint_voxel_field.shape[0]
    chunks = CHUNKS if ds % (CHUNKS * 8) == 0 else 1
    r = ds // chunks
    swap = [(i, i ^ 1) for i in range(2 * na)]
    pair = [(j, j ^ 1) for j in range(vox)]

    def chip_perm(k):
        return [(g * 2 + p, ((g + k) % m) * 2 + p) for g in range(m) for p in range(2)]

    def rows(col, blk):
        return lax.dynamic_slice_in_dim(col, ((blk - ia) % na) * r, r, axis=0)

    fwd = jnp.concatenate(
        [forward_voxel_field, lax.ppermute(forward_voxel_field, "src", swap)], axis=0
    )
    scaled = lax.optimization_barrier(
        (fwd.astype(jnp.float32) * voxel_input_vector[None, :]).astype(jnp.bfloat16)
    )
    weight = measurement_weight.reshape(sl, 2, ds)
    w_mine = jnp.where(first, weight[:, 0], weight[:, 1])
    w_other = jnp.where(first, weight[:, 1], weight[:, 0])
    weight = jnp.concatenate([w_mine, lax.ppermute(w_other, "src", swap)], axis=0)
    back = jnp.zeros((2 * sl, vl), jnp.float32)
    nxt = _zline(adjoint_voxel_field[:r], na)
    for c in range(chunks):
        col = nxt

        def pblock(blk):
            return lax.dot_general(
                scaled, rows(col, blk), (((1,), (1,)), ((), ())),
                preferred_element_type=jnp.float32,
            )

        keeps = [pblock(2 * ((q + k) % m) + par) for k in range(m)]
        sends = [pblock(2 * ((q + k) % m) + 1 - par) for k in range(m)]
        halves = [a + b for a, b in zip(keeps, lax.ppermute(tuple(sends), "vox", pair))]
        share = halves[0]
        for k in range(1, m):
            share = share + lax.ppermute(
                halves[k].astype(jnp.bfloat16), "vox", chip_perm(k)
            ).astype(jnp.float32)

        piece = (weight[:, c * r:(c + 1) * r] * share).astype(jnp.bfloat16)

        got = [(me, piece)]
        for k in range(1, m):
            got.append((2 * ((q - k) % m) + par, lax.ppermute(piece, "vox", chip_perm(k))))
        mates = lax.ppermute(tuple(w for _, w in got), "vox", pair)
        got = got + [(blk ^ 1, w) for (blk, _), w in zip(got, mates)]
        if c + 1 < chunks:
            nxt, ws = lax.optimization_barrier(
                (_zline(adjoint_voxel_field[(c + 1) * r:(c + 2) * r], na), [w for _, w in got])
            )
            got = [(blk, w) for (blk, _), w in zip(got, ws)]
        back = back + jnp.dot(
            jnp.concatenate([w for _, w in got], axis=1),
            jnp.concatenate([rows(col, blk) for blk, _ in got], axis=0),
            preferred_element_type=jnp.float32,
        )

    local_sum = jnp.sum(fwd.astype(jnp.float32) * back, axis=0)
    return _sum_over_src(local_sum)


def per_device(grid, forward_voxel_field, adjoint_voxel_field, voxel_input_vector, measurement_weight):
    nsrc = lax.axis_size("src")
    vox = lax.axis_size("vox")
    me = lax.axis_index("vox")
    m = vox // 2
    par = me % 2
    q = me // 2
    t = nsrc // vox
    sl, vl = forward_voxel_field.shape
    ds = adjoint_voxel_field.shape[0]
    chunks = CHUNKS if ds % CHUNKS == 0 else 1
    r = ds // chunks
    n = t * r
    pair = [(j, j ^ 1) for j in range(vox)]

    def chip_perm(k):
        return [(g * 2 + p, ((g + k) % m) * 2 + p) for g in range(m) for p in range(2)]

    scaled = (forward_voxel_field.astype(jnp.float32) * voxel_input_vector[None, :]).astype(
        jnp.bfloat16
    )
    weight = measurement_weight.reshape(sl, t, ds)
    if grid is not None and grid[0] == t:
        na = grid[1]
        ia = lax.axis_index("src") // t

        def rel(blk):
            return (blk - ia) % na
    else:
        grid = None

        def rel(blk):
            return blk
    def gather(c):
        return _gather_src(adjoint_voxel_field[c * r:(c + 1) * r], grid)

    back = jnp.zeros((sl, vl), jnp.float32)
    nxt = gather(0)
    for c in range(chunks):
        adj = nxt

        def pblock(blk):
            return lax.dot_general(
                scaled, _rows(adj, rel(blk), n), (((1,), (1,)), ((), ())),
                preferred_element_type=jnp.float32,
            )

        keeps = [pblock(2 * ((q + k) % m) + par) for k in range(m)]
        sends = [pblock(2 * ((q + k) % m) + 1 - par) for k in range(m)]
        halves = [a + b for a, b in zip(keeps, lax.ppermute(tuple(sends), "vox", pair))]
        share = halves[0]
        for k in range(1, m):
            share = share + lax.ppermute(
                halves[k].astype(jnp.bfloat16), "vox", chip_perm(k)
            ).astype(jnp.float32)

        w_c = weight[:, :, c * r:(c + 1) * r].reshape(sl, n)
        wt = (w_c * share).astype(jnp.bfloat16)

        got = [(me, wt)]
        for k in range(1, m):
            got.append((2 * ((q - k) % m) + par, lax.ppermute(wt, "vox", chip_perm(k))))
        mine = lax.ppermute(tuple(w for _, w in got), "vox", pair)
        got = got + [(blk ^ 1, w) for (blk, _), w in zip(got, mine)]
        if c + 1 < chunks:
            nxt, ws = lax.optimization_barrier((gather(c + 1), [w for _, w in got]))
            got = [(blk, w) for (blk, _), w in zip(got, ws)]
        for blk, w in got:
            back = back + jnp.dot(w, _rows(adj, rel(blk), n), preferred_element_type=jnp.float32)

    local_sum = jnp.sum(forward_voxel_field.astype(jnp.float32) * back, axis=0)
    return _sum_over_src(local_sum)


def solution(mesh):
    placed = (P("src", "vox"), P("src", "vox"), P("vox"), P("src", "vox"))
    grid = _src_grid(mesh)
    nsrc, vox = mesh.shape["src"], mesh.shape["vox"]
    if grid is not None and grid[0] == 2 and nsrc == 2 * vox and vox % 2 == 0 and grid[1] == vox:
        body = functools.partial(_fast, grid[1])
    else:
        body = functools.partial(per_device, None)
    return jax.shard_map(
        body, mesh=mesh, in_specs=placed, out_specs=P("vox"), check_vma=False
    )
```

```python
import functools

import jax
import jax.numpy as jnp
from jax import lax
from jax.sharding import PartitionSpec as P

CHUNKS = 1


def _rows(a, blk, n):
    return lax.dynamic_slice_in_dim(a, blk * n, n, axis=0)


def _src_grid(mesh):
    devs = mesh.devices
    ax = mesh.axis_names.index("src")
    row = [devs[(i,) + (0,) * (devs.ndim - 1)] if ax == 0 else None for i in range(devs.shape[0])]
    if ax != 0 or any(not hasattr(d, "coords") for d in row):
        return None
    co = [tuple(d.coords) for d in row]
    n = len(co)
    diff = [k for k in range(len(co[0])) if n > 1 and co[1][k] != co[0][k]]
    if len(diff) != 1:
        return None
    nb = 1
    while nb < n and co[nb][diff[0]] != co[0][diff[0]]:
        nb += 1
    if n % nb:
        return None
    na = n // nb

    def near(i, j):
        return sum(abs(a - b) for a, b in zip(co[i], co[j])) == 1

    for i in range(n):
        ia, ib = divmod(i, nb)
        if ib + 1 < nb and not near(i, i + 1):
            return None
        if ia + 1 < na and not near(i, i + nb):
            return None
    if nb != 2 or na < 2:
        return None
    return nb, na


def _gather_src(block, grid):
    if grid is None:
        return lax.all_gather(block, "src", axis=0, tiled=True)
    nb, na = grid
    me = lax.axis_index("src")
    ia, ib = me // nb, me % nb
    swap = [(i, i ^ 1) for i in range(na * nb)]

    def along(p, d):
        return [(p * nb + o, d * nb + o) for o in range(nb)]

    got = {}
    for sign in (1, -1):
        cur = block
        for s in range(1, na):
            pairs = []
            for p in range(na):
                if 0 <= p + sign < na and 0 <= p - sign * (s - 1) < na:
                    pairs.extend(along(p, p + sign))
            cur = lax.ppermute(cur, "src", pairs)
            got[(sign, s)] = cur
    col = [block] + [
        jnp.where(ia + k < na, got[(-1, k)], got[(1, na - k)]) for k in range(1, na)
    ]
    col = jnp.stack(col)
    other = lax.ppermute(col, "src", swap)
    first = ib == 0
    planes = jnp.stack([jnp.where(first, col, other), jnp.where(first, other, col)], axis=1)
    return planes.reshape((-1,) + block.shape[1:])


def _sum_over_src(v):
    n = lax.axis_size("src")
    if n & (n - 1):
        return lax.psum(v, "src")
    b = 1
    while b < n:
        v = v + lax.ppermute(v, "src", [(i, i ^ b) for i in range(n)])
        b *= 2
    return v


def _zline(block, na):
    me = lax.axis_index("src")
    ia = me // 2

    def along(p, d):
        return [(p * 2 + o, d * 2 + o) for o in range(2)]

    got = {}
    for sign in (1, -1):
        cur = block
        for s in range(1, na):
            pairs = []
            for p in range(na):
                if 0 <= p + sign < na and 0 <= p - sign * (s - 1) < na:
                    pairs.extend(along(p, p + sign))
            cur = lax.ppermute(cur, "src", pairs)
            got[(sign, s)] = cur
    col = [block] + [
        jnp.where(ia + k < na, got[(-1, k)], got[(1, na - k)]) for k in range(1, na)
    ]
    return jnp.concatenate(col, axis=0)


def _fast(na, forward_voxel_field, adjoint_voxel_field, voxel_input_vector, measurement_weight):
    vox = lax.axis_size("vox")
    me = lax.axis_index("vox")
    m = vox // 2
    par = me % 2
    q = me // 2
    si = lax.axis_index("src")
    ia = si // 2
    first = si % 2 == 0
    sl, vl = forward_voxel_field.shape
    ds = adjoint_voxel_field.shape[0]
    chunks = CHUNKS if ds % (CHUNKS * 8) == 0 else 1
    r = ds // chunks
    swap = [(i, i ^ 1) for i in range(2 * na)]
    pair = [(j, j ^ 1) for j in range(vox)]

    def chip_perm(k):
        return [(g * 2 + p, ((g + k) % m) * 2 + p) for g in range(m) for p in range(2)]

    def rows(col, blk):
        return lax.dynamic_slice_in_dim(col, ((blk - ia) % na) * r, r, axis=0)

    fwd = jnp.concatenate(
        [forward_voxel_field, lax.ppermute(forward_voxel_field, "src", swap)], axis=0
    )
    scaled = lax.optimization_barrier(
        (fwd.astype(jnp.float32) * voxel_input_vector[None, :]).astype(jnp.bfloat16)
    )
    weight = measurement_weight.reshape(sl, 2, ds)
    w_mine = jnp.where(first, weight[:, 0], weight[:, 1])
    w_other = jnp.where(first, weight[:, 1], weight[:, 0])
    weight = jnp.concatenate([w_mine, lax.ppermute(w_other, "src", swap)], axis=0)
    back = jnp.zeros((2 * sl, vl), jnp.float32)
    nxt = _zline(adjoint_voxel_field[:r], na)
    for c in range(chunks):
        col = nxt

        def pblock(blk):
            return lax.dot_general(
                scaled, rows(col, blk), (((1,), (1,)), ((), ())),
                preferred_element_type=jnp.float32,
            )

        keeps = [pblock(2 * ((q + k) % m) + par) for k in range(m)]
        sends = [pblock(2 * ((q + k) % m) + 1 - par) for k in range(m)]
        halves = [a + b for a, b in zip(keeps, lax.ppermute(tuple(sends), "vox", pair))]
        share = halves[0]
        for k in range(1, m):
            share = share + lax.ppermute(
                halves[k].astype(jnp.bfloat16), "vox", chip_perm(k)
            ).astype(jnp.float32)

        piece = (weight[:, c * r:(c + 1) * r] * share).astype(jnp.bfloat16)

        got = [(me, piece)]
        for k in range(1, m):
            got.append((2 * ((q - k) % m) + par, lax.ppermute(piece, "vox", chip_perm(k))))
        mates = lax.ppermute(tuple(w for _, w in got), "vox", pair)
        got = got + [(blk ^ 1, w) for (blk, _), w in zip(got, mates)]
        if c + 1 < chunks:
            nxt, ws = lax.optimization_barrier(
                (_zline(adjoint_voxel_field[(c + 1) * r:(c + 2) * r], na), [w for _, w in got])
            )
            got = [(blk, w) for (blk, _), w in zip(got, ws)]
        back = back + jnp.dot(
            jnp.concatenate([w for _, w in got], axis=1),
            jnp.concatenate([rows(col, blk) for blk, _ in got], axis=0),
            preferred_element_type=jnp.float32,
        )

    local_sum = jnp.sum(fwd.astype(jnp.float32) * back, axis=0)
    return _sum_over_src(local_sum)


def per_device(grid, forward_voxel_field, adjoint_voxel_field, voxel_input_vector, measurement_weight):
    nsrc = lax.axis_size("src")
    vox = lax.axis_size("vox")
    me = lax.axis_index("vox")
    m = vox // 2
    par = me % 2
    q = me // 2
    t = nsrc // vox
    sl, vl = forward_voxel_field.shape
    ds = adjoint_voxel_field.shape[0]
    chunks = CHUNKS if ds % CHUNKS == 0 else 1
    r = ds // chunks
    n = t * r
    pair = [(j, j ^ 1) for j in range(vox)]

    def chip_perm(k):
        return [(g * 2 + p, ((g + k) % m) * 2 + p) for g in range(m) for p in range(2)]

    scaled = (forward_voxel_field.astype(jnp.float32) * voxel_input_vector[None, :]).astype(
        jnp.bfloat16
    )
    weight = measurement_weight.reshape(sl, t, ds)
    if grid is not None and grid[0] == t:
        na = grid[1]
        ia = lax.axis_index("src") // t

        def rel(blk):
            return (blk - ia) % na
    else:
        grid = None

        def rel(blk):
            return blk
    def gather(c):
        return _gather_src(adjoint_voxel_field[c * r:(c + 1) * r], grid)

    back = jnp.zeros((sl, vl), jnp.float32)
    nxt = gather(0)
    for c in range(chunks):
        adj = nxt

        def pblock(blk):
            return lax.dot_general(
                scaled, _rows(adj, rel(blk), n), (((1,), (1,)), ((), ())),
                preferred_element_type=jnp.float32,
            )

        keeps = [pblock(2 * ((q + k) % m) + par) for k in range(m)]
        sends = [pblock(2 * ((q + k) % m) + 1 - par) for k in range(m)]
        halves = [a + b for a, b in zip(keeps, lax.ppermute(tuple(sends), "vox", pair))]
        share = halves[0]
        for k in range(1, m):
            share = share + lax.ppermute(
                halves[k].astype(jnp.bfloat16), "vox", chip_perm(k)
            ).astype(jnp.float32)

        w_c = weight[:, :, c * r:(c + 1) * r].reshape(sl, n)
        wt = (w_c * share).astype(jnp.bfloat16)

        got = [(me, wt)]
        for k in range(1, m):
            got.append((2 * ((q - k) % m) + par, lax.ppermute(wt, "vox", chip_perm(k))))
        mine = lax.ppermute(tuple(w for _, w in got), "vox", pair)
        got = got + [(blk ^ 1, w) for (blk, _), w in zip(got, mine)]
        if c + 1 < chunks:
            nxt, ws = lax.optimization_barrier((gather(c + 1), [w for _, w in got]))
            got = [(blk, w) for (blk, _), w in zip(got, ws)]
        for blk, w in got:
            back = back + jnp.dot(w, _rows(adj, rel(blk), n), preferred_element_type=jnp.float32)

    local_sum = jnp.sum(forward_voxel_field.astype(jnp.float32) * back, axis=0)
    return _sum_over_src(local_sum)


def solution(mesh):
    placed = (P("src", "vox"), P("src", "vox"), P("vox"), P("src", "vox"))
    grid = _src_grid(mesh)
    nsrc, vox = mesh.shape["src"], mesh.shape["vox"]
    if grid is not None and grid[0] == 2 and nsrc == 2 * vox and vox % 2 == 0 and grid[1] == vox:
        body = functools.partial(_fast, grid[1])
    else:
        body = functools.partial(per_device, None)
    return jax.shard_map(
        body, mesh=mesh, in_specs=placed, out_specs=P("vox"), check_vma=False
    )
```

```python
import functools

import jax
import jax.numpy as jnp
from jax import lax
from jax.sharding import PartitionSpec as P

CHUNKS = 2


def _rows(a, blk, n):
    return lax.dynamic_slice_in_dim(a, blk * n, n, axis=0)


def _src_grid(mesh):
    devs = mesh.devices
    ax = mesh.axis_names.index("src")
    row = [devs[(i,) + (0,) * (devs.ndim - 1)] if ax == 0 else None for i in range(devs.shape[0])]
    if ax != 0 or any(not hasattr(d, "coords") for d in row):
        return None
    co = [tuple(d.coords) for d in row]
    n = len(co)
    diff = [k for k in range(len(co[0])) if n > 1 and co[1][k] != co[0][k]]
    if len(diff) != 1:
        return None
    nb = 1
    while nb < n and co[nb][diff[0]] != co[0][diff[0]]:
        nb += 1
    if n % nb:
        return None
    na = n // nb

    def near(i, j):
        return sum(abs(a - b) for a, b in zip(co[i], co[j])) == 1

    for i in range(n):
        ia, ib = divmod(i, nb)
        if ib + 1 < nb and not near(i, i + 1):
            return None
        if ia + 1 < na and not near(i, i + nb):
            return None
    if nb != 2 or na < 2:
        return None
    return nb, na


def _gather_src(block, grid):
    if grid is None:
        return lax.all_gather(block, "src", axis=0, tiled=True)
    nb, na = grid
    me = lax.axis_index("src")
    ia, ib = me // nb, me % nb
    swap = [(i, i ^ 1) for i in range(na * nb)]

    def along(p, d):
        return [(p * nb + o, d * nb + o) for o in range(nb)]

    got = {}
    for sign in (1, -1):
        cur = block
        for s in range(1, na):
            pairs = []
            for p in range(na):
                if 0 <= p + sign < na and 0 <= p - sign * (s - 1) < na:
                    pairs.extend(along(p, p + sign))
            cur = lax.ppermute(cur, "src", pairs)
            got[(sign, s)] = cur
    col = [block] + [
        jnp.where(ia + k < na, got[(-1, k)], got[(1, na - k)]) for k in range(1, na)
    ]
    col = jnp.stack(col)
    other = lax.ppermute(col, "src", swap)
    first = ib == 0
    planes = jnp.stack([jnp.where(first, col, other), jnp.where(first, other, col)], axis=1)
    return planes.reshape((-1,) + block.shape[1:])


def _sum_over_src(v):
    n = lax.axis_size("src")
    if n & (n - 1):
        return lax.psum(v, "src")
    b = 1
    while b < n:
        v = v + lax.ppermute(v, "src", [(i, i ^ b) for i in range(n)])
        b *= 2
    return v


def _zline(block, na):
    me = lax.axis_index("src")
    ia = me // 2

    def along(p, d):
        return [(p * 2 + o, d * 2 + o) for o in range(2)]

    got = {}
    for sign in (1, -1):
        cur = block
        for s in range(1, na):
            pairs = []
            for p in range(na):
                if 0 <= p + sign < na and 0 <= p - sign * (s - 1) < na:
                    pairs.extend(along(p, p + sign))
            cur = lax.ppermute(cur, "src", pairs)
            got[(sign, s)] = cur
    col = [block] + [
        jnp.where(ia + k < na, got[(-1, k)], got[(1, na - k)]) for k in range(1, na)
    ]
    return jnp.concatenate(col, axis=0)


def _fast(na, forward_voxel_field, adjoint_voxel_field, voxel_input_vector, measurement_weight):
    vox = lax.axis_size("vox")
    me = lax.axis_index("vox")
    m = vox // 2
    par = me % 2
    q = me // 2
    si = lax.axis_index("src")
    ia = si // 2
    first = si % 2 == 0
    sl, vl = forward_voxel_field.shape
    ds = adjoint_voxel_field.shape[0]
    chunks = CHUNKS if ds % (CHUNKS * 8) == 0 else 1
    r = ds // chunks
    swap = [(i, i ^ 1) for i in range(2 * na)]
    pair = [(j, j ^ 1) for j in range(vox)]

    def chip_perm(k):
        return [(g * 2 + p, ((g + k) % m) * 2 + p) for g in range(m) for p in range(2)]

    def rows(col, blk):
        return lax.dynamic_slice(col, (((blk - ia) % na) * ds + c * r, 0), (r, vl))

    fwd = jnp.concatenate(
        [forward_voxel_field, lax.ppermute(forward_voxel_field, "src", swap)], axis=0
    )
    scaled = lax.optimization_barrier(
        (fwd.astype(jnp.float32) * voxel_input_vector[None, :]).astype(jnp.bfloat16)
    )
    weight = measurement_weight.reshape(sl, 2, ds)
    w_mine = jnp.where(first, weight[:, 0], weight[:, 1])
    w_other = jnp.where(first, weight[:, 1], weight[:, 0])
    weight = jnp.concatenate([w_mine, lax.ppermute(w_other, "src", swap)], axis=0)
    back = jnp.zeros((2 * sl, vl), jnp.float32)
    col = _zline(adjoint_voxel_field, na)
    for c in range(chunks):

        def pblock(blk):
            return lax.dot_general(
                scaled, rows(col, blk), (((1,), (1,)), ((), ())),
                preferred_element_type=jnp.float32,
            )

        keeps = [pblock(2 * ((q + k) % m) + par) for k in range(m)]
        sends = [pblock(2 * ((q + k) % m) + 1 - par) for k in range(m)]
        halves = [a + b for a, b in zip(keeps, lax.ppermute(tuple(sends), "vox", pair))]
        share = halves[0]
        for k in range(1, m):
            share = share + lax.ppermute(
                halves[k].astype(jnp.bfloat16), "vox", chip_perm(k)
            ).astype(jnp.float32)

        piece = (weight[:, c * r:(c + 1) * r] * share).astype(jnp.bfloat16)

        got = [(me, piece)]
        for k in range(1, m):
            got.append((2 * ((q - k) % m) + par, lax.ppermute(piece, "vox", chip_perm(k))))
        mates = lax.ppermute(tuple(w for _, w in got), "vox", pair)
        got = got + [(blk ^ 1, w) for (blk, _), w in zip(got, mates)]
        back = back + jnp.dot(
            jnp.concatenate([w for _, w in got], axis=1),
            jnp.concatenate([rows(col, blk) for blk, _ in got], axis=0),
            preferred_element_type=jnp.float32,
        )

    local_sum = jnp.sum(fwd.astype(jnp.float32) * back, axis=0)
    return _sum_over_src(local_sum)


def per_device(grid, forward_voxel_field, adjoint_voxel_field, voxel_input_vector, measurement_weight):
    nsrc = lax.axis_size("src")
    vox = lax.axis_size("vox")
    me = lax.axis_index("vox")
    m = vox // 2
    par = me % 2
    q = me // 2
    t = nsrc // vox
    sl, vl = forward_voxel_field.shape
    ds = adjoint_voxel_field.shape[0]
    chunks = CHUNKS if ds % CHUNKS == 0 else 1
    r = ds // chunks
    n = t * r
    pair = [(j, j ^ 1) for j in range(vox)]

    def chip_perm(k):
        return [(g * 2 + p, ((g + k) % m) * 2 + p) for g in range(m) for p in range(2)]

    scaled = (forward_voxel_field.astype(jnp.float32) * voxel_input_vector[None, :]).astype(
        jnp.bfloat16
    )
    weight = measurement_weight.reshape(sl, t, ds)
    if grid is not None and grid[0] == t:
        na = grid[1]
        ia = lax.axis_index("src") // t

        def rel(blk):
            return (blk - ia) % na
    else:
        grid = None

        def rel(blk):
            return blk
    def gather(c):
        return _gather_src(adjoint_voxel_field[c * r:(c + 1) * r], grid)

    back = jnp.zeros((sl, vl), jnp.float32)
    nxt = gather(0)
    for c in range(chunks):
        adj = nxt

        def pblock(blk):
            return lax.dot_general(
                scaled, _rows(adj, rel(blk), n), (((1,), (1,)), ((), ())),
                preferred_element_type=jnp.float32,
            )

        keeps = [pblock(2 * ((q + k) % m) + par) for k in range(m)]
        sends = [pblock(2 * ((q + k) % m) + 1 - par) for k in range(m)]
        halves = [a + b for a, b in zip(keeps, lax.ppermute(tuple(sends), "vox", pair))]
        share = halves[0]
        for k in range(1, m):
            share = share + lax.ppermute(
                halves[k].astype(jnp.bfloat16), "vox", chip_perm(k)
            ).astype(jnp.float32)

        w_c = weight[:, :, c * r:(c + 1) * r].reshape(sl, n)
        wt = (w_c * share).astype(jnp.bfloat16)

        got = [(me, wt)]
        for k in range(1, m):
            got.append((2 * ((q - k) % m) + par, lax.ppermute(wt, "vox", chip_perm(k))))
        mine = lax.ppermute(tuple(w for _, w in got), "vox", pair)
        got = got + [(blk ^ 1, w) for (blk, _), w in zip(got, mine)]
        if c + 1 < chunks:
            nxt, ws = lax.optimization_barrier((gather(c + 1), [w for _, w in got]))
            got = [(blk, w) for (blk, _), w in zip(got, ws)]
        for blk, w in got:
            back = back + jnp.dot(w, _rows(adj, rel(blk), n), preferred_element_type=jnp.float32)

    local_sum = jnp.sum(forward_voxel_field.astype(jnp.float32) * back, axis=0)
    return _sum_over_src(local_sum)


def solution(mesh):
    placed = (P("src", "vox"), P("src", "vox"), P("vox"), P("src", "vox"))
    grid = _src_grid(mesh)
    nsrc, vox = mesh.shape["src"], mesh.shape["vox"]
    if grid is not None and grid[0] == 2 and nsrc == 2 * vox and vox % 2 == 0 and grid[1] == vox:
        body = functools.partial(_fast, grid[1])
    else:
        body = functools.partial(per_device, None)
    return jax.shard_map(
        body, mesh=mesh, in_specs=placed, out_specs=P("vox"), check_vma=False
    )
```

```python
import functools

import jax
import jax.numpy as jnp
from jax import lax
from jax.sharding import PartitionSpec as P

CHUNKS = 4


def _rows(a, blk, n):
    return lax.dynamic_slice_in_dim(a, blk * n, n, axis=0)


def _src_grid(mesh):
    devs = mesh.devices
    ax = mesh.axis_names.index("src")
    row = [devs[(i,) + (0,) * (devs.ndim - 1)] if ax == 0 else None for i in range(devs.shape[0])]
    if ax != 0 or any(not hasattr(d, "coords") for d in row):
        return None
    co = [tuple(d.coords) for d in row]
    n = len(co)
    diff = [k for k in range(len(co[0])) if n > 1 and co[1][k] != co[0][k]]
    if len(diff) != 1:
        return None
    nb = 1
    while nb < n and co[nb][diff[0]] != co[0][diff[0]]:
        nb += 1
    if n % nb:
        return None
    na = n // nb

    def near(i, j):
        return sum(abs(a - b) for a, b in zip(co[i], co[j])) == 1

    for i in range(n):
        ia, ib = divmod(i, nb)
        if ib + 1 < nb and not near(i, i + 1):
            return None
        if ia + 1 < na and not near(i, i + nb):
            return None
    if nb != 2 or na < 2:
        return None
    return nb, na


def _gather_src(block, grid):
    if grid is None:
        return lax.all_gather(block, "src", axis=0, tiled=True)
    nb, na = grid
    me = lax.axis_index("src")
    ia, ib = me // nb, me % nb
    swap = [(i, i ^ 1) for i in range(na * nb)]

    def along(p, d):
        return [(p * nb + o, d * nb + o) for o in range(nb)]

    got = {}
    for sign in (1, -1):
        cur = block
        for s in range(1, na):
            pairs = []
            for p in range(na):
                if 0 <= p + sign < na and 0 <= p - sign * (s - 1) < na:
                    pairs.extend(along(p, p + sign))
            cur = lax.ppermute(cur, "src", pairs)
            got[(sign, s)] = cur
    col = [block] + [
        jnp.where(ia + k < na, got[(-1, k)], got[(1, na - k)]) for k in range(1, na)
    ]
    col = jnp.stack(col)
    other = lax.ppermute(col, "src", swap)
    first = ib == 0
    planes = jnp.stack([jnp.where(first, col, other), jnp.where(first, other, col)], axis=1)
    return planes.reshape((-1,) + block.shape[1:])


def _sum_over_src(v):
    n = lax.axis_size("src")
    if n & (n - 1):
        return lax.psum(v, "src")
    b = 1
    while b < n:
        v = v + lax.ppermute(v, "src", [(i, i ^ b) for i in range(n)])
        b *= 2
    return v


def _zline(block, na):
    me = lax.axis_index("src")
    ia = me // 2

    def along(p, d):
        return [(p * 2 + o, d * 2 + o) for o in range(2)]

    got = {}
    for sign in (1, -1):
        cur = block
        for s in range(1, na):
            pairs = []
            for p in range(na):
                if 0 <= p + sign < na and 0 <= p - sign * (s - 1) < na:
                    pairs.extend(along(p, p + sign))
            cur = lax.ppermute(cur, "src", pairs)
            got[(sign, s)] = cur
    col = [block] + [
        jnp.where(ia + k < na, got[(-1, k)], got[(1, na - k)]) for k in range(1, na)
    ]
    return jnp.concatenate(col, axis=0)


def _fast(na, forward_voxel_field, adjoint_voxel_field, voxel_input_vector, measurement_weight):
    vox = lax.axis_size("vox")
    me = lax.axis_index("vox")
    m = vox // 2
    par = me % 2
    q = me // 2
    si = lax.axis_index("src")
    ia = si // 2
    first = si % 2 == 0
    sl, vl = forward_voxel_field.shape
    ds = adjoint_voxel_field.shape[0]
    chunks = CHUNKS if ds % (CHUNKS * 8) == 0 else 1
    r = ds // chunks
    swap = [(i, i ^ 1) for i in range(2 * na)]
    pair = [(j, j ^ 1) for j in range(vox)]

    def chip_perm(k):
        return [(g * 2 + p, ((g + k) % m) * 2 + p) for g in range(m) for p in range(2)]

    def rows(col, blk):
        return lax.dynamic_slice(col, (((blk - ia) % na) * ds + c * r, 0), (r, vl))

    fwd = jnp.concatenate(
        [forward_voxel_field, lax.ppermute(forward_voxel_field, "src", swap)], axis=0
    )
    scaled = lax.optimization_barrier(
        (fwd.astype(jnp.float32) * voxel_input_vector[None, :]).astype(jnp.bfloat16)
    )
    weight = measurement_weight.reshape(sl, 2, ds)
    w_mine = jnp.where(first, weight[:, 0], weight[:, 1])
    w_other = jnp.where(first, weight[:, 1], weight[:, 0])
    weight = jnp.concatenate([w_mine, lax.ppermute(w_other, "src", swap)], axis=0)
    back = jnp.zeros((2 * sl, vl), jnp.float32)
    col = _zline(adjoint_voxel_field, na)
    for c in range(chunks):

        def pblock(blk):
            return lax.dot_general(
                scaled, rows(col, blk), (((1,), (1,)), ((), ())),
                preferred_element_type=jnp.float32,
            )

        keeps = [pblock(2 * ((q + k) % m) + par) for k in range(m)]
        sends = [pblock(2 * ((q + k) % m) + 1 - par) for k in range(m)]
        halves = [a + b for a, b in zip(keeps, lax.ppermute(tuple(sends), "vox", pair))]
        share = halves[0]
        for k in range(1, m):
            share = share + lax.ppermute(
                halves[k].astype(jnp.bfloat16), "vox", chip_perm(k)
            ).astype(jnp.float32)

        piece = (weight[:, c * r:(c + 1) * r] * share).astype(jnp.bfloat16)

        got = [(me, piece)]
        for k in range(1, m):
            got.append((2 * ((q - k) % m) + par, lax.ppermute(piece, "vox", chip_perm(k))))
        mates = lax.ppermute(tuple(w for _, w in got), "vox", pair)
        got = got + [(blk ^ 1, w) for (blk, _), w in zip(got, mates)]
        back = back + jnp.dot(
            jnp.concatenate([w for _, w in got], axis=1),
            jnp.concatenate([rows(col, blk) for blk, _ in got], axis=0),
            preferred_element_type=jnp.float32,
        )

    local_sum = jnp.sum(fwd.astype(jnp.float32) * back, axis=0)
    return _sum_over_src(local_sum)


def per_device(grid, forward_voxel_field, adjoint_voxel_field, voxel_input_vector, measurement_weight):
    nsrc = lax.axis_size("src")
    vox = lax.axis_size("vox")
    me = lax.axis_index("vox")
    m = vox // 2
    par = me % 2
    q = me // 2
    t = nsrc // vox
    sl, vl = forward_voxel_field.shape
    ds = adjoint_voxel_field.shape[0]
    chunks = CHUNKS if ds % CHUNKS == 0 else 1
    r = ds // chunks
    n = t * r
    pair = [(j, j ^ 1) for j in range(vox)]

    def chip_perm(k):
        return [(g * 2 + p, ((g + k) % m) * 2 + p) for g in range(m) for p in range(2)]

    scaled = (forward_voxel_field.astype(jnp.float32) * voxel_input_vector[None, :]).astype(
        jnp.bfloat16
    )
    weight = measurement_weight.reshape(sl, t, ds)
    if grid is not None and grid[0] == t:
        na = grid[1]
        ia = lax.axis_index("src") // t

        def rel(blk):
            return (blk - ia) % na
    else:
        grid = None

        def rel(blk):
            return blk
    def gather(c):
        return _gather_src(adjoint_voxel_field[c * r:(c + 1) * r], grid)

    back = jnp.zeros((sl, vl), jnp.float32)
    nxt = gather(0)
    for c in range(chunks):
        adj = nxt

        def pblock(blk):
            return lax.dot_general(
                scaled, _rows(adj, rel(blk), n), (((1,), (1,)), ((), ())),
                preferred_element_type=jnp.float32,
            )

        keeps = [pblock(2 * ((q + k) % m) + par) for k in range(m)]
        sends = [pblock(2 * ((q + k) % m) + 1 - par) for k in range(m)]
        halves = [a + b for a, b in zip(keeps, lax.ppermute(tuple(sends), "vox", pair))]
        share = halves[0]
        for k in range(1, m):
            share = share + lax.ppermute(
                halves[k].astype(jnp.bfloat16), "vox", chip_perm(k)
            ).astype(jnp.float32)

        w_c = weight[:, :, c * r:(c + 1) * r].reshape(sl, n)
        wt = (w_c * share).astype(jnp.bfloat16)

        got = [(me, wt)]
        for k in range(1, m):
            got.append((2 * ((q - k) % m) + par, lax.ppermute(wt, "vox", chip_perm(k))))
        mine = lax.ppermute(tuple(w for _, w in got), "vox", pair)
        got = got + [(blk ^ 1, w) for (blk, _), w in zip(got, mine)]
        if c + 1 < chunks:
            nxt, ws = lax.optimization_barrier((gather(c + 1), [w for _, w in got]))
            got = [(blk, w) for (blk, _), w in zip(got, ws)]
        for blk, w in got:
            back = back + jnp.dot(w, _rows(adj, rel(blk), n), preferred_element_type=jnp.float32)

    local_sum = jnp.sum(forward_voxel_field.astype(jnp.float32) * back, axis=0)
    return _sum_over_src(local_sum)


def solution(mesh):
    placed = (P("src", "vox"), P("src", "vox"), P("vox"), P("src", "vox"))
    grid = _src_grid(mesh)
    nsrc, vox = mesh.shape["src"], mesh.shape["vox"]
    if grid is not None and grid[0] == 2 and nsrc == 2 * vox and vox % 2 == 0 and grid[1] == vox:
        body = functools.partial(_fast, grid[1])
    else:
        body = functools.partial(per_device, None)
    return jax.shard_map(
        body, mesh=mesh, in_specs=placed, out_specs=P("vox"), check_vma=False
    )
```

```python
import functools

import jax
import jax.numpy as jnp
from jax import lax
from jax.sharding import PartitionSpec as P

CHUNKS = 4
FAST_CHUNKS = 8


def _rows(a, blk, n):
    return lax.dynamic_slice_in_dim(a, blk * n, n, axis=0)


def _src_grid(mesh):
    devs = mesh.devices
    ax = mesh.axis_names.index("src")
    row = [devs[(i,) + (0,) * (devs.ndim - 1)] if ax == 0 else None for i in range(devs.shape[0])]
    if ax != 0 or any(not hasattr(d, "coords") for d in row):
        return None
    co = [tuple(d.coords) for d in row]
    n = len(co)
    diff = [k for k in range(len(co[0])) if n > 1 and co[1][k] != co[0][k]]
    if len(diff) != 1:
        return None
    nb = 1
    while nb < n and co[nb][diff[0]] != co[0][diff[0]]:
        nb += 1
    if n % nb:
        return None
    na = n // nb

    def near(i, j):
        return sum(abs(a - b) for a, b in zip(co[i], co[j])) == 1

    for i in range(n):
        ia, ib = divmod(i, nb)
        if ib + 1 < nb and not near(i, i + 1):
            return None
        if ia + 1 < na and not near(i, i + nb):
            return None
    if nb != 2 or na < 2:
        return None
    return nb, na


def _gather_src(block, grid):
    if grid is None:
        return lax.all_gather(block, "src", axis=0, tiled=True)
    nb, na = grid
    me = lax.axis_index("src")
    ia, ib = me // nb, me % nb
    swap = [(i, i ^ 1) for i in range(na * nb)]

    def along(p, d):
        return [(p * nb + o, d * nb + o) for o in range(nb)]

    got = {}
    for sign in (1, -1):
        cur = block
        for s in range(1, na):
            pairs = []
            for p in range(na):
                if 0 <= p + sign < na and 0 <= p - sign * (s - 1) < na:
                    pairs.extend(along(p, p + sign))
            cur = lax.ppermute(cur, "src", pairs)
            got[(sign, s)] = cur
    col = [block] + [
        jnp.where(ia + k < na, got[(-1, k)], got[(1, na - k)]) for k in range(1, na)
    ]
    col = jnp.stack(col)
    other = lax.ppermute(col, "src", swap)
    first = ib == 0
    planes = jnp.stack([jnp.where(first, col, other), jnp.where(first, other, col)], axis=1)
    return planes.reshape((-1,) + block.shape[1:])


def _sum_over_src(v):
    n = lax.axis_size("src")
    if n & (n - 1):
        return lax.psum(v, "src")
    b = 1
    while b < n:
        v = v + lax.ppermute(v, "src", [(i, i ^ b) for i in range(n)])
        b *= 2
    return v


def _zline(block, na):
    me = lax.axis_index("src")
    ia = me // 2

    def along(p, d):
        return [(p * 2 + o, d * 2 + o) for o in range(2)]

    got = {}
    for sign in (1, -1):
        cur = block
        for s in range(1, na):
            pairs = []
            for p in range(na):
                if 0 <= p + sign < na and 0 <= p - sign * (s - 1) < na:
                    pairs.extend(along(p, p + sign))
            cur = lax.ppermute(cur, "src", pairs)
            got[(sign, s)] = cur
    col = [block] + [
        jnp.where(ia + k < na, got[(-1, k)], got[(1, na - k)]) for k in range(1, na)
    ]
    return jnp.concatenate(col, axis=0)


def _fast(na, forward_voxel_field, adjoint_voxel_field, voxel_input_vector, measurement_weight):
    vox = lax.axis_size("vox")
    me = lax.axis_index("vox")
    m = vox // 2
    par = me % 2
    q = me // 2
    si = lax.axis_index("src")
    ia = si // 2
    first = si % 2 == 0
    sl, vl = forward_voxel_field.shape
    ds = adjoint_voxel_field.shape[0]
    chunks = FAST_CHUNKS if ds % (FAST_CHUNKS * 8) == 0 else 1
    r = ds // chunks
    swap = [(i, i ^ 1) for i in range(2 * na)]
    pair = [(j, j ^ 1) for j in range(vox)]

    def chip_perm(k):
        return [(g * 2 + p, ((g + k) % m) * 2 + p) for g in range(m) for p in range(2)]

    def rows(col, blk):
        return lax.dynamic_slice(col, (((blk - ia) % na) * ds + c * r, 0), (r, vl))

    fwd = jnp.concatenate(
        [forward_voxel_field, lax.ppermute(forward_voxel_field, "src", swap)], axis=0
    )
    scaled = lax.optimization_barrier(
        (fwd.astype(jnp.float32) * voxel_input_vector[None, :]).astype(jnp.bfloat16)
    )
    weight = measurement_weight.reshape(sl, 2, ds)
    w_mine = jnp.where(first, weight[:, 0], weight[:, 1])
    w_other = jnp.where(first, weight[:, 1], weight[:, 0])
    weight = jnp.concatenate([w_mine, lax.ppermute(w_other, "src", swap)], axis=0)
    back = jnp.zeros((2 * sl, vl), jnp.float32)
    col = _zline(adjoint_voxel_field, na)
    for c in range(chunks):

        def pblock(blk):
            return lax.dot_general(
                scaled, rows(col, blk), (((1,), (1,)), ((), ())),
                preferred_element_type=jnp.float32,
            )

        keeps = [pblock(2 * ((q + k) % m) + par) for k in range(m)]
        sends = [pblock(2 * ((q + k) % m) + 1 - par) for k in range(m)]
        halves = [a + b for a, b in zip(keeps, lax.ppermute(tuple(sends), "vox", pair))]
        share = halves[0]
        for k in range(1, m):
            share = share + lax.ppermute(
                halves[k].astype(jnp.bfloat16), "vox", chip_perm(k)
            ).astype(jnp.float32)

        piece = (weight[:, c * r:(c + 1) * r] * share).astype(jnp.bfloat16)

        got = [(me, piece)]
        for k in range(1, m):
            got.append((2 * ((q - k) % m) + par, lax.ppermute(piece, "vox", chip_perm(k))))
        mates = lax.ppermute(tuple(w for _, w in got), "vox", pair)
        got = got + [(blk ^ 1, w) for (blk, _), w in zip(got, mates)]
        back = back + jnp.dot(
            jnp.concatenate([w for _, w in got], axis=1),
            jnp.concatenate([rows(col, blk) for blk, _ in got], axis=0),
            preferred_element_type=jnp.float32,
        )

    local_sum = jnp.sum(fwd.astype(jnp.float32) * back, axis=0)
    return _sum_over_src(local_sum)


def per_device(grid, forward_voxel_field, adjoint_voxel_field, voxel_input_vector, measurement_weight):
    nsrc = lax.axis_size("src")
    vox = lax.axis_size("vox")
    me = lax.axis_index("vox")
    m = vox // 2
    par = me % 2
    q = me // 2
    t = nsrc // vox
    sl, vl = forward_voxel_field.shape
    ds = adjoint_voxel_field.shape[0]
    chunks = CHUNKS if ds % CHUNKS == 0 else 1
    r = ds // chunks
    n = t * r
    pair = [(j, j ^ 1) for j in range(vox)]

    def chip_perm(k):
        return [(g * 2 + p, ((g + k) % m) * 2 + p) for g in range(m) for p in range(2)]

    scaled = (forward_voxel_field.astype(jnp.float32) * voxel_input_vector[None, :]).astype(
        jnp.bfloat16
    )
    weight = measurement_weight.reshape(sl, t, ds)
    if grid is not None and grid[0] == t:
        na = grid[1]
        ia = lax.axis_index("src") // t

        def rel(blk):
            return (blk - ia) % na
    else:
        grid = None

        def rel(blk):
            return blk
    def gather(c):
        return _gather_src(adjoint_voxel_field[c * r:(c + 1) * r], grid)

    back = jnp.zeros((sl, vl), jnp.float32)
    nxt = gather(0)
    for c in range(chunks):
        adj = nxt

        def pblock(blk):
            return lax.dot_general(
                scaled, _rows(adj, rel(blk), n), (((1,), (1,)), ((), ())),
                preferred_element_type=jnp.float32,
            )

        keeps = [pblock(2 * ((q + k) % m) + par) for k in range(m)]
        sends = [pblock(2 * ((q + k) % m) + 1 - par) for k in range(m)]
        halves = [a + b for a, b in zip(keeps, lax.ppermute(tuple(sends), "vox", pair))]
        share = halves[0]
        for k in range(1, m):
            share = share + lax.ppermute(
                halves[k].astype(jnp.bfloat16), "vox", chip_perm(k)
            ).astype(jnp.float32)

        w_c = weight[:, :, c * r:(c + 1) * r].reshape(sl, n)
        wt = (w_c * share).astype(jnp.bfloat16)

        got = [(me, wt)]
        for k in range(1, m):
            got.append((2 * ((q - k) % m) + par, lax.ppermute(wt, "vox", chip_perm(k))))
        mine = lax.ppermute(tuple(w for _, w in got), "vox", pair)
        got = got + [(blk ^ 1, w) for (blk, _), w in zip(got, mine)]
        if c + 1 < chunks:
            nxt, ws = lax.optimization_barrier((gather(c + 1), [w for _, w in got]))
            got = [(blk, w) for (blk, _), w in zip(got, ws)]
        for blk, w in got:
            back = back + jnp.dot(w, _rows(adj, rel(blk), n), preferred_element_type=jnp.float32)

    local_sum = jnp.sum(forward_voxel_field.astype(jnp.float32) * back, axis=0)
    return _sum_over_src(local_sum)


def solution(mesh):
    placed = (P("src", "vox"), P("src", "vox"), P("vox"), P("src", "vox"))
    grid = _src_grid(mesh)
    nsrc, vox = mesh.shape["src"], mesh.shape["vox"]
    if grid is not None and grid[0] == 2 and nsrc == 2 * vox and vox % 2 == 0 and grid[1] == vox:
        body = functools.partial(_fast, grid[1])
    else:
        body = functools.partial(per_device, None)
    return jax.shard_map(
        body, mesh=mesh, in_specs=placed, out_specs=P("vox"), check_vma=False
    )
```

```python
import functools

import jax
import jax.numpy as jnp
from jax import lax
from jax.sharding import PartitionSpec as P

CHUNKS = 4
RELAYS = 2


def _rows(a, blk, n):
    return lax.dynamic_slice_in_dim(a, blk * n, n, axis=0)


def _src_grid(mesh):
    devs = mesh.devices
    ax = mesh.axis_names.index("src")
    row = [devs[(i,) + (0,) * (devs.ndim - 1)] if ax == 0 else None for i in range(devs.shape[0])]
    if ax != 0 or any(not hasattr(d, "coords") for d in row):
        return None
    co = [tuple(d.coords) for d in row]
    n = len(co)
    diff = [k for k in range(len(co[0])) if n > 1 and co[1][k] != co[0][k]]
    if len(diff) != 1:
        return None
    nb = 1
    while nb < n and co[nb][diff[0]] != co[0][diff[0]]:
        nb += 1
    if n % nb:
        return None
    na = n // nb

    def near(i, j):
        return sum(abs(a - b) for a, b in zip(co[i], co[j])) == 1

    for i in range(n):
        ia, ib = divmod(i, nb)
        if ib + 1 < nb and not near(i, i + 1):
            return None
        if ia + 1 < na and not near(i, i + nb):
            return None
    if nb != 2 or na < 2:
        return None
    return nb, na


def _gather_src(block, grid):
    if grid is None:
        return lax.all_gather(block, "src", axis=0, tiled=True)
    nb, na = grid
    me = lax.axis_index("src")
    ia, ib = me // nb, me % nb
    swap = [(i, i ^ 1) for i in range(na * nb)]

    def along(p, d):
        return [(p * nb + o, d * nb + o) for o in range(nb)]

    got = {}
    for sign in (1, -1):
        cur = block
        for s in range(1, na):
            pairs = []
            for p in range(na):
                if 0 <= p + sign < na and 0 <= p - sign * (s - 1) < na:
                    pairs.extend(along(p, p + sign))
            cur = lax.ppermute(cur, "src", pairs)
            got[(sign, s)] = cur
    col = [block] + [
        jnp.where(ia + k < na, got[(-1, k)], got[(1, na - k)]) for k in range(1, na)
    ]
    col = jnp.stack(col)
    other = lax.ppermute(col, "src", swap)
    first = ib == 0
    planes = jnp.stack([jnp.where(first, col, other), jnp.where(first, other, col)], axis=1)
    return planes.reshape((-1,) + block.shape[1:])


def _sum_over_src(v):
    n = lax.axis_size("src")
    if n & (n - 1):
        return lax.psum(v, "src")
    b = 1
    while b < n:
        v = v + lax.ppermute(v, "src", [(i, i ^ b) for i in range(n)])
        b *= 2
    return v


def _zline(block, na):
    me = lax.axis_index("src")
    ia = me // 2

    def along(p, d):
        return [(p * 2 + o, d * 2 + o) for o in range(2)]

    got = {}
    for sign in (1, -1):
        cur = block
        for s in range(1, na):
            pairs = []
            for p in range(na):
                if 0 <= p + sign < na and 0 <= p - sign * (s - 1) < na:
                    pairs.extend(along(p, p + sign))
            cur = lax.ppermute(cur, "src", pairs)
            got[(sign, s)] = cur
    col = [block] + [
        jnp.where(ia + k < na, got[(-1, k)], got[(1, na - k)]) for k in range(1, na)
    ]
    return jnp.concatenate(col, axis=0)


def _fast(na, forward_voxel_field, adjoint_voxel_field, voxel_input_vector, measurement_weight):
    vox = lax.axis_size("vox")
    me = lax.axis_index("vox")
    m = vox // 2
    par = me % 2
    q = me // 2
    si = lax.axis_index("src")
    ia = si // 2
    first = si % 2 == 0
    sl, vl = forward_voxel_field.shape
    ds = adjoint_voxel_field.shape[0]
    chunks = CHUNKS if ds % (CHUNKS * 8) == 0 else 1
    r = ds // chunks
    swap = [(i, i ^ 1) for i in range(2 * na)]
    pair = [(j, j ^ 1) for j in range(vox)]

    def chip_perm(k):
        return [(g * 2 + p, ((g + k) % m) * 2 + p) for g in range(m) for p in range(2)]

    relays = RELAYS if chunks % RELAYS == 0 else 1
    hr = ds // relays
    per = chunks // relays

    def rows(col, blk):
        return lax.dynamic_slice(col, (((blk - ia) % na) * hr + (c % per) * r, 0), (r, vl))

    fwd = jnp.concatenate(
        [forward_voxel_field, lax.ppermute(forward_voxel_field, "src", swap)], axis=0
    )
    scaled = lax.optimization_barrier(
        (fwd.astype(jnp.float32) * voxel_input_vector[None, :]).astype(jnp.bfloat16)
    )
    weight = measurement_weight.reshape(sl, 2, ds)
    w_mine = jnp.where(first, weight[:, 0], weight[:, 1])
    w_other = jnp.where(first, weight[:, 1], weight[:, 0])
    weight = jnp.concatenate([w_mine, lax.ppermute(w_other, "src", swap)], axis=0)
    back = jnp.zeros((2 * sl, vl), jnp.float32)
    cols = [_zline(adjoint_voxel_field[h * hr:(h + 1) * hr], na) for h in range(relays)]
    for c in range(chunks):
        col = cols[c // per]

        def pblock(blk):
            return lax.dot_general(
                scaled, rows(col, blk), (((1,), (1,)), ((), ())),
                preferred_element_type=jnp.float32,
            )

        keeps = [pblock(2 * ((q + k) % m) + par) for k in range(m)]
        sends = [pblock(2 * ((q + k) % m) + 1 - par) for k in range(m)]
        halves = [a + b for a, b in zip(keeps, lax.ppermute(tuple(sends), "vox", pair))]
        share = halves[0]
        for k in range(1, m):
            share = share + lax.ppermute(
                halves[k].astype(jnp.bfloat16), "vox", chip_perm(k)
            ).astype(jnp.float32)

        piece = (weight[:, c * r:(c + 1) * r] * share).astype(jnp.bfloat16)

        got = [(me, piece)]
        for k in range(1, m):
            got.append((2 * ((q - k) % m) + par, lax.ppermute(piece, "vox", chip_perm(k))))
        mates = lax.ppermute(tuple(w for _, w in got), "vox", pair)
        got = got + [(blk ^ 1, w) for (blk, _), w in zip(got, mates)]
        back = back + jnp.dot(
            jnp.concatenate([w for _, w in got], axis=1),
            jnp.concatenate([rows(col, blk) for blk, _ in got], axis=0),
            preferred_element_type=jnp.float32,
        )

    local_sum = jnp.sum(fwd.astype(jnp.float32) * back, axis=0)
    return _sum_over_src(local_sum)


def per_device(grid, forward_voxel_field, adjoint_voxel_field, voxel_input_vector, measurement_weight):
    nsrc = lax.axis_size("src")
    vox = lax.axis_size("vox")
    me = lax.axis_index("vox")
    m = vox // 2
    par = me % 2
    q = me // 2
    t = nsrc // vox
    sl, vl = forward_voxel_field.shape
    ds = adjoint_voxel_field.shape[0]
    chunks = CHUNKS if ds % CHUNKS == 0 else 1
    r = ds // chunks
    n = t * r
    pair = [(j, j ^ 1) for j in range(vox)]

    def chip_perm(k):
        return [(g * 2 + p, ((g + k) % m) * 2 + p) for g in range(m) for p in range(2)]

    scaled = (forward_voxel_field.astype(jnp.float32) * voxel_input_vector[None, :]).astype(
        jnp.bfloat16
    )
    weight = measurement_weight.reshape(sl, t, ds)
    if grid is not None and grid[0] == t:
        na = grid[1]
        ia = lax.axis_index("src") // t

        def rel(blk):
            return (blk - ia) % na
    else:
        grid = None

        def rel(blk):
            return blk
    def gather(c):
        return _gather_src(adjoint_voxel_field[c * r:(c + 1) * r], grid)

    back = jnp.zeros((sl, vl), jnp.float32)
    nxt = gather(0)
    for c in range(chunks):
        adj = nxt

        def pblock(blk):
            return lax.dot_general(
                scaled, _rows(adj, rel(blk), n), (((1,), (1,)), ((), ())),
                preferred_element_type=jnp.float32,
            )

        keeps = [pblock(2 * ((q + k) % m) + par) for k in range(m)]
        sends = [pblock(2 * ((q + k) % m) + 1 - par) for k in range(m)]
        halves = [a + b for a, b in zip(keeps, lax.ppermute(tuple(sends), "vox", pair))]
        share = halves[0]
        for k in range(1, m):
            share = share + lax.ppermute(
                halves[k].astype(jnp.bfloat16), "vox", chip_perm(k)
            ).astype(jnp.float32)

        w_c = weight[:, :, c * r:(c + 1) * r].reshape(sl, n)
        wt = (w_c * share).astype(jnp.bfloat16)

        got = [(me, wt)]
        for k in range(1, m):
            got.append((2 * ((q - k) % m) + par, lax.ppermute(wt, "vox", chip_perm(k))))
        mine = lax.ppermute(tuple(w for _, w in got), "vox", pair)
        got = got + [(blk ^ 1, w) for (blk, _), w in zip(got, mine)]
        if c + 1 < chunks:
            nxt, ws = lax.optimization_barrier((gather(c + 1), [w for _, w in got]))
            got = [(blk, w) for (blk, _), w in zip(got, ws)]
        for blk, w in got:
            back = back + jnp.dot(w, _rows(adj, rel(blk), n), preferred_element_type=jnp.float32)

    local_sum = jnp.sum(forward_voxel_field.astype(jnp.float32) * back, axis=0)
    return _sum_over_src(local_sum)


def solution(mesh):
    placed = (P("src", "vox"), P("src", "vox"), P("vox"), P("src", "vox"))
    grid = _src_grid(mesh)
    nsrc, vox = mesh.shape["src"], mesh.shape["vox"]
    if grid is not None and grid[0] == 2 and nsrc == 2 * vox and vox % 2 == 0 and grid[1] == vox:
        body = functools.partial(_fast, grid[1])
    else:
        body = functools.partial(per_device, None)
    return jax.shard_map(
        body, mesh=mesh, in_specs=placed, out_specs=P("vox"), check_vma=False
    )
```

```python
import functools

import jax
import jax.numpy as jnp
from jax import lax
from jax.sharding import PartitionSpec as P

CHUNKS = 4
RELAYS = 4


def _rows(a, blk, n):
    return lax.dynamic_slice_in_dim(a, blk * n, n, axis=0)


def _src_grid(mesh):
    devs = mesh.devices
    ax = mesh.axis_names.index("src")
    row = [devs[(i,) + (0,) * (devs.ndim - 1)] if ax == 0 else None for i in range(devs.shape[0])]
    if ax != 0 or any(not hasattr(d, "coords") for d in row):
        return None
    co = [tuple(d.coords) for d in row]
    n = len(co)
    diff = [k for k in range(len(co[0])) if n > 1 and co[1][k] != co[0][k]]
    if len(diff) != 1:
        return None
    nb = 1
    while nb < n and co[nb][diff[0]] != co[0][diff[0]]:
        nb += 1
    if n % nb:
        return None
    na = n // nb

    def near(i, j):
        return sum(abs(a - b) for a, b in zip(co[i], co[j])) == 1

    for i in range(n):
        ia, ib = divmod(i, nb)
        if ib + 1 < nb and not near(i, i + 1):
            return None
        if ia + 1 < na and not near(i, i + nb):
            return None
    if nb != 2 or na < 2:
        return None
    return nb, na


def _gather_src(block, grid):
    if grid is None:
        return lax.all_gather(block, "src", axis=0, tiled=True)
    nb, na = grid
    me = lax.axis_index("src")
    ia, ib = me // nb, me % nb
    swap = [(i, i ^ 1) for i in range(na * nb)]

    def along(p, d):
        return [(p * nb + o, d * nb + o) for o in range(nb)]

    got = {}
    for sign in (1, -1):
        cur = block
        for s in range(1, na):
            pairs = []
            for p in range(na):
                if 0 <= p + sign < na and 0 <= p - sign * (s - 1) < na:
                    pairs.extend(along(p, p + sign))
            cur = lax.ppermute(cur, "src", pairs)
            got[(sign, s)] = cur
    col = [block] + [
        jnp.where(ia + k < na, got[(-1, k)], got[(1, na - k)]) for k in range(1, na)
    ]
    col = jnp.stack(col)
    other = lax.ppermute(col, "src", swap)
    first = ib == 0
    planes = jnp.stack([jnp.where(first, col, other), jnp.where(first, other, col)], axis=1)
    return planes.reshape((-1,) + block.shape[1:])


def _sum_over_src(v):
    n = lax.axis_size("src")
    if n & (n - 1):
        return lax.psum(v, "src")
    b = 1
    while b < n:
        v = v + lax.ppermute(v, "src", [(i, i ^ b) for i in range(n)])
        b *= 2
    return v


def _zline(block, na):
    me = lax.axis_index("src")
    ia = me // 2

    def along(p, d):
        return [(p * 2 + o, d * 2 + o) for o in range(2)]

    got = {}
    for sign in (1, -1):
        cur = block
        for s in range(1, na):
            pairs = []
            for p in range(na):
                if 0 <= p + sign < na and 0 <= p - sign * (s - 1) < na:
                    pairs.extend(along(p, p + sign))
            cur = lax.ppermute(cur, "src", pairs)
            got[(sign, s)] = cur
    col = [block] + [
        jnp.where(ia + k < na, got[(-1, k)], got[(1, na - k)]) for k in range(1, na)
    ]
    return jnp.concatenate(col, axis=0)


def _fast(na, forward_voxel_field, adjoint_voxel_field, voxel_input_vector, measurement_weight):
    vox = lax.axis_size("vox")
    me = lax.axis_index("vox")
    m = vox // 2
    par = me % 2
    q = me // 2
    si = lax.axis_index("src")
    ia = si // 2
    first = si % 2 == 0
    sl, vl = forward_voxel_field.shape
    ds = adjoint_voxel_field.shape[0]
    chunks = CHUNKS if ds % (CHUNKS * 8) == 0 else 1
    r = ds // chunks
    swap = [(i, i ^ 1) for i in range(2 * na)]
    pair = [(j, j ^ 1) for j in range(vox)]

    def chip_perm(k):
        return [(g * 2 + p, ((g + k) % m) * 2 + p) for g in range(m) for p in range(2)]

    relays = RELAYS if chunks % RELAYS == 0 else 1
    hr = ds // relays
    per = chunks // relays

    def rows(col, blk):
        return lax.dynamic_slice(col, (((blk - ia) % na) * hr + (c % per) * r, 0), (r, vl))

    fwd = jnp.concatenate(
        [forward_voxel_field, lax.ppermute(forward_voxel_field, "src", swap)], axis=0
    )
    scaled = lax.optimization_barrier(
        (fwd.astype(jnp.float32) * voxel_input_vector[None, :]).astype(jnp.bfloat16)
    )
    weight = measurement_weight.reshape(sl, 2, ds)
    w_mine = jnp.where(first, weight[:, 0], weight[:, 1])
    w_other = jnp.where(first, weight[:, 1], weight[:, 0])
    weight = jnp.concatenate([w_mine, lax.ppermute(w_other, "src", swap)], axis=0)
    back = jnp.zeros((2 * sl, vl), jnp.float32)
    cols = [_zline(adjoint_voxel_field[h * hr:(h + 1) * hr], na) for h in range(relays)]
    for c in range(chunks):
        col = cols[c // per]

        def pblock(blk):
            return lax.dot_general(
                scaled, rows(col, blk), (((1,), (1,)), ((), ())),
                preferred_element_type=jnp.float32,
            )

        keeps = [pblock(2 * ((q + k) % m) + par) for k in range(m)]
        sends = [pblock(2 * ((q + k) % m) + 1 - par) for k in range(m)]
        halves = [a + b for a, b in zip(keeps, lax.ppermute(tuple(sends), "vox", pair))]
        share = halves[0]
        for k in range(1, m):
            share = share + lax.ppermute(
                halves[k].astype(jnp.bfloat16), "vox", chip_perm(k)
            ).astype(jnp.float32)

        piece = (weight[:, c * r:(c + 1) * r] * share).astype(jnp.bfloat16)

        got = [(me, piece)]
        for k in range(1, m):
            got.append((2 * ((q - k) % m) + par, lax.ppermute(piece, "vox", chip_perm(k))))
        mates = lax.ppermute(tuple(w for _, w in got), "vox", pair)
        got = got + [(blk ^ 1, w) for (blk, _), w in zip(got, mates)]
        back = back + jnp.dot(
            jnp.concatenate([w for _, w in got], axis=1),
            jnp.concatenate([rows(col, blk) for blk, _ in got], axis=0),
            preferred_element_type=jnp.float32,
        )

    local_sum = jnp.sum(fwd.astype(jnp.float32) * back, axis=0)
    return _sum_over_src(local_sum)


def per_device(grid, forward_voxel_field, adjoint_voxel_field, voxel_input_vector, measurement_weight):
    nsrc = lax.axis_size("src")
    vox = lax.axis_size("vox")
    me = lax.axis_index("vox")
    m = vox // 2
    par = me % 2
    q = me // 2
    t = nsrc // vox
    sl, vl = forward_voxel_field.shape
    ds = adjoint_voxel_field.shape[0]
    chunks = CHUNKS if ds % CHUNKS == 0 else 1
    r = ds // chunks
    n = t * r
    pair = [(j, j ^ 1) for j in range(vox)]

    def chip_perm(k):
        return [(g * 2 + p, ((g + k) % m) * 2 + p) for g in range(m) for p in range(2)]

    scaled = (forward_voxel_field.astype(jnp.float32) * voxel_input_vector[None, :]).astype(
        jnp.bfloat16
    )
    weight = measurement_weight.reshape(sl, t, ds)
    if grid is not None and grid[0] == t:
        na = grid[1]
        ia = lax.axis_index("src") // t

        def rel(blk):
            return (blk - ia) % na
    else:
        grid = None

        def rel(blk):
            return blk
    def gather(c):
        return _gather_src(adjoint_voxel_field[c * r:(c + 1) * r], grid)

    back = jnp.zeros((sl, vl), jnp.float32)
    nxt = gather(0)
    for c in range(chunks):
        adj = nxt

        def pblock(blk):
            return lax.dot_general(
                scaled, _rows(adj, rel(blk), n), (((1,), (1,)), ((), ())),
                preferred_element_type=jnp.float32,
            )

        keeps = [pblock(2 * ((q + k) % m) + par) for k in range(m)]
        sends = [pblock(2 * ((q + k) % m) + 1 - par) for k in range(m)]
        halves = [a + b for a, b in zip(keeps, lax.ppermute(tuple(sends), "vox", pair))]
        share = halves[0]
        for k in range(1, m):
            share = share + lax.ppermute(
                halves[k].astype(jnp.bfloat16), "vox", chip_perm(k)
            ).astype(jnp.float32)

        w_c = weight[:, :, c * r:(c + 1) * r].reshape(sl, n)
        wt = (w_c * share).astype(jnp.bfloat16)

        got = [(me, wt)]
        for k in range(1, m):
            got.append((2 * ((q - k) % m) + par, lax.ppermute(wt, "vox", chip_perm(k))))
        mine = lax.ppermute(tuple(w for _, w in got), "vox", pair)
        got = got + [(blk ^ 1, w) for (blk, _), w in zip(got, mine)]
        if c + 1 < chunks:
            nxt, ws = lax.optimization_barrier((gather(c + 1), [w for _, w in got]))
            got = [(blk, w) for (blk, _), w in zip(got, ws)]
        for blk, w in got:
            back = back + jnp.dot(w, _rows(adj, rel(blk), n), preferred_element_type=jnp.float32)

    local_sum = jnp.sum(forward_voxel_field.astype(jnp.float32) * back, axis=0)
    return _sum_over_src(local_sum)


def solution(mesh):
    placed = (P("src", "vox"), P("src", "vox"), P("vox"), P("src", "vox"))
    grid = _src_grid(mesh)
    nsrc, vox = mesh.shape["src"], mesh.shape["vox"]
    if grid is not None and grid[0] == 2 and nsrc == 2 * vox and vox % 2 == 0 and grid[1] == vox:
        body = functools.partial(_fast, grid[1])
    else:
        body = functools.partial(per_device, None)
    return jax.shard_map(
        body, mesh=mesh, in_specs=placed, out_specs=P("vox"), check_vma=False
    )
```

```python
import functools

import jax
import jax.numpy as jnp
from jax import lax
from jax.sharding import PartitionSpec as P

CHUNKS = 4
RELAY_SPLIT = (1, 3)


def _rows(a, blk, n):
    return lax.dynamic_slice_in_dim(a, blk * n, n, axis=0)


def _src_grid(mesh):
    devs = mesh.devices
    ax = mesh.axis_names.index("src")
    row = [devs[(i,) + (0,) * (devs.ndim - 1)] if ax == 0 else None for i in range(devs.shape[0])]
    if ax != 0 or any(not hasattr(d, "coords") for d in row):
        return None
    co = [tuple(d.coords) for d in row]
    n = len(co)
    diff = [k for k in range(len(co[0])) if n > 1 and co[1][k] != co[0][k]]
    if len(diff) != 1:
        return None
    nb = 1
    while nb < n and co[nb][diff[0]] != co[0][diff[0]]:
        nb += 1
    if n % nb:
        return None
    na = n // nb

    def near(i, j):
        return sum(abs(a - b) for a, b in zip(co[i], co[j])) == 1

    for i in range(n):
        ia, ib = divmod(i, nb)
        if ib + 1 < nb and not near(i, i + 1):
            return None
        if ia + 1 < na and not near(i, i + nb):
            return None
    if nb != 2 or na < 2:
        return None
    return nb, na


def _gather_src(block, grid):
    if grid is None:
        return lax.all_gather(block, "src", axis=0, tiled=True)
    nb, na = grid
    me = lax.axis_index("src")
    ia, ib = me // nb, me % nb
    swap = [(i, i ^ 1) for i in range(na * nb)]

    def along(p, d):
        return [(p * nb + o, d * nb + o) for o in range(nb)]

    got = {}
    for sign in (1, -1):
        cur = block
        for s in range(1, na):
            pairs = []
            for p in range(na):
                if 0 <= p + sign < na and 0 <= p - sign * (s - 1) < na:
                    pairs.extend(along(p, p + sign))
            cur = lax.ppermute(cur, "src", pairs)
            got[(sign, s)] = cur
    col = [block] + [
        jnp.where(ia + k < na, got[(-1, k)], got[(1, na - k)]) for k in range(1, na)
    ]
    col = jnp.stack(col)
    other = lax.ppermute(col, "src", swap)
    first = ib == 0
    planes = jnp.stack([jnp.where(first, col, other), jnp.where(first, other, col)], axis=1)
    return planes.reshape((-1,) + block.shape[1:])


def _sum_over_src(v):
    n = lax.axis_size("src")
    if n & (n - 1):
        return lax.psum(v, "src")
    b = 1
    while b < n:
        v = v + lax.ppermute(v, "src", [(i, i ^ b) for i in range(n)])
        b *= 2
    return v


def _zline(block, na):
    me = lax.axis_index("src")
    ia = me // 2

    def along(p, d):
        return [(p * 2 + o, d * 2 + o) for o in range(2)]

    got = {}
    for sign in (1, -1):
        cur = block
        for s in range(1, na):
            pairs = []
            for p in range(na):
                if 0 <= p + sign < na and 0 <= p - sign * (s - 1) < na:
                    pairs.extend(along(p, p + sign))
            cur = lax.ppermute(cur, "src", pairs)
            got[(sign, s)] = cur
    col = [block] + [
        jnp.where(ia + k < na, got[(-1, k)], got[(1, na - k)]) for k in range(1, na)
    ]
    return jnp.concatenate(col, axis=0)


def _fast(na, forward_voxel_field, adjoint_voxel_field, voxel_input_vector, measurement_weight):
    vox = lax.axis_size("vox")
    me = lax.axis_index("vox")
    m = vox // 2
    par = me % 2
    q = me // 2
    si = lax.axis_index("src")
    ia = si // 2
    first = si % 2 == 0
    sl, vl = forward_voxel_field.shape
    ds = adjoint_voxel_field.shape[0]
    chunks = CHUNKS if ds % (CHUNKS * 8) == 0 else 1
    r = ds // chunks
    swap = [(i, i ^ 1) for i in range(2 * na)]
    pair = [(j, j ^ 1) for j in range(vox)]

    def chip_perm(k):
        return [(g * 2 + p, ((g + k) % m) * 2 + p) for g in range(m) for p in range(2)]

    split = RELAY_SPLIT if sum(RELAY_SPLIT) == chunks else (chunks,)
    starts = [sum(split[:h]) for h in range(len(split))]
    part = [h for h, k in enumerate(split) for _ in range(k)]

    def rows(col, blk):
        h = part[c]
        return lax.dynamic_slice(
            col, (((blk - ia) % na) * split[h] * r + (c - starts[h]) * r, 0), (r, vl)
        )

    fwd = jnp.concatenate(
        [forward_voxel_field, lax.ppermute(forward_voxel_field, "src", swap)], axis=0
    )
    scaled = lax.optimization_barrier(
        (fwd.astype(jnp.float32) * voxel_input_vector[None, :]).astype(jnp.bfloat16)
    )
    weight = measurement_weight.reshape(sl, 2, ds)
    w_mine = jnp.where(first, weight[:, 0], weight[:, 1])
    w_other = jnp.where(first, weight[:, 1], weight[:, 0])
    weight = jnp.concatenate([w_mine, lax.ppermute(w_other, "src", swap)], axis=0)
    back = jnp.zeros((2 * sl, vl), jnp.float32)
    cols = [
        _zline(adjoint_voxel_field[s0 * r:(s0 + k) * r], na) for s0, k in zip(starts, split)
    ]
    for c in range(chunks):
        col = cols[part[c]]

        def pblock(blk):
            return lax.dot_general(
                scaled, rows(col, blk), (((1,), (1,)), ((), ())),
                preferred_element_type=jnp.float32,
            )

        keeps = [pblock(2 * ((q + k) % m) + par) for k in range(m)]
        sends = [pblock(2 * ((q + k) % m) + 1 - par) for k in range(m)]
        halves = [a + b for a, b in zip(keeps, lax.ppermute(tuple(sends), "vox", pair))]
        share = halves[0]
        for k in range(1, m):
            share = share + lax.ppermute(
                halves[k].astype(jnp.bfloat16), "vox", chip_perm(k)
            ).astype(jnp.float32)

        piece = (weight[:, c * r:(c + 1) * r] * share).astype(jnp.bfloat16)

        got = [(me, piece)]
        for k in range(1, m):
            got.append((2 * ((q - k) % m) + par, lax.ppermute(piece, "vox", chip_perm(k))))
        mates = lax.ppermute(tuple(w for _, w in got), "vox", pair)
        got = got + [(blk ^ 1, w) for (blk, _), w in zip(got, mates)]
        back = back + jnp.dot(
            jnp.concatenate([w for _, w in got], axis=1),
            jnp.concatenate([rows(col, blk) for blk, _ in got], axis=0),
            preferred_element_type=jnp.float32,
        )

    local_sum = jnp.sum(fwd.astype(jnp.float32) * back, axis=0)
    return _sum_over_src(local_sum)


def per_device(grid, forward_voxel_field, adjoint_voxel_field, voxel_input_vector, measurement_weight):
    nsrc = lax.axis_size("src")
    vox = lax.axis_size("vox")
    me = lax.axis_index("vox")
    m = vox // 2
    par = me % 2
    q = me // 2
    t = nsrc // vox
    sl, vl = forward_voxel_field.shape
    ds = adjoint_voxel_field.shape[0]
    chunks = CHUNKS if ds % CHUNKS == 0 else 1
    r = ds // chunks
    n = t * r
    pair = [(j, j ^ 1) for j in range(vox)]

    def chip_perm(k):
        return [(g * 2 + p, ((g + k) % m) * 2 + p) for g in range(m) for p in range(2)]

    scaled = (forward_voxel_field.astype(jnp.float32) * voxel_input_vector[None, :]).astype(
        jnp.bfloat16
    )
    weight = measurement_weight.reshape(sl, t, ds)
    if grid is not None and grid[0] == t:
        na = grid[1]
        ia = lax.axis_index("src") // t

        def rel(blk):
            return (blk - ia) % na
    else:
        grid = None

        def rel(blk):
            return blk
    def gather(c):
        return _gather_src(adjoint_voxel_field[c * r:(c + 1) * r], grid)

    back = jnp.zeros((sl, vl), jnp.float32)
    nxt = gather(0)
    for c in range(chunks):
        adj = nxt

        def pblock(blk):
            return lax.dot_general(
                scaled, _rows(adj, rel(blk), n), (((1,), (1,)), ((), ())),
                preferred_element_type=jnp.float32,
            )

        keeps = [pblock(2 * ((q + k) % m) + par) for k in range(m)]
        sends = [pblock(2 * ((q + k) % m) + 1 - par) for k in range(m)]
        halves = [a + b for a, b in zip(keeps, lax.ppermute(tuple(sends), "vox", pair))]
        share = halves[0]
        for k in range(1, m):
            share = share + lax.ppermute(
                halves[k].astype(jnp.bfloat16), "vox", chip_perm(k)
            ).astype(jnp.float32)

        w_c = weight[:, :, c * r:(c + 1) * r].reshape(sl, n)
        wt = (w_c * share).astype(jnp.bfloat16)

        got = [(me, wt)]
        for k in range(1, m):
            got.append((2 * ((q - k) % m) + par, lax.ppermute(wt, "vox", chip_perm(k))))
        mine = lax.ppermute(tuple(w for _, w in got), "vox", pair)
        got = got + [(blk ^ 1, w) for (blk, _), w in zip(got, mine)]
        if c + 1 < chunks:
            nxt, ws = lax.optimization_barrier((gather(c + 1), [w for _, w in got]))
            got = [(blk, w) for (blk, _), w in zip(got, ws)]
        for blk, w in got:
            back = back + jnp.dot(w, _rows(adj, rel(blk), n), preferred_element_type=jnp.float32)

    local_sum = jnp.sum(forward_voxel_field.astype(jnp.float32) * back, axis=0)
    return _sum_over_src(local_sum)


def solution(mesh):
    placed = (P("src", "vox"), P("src", "vox"), P("vox"), P("src", "vox"))
    grid = _src_grid(mesh)
    nsrc, vox = mesh.shape["src"], mesh.shape["vox"]
    if grid is not None and grid[0] == 2 and nsrc == 2 * vox and vox % 2 == 0 and grid[1] == vox:
        body = functools.partial(_fast, grid[1])
    else:
        body = functools.partial(per_device, None)
    return jax.shard_map(
        body, mesh=mesh, in_specs=placed, out_specs=P("vox"), check_vma=False
    )
```

```python
import functools

import jax
import jax.numpy as jnp
from jax import lax
from jax.sharding import PartitionSpec as P

CHUNKS = 4
RELAYS = 2


def _rows(a, blk, n):
    return lax.dynamic_slice_in_dim(a, blk * n, n, axis=0)


def _src_grid(mesh):
    devs = mesh.devices
    ax = mesh.axis_names.index("src")
    row = [devs[(i,) + (0,) * (devs.ndim - 1)] if ax == 0 else None for i in range(devs.shape[0])]
    if ax != 0 or any(not hasattr(d, "coords") for d in row):
        return None
    co = [tuple(d.coords) for d in row]
    n = len(co)
    diff = [k for k in range(len(co[0])) if n > 1 and co[1][k] != co[0][k]]
    if len(diff) != 1:
        return None
    nb = 1
    while nb < n and co[nb][diff[0]] != co[0][diff[0]]:
        nb += 1
    if n % nb:
        return None
    na = n // nb

    def near(i, j):
        return sum(abs(a - b) for a, b in zip(co[i], co[j])) == 1

    for i in range(n):
        ia, ib = divmod(i, nb)
        if ib + 1 < nb and not near(i, i + 1):
            return None
        if ia + 1 < na and not near(i, i + nb):
            return None
    if nb != 2 or na < 2:
        return None
    return nb, na


def _gather_src(block, grid):
    if grid is None:
        return lax.all_gather(block, "src", axis=0, tiled=True)
    nb, na = grid
    me = lax.axis_index("src")
    ia, ib = me // nb, me % nb
    swap = [(i, i ^ 1) for i in range(na * nb)]

    def along(p, d):
        return [(p * nb + o, d * nb + o) for o in range(nb)]

    got = {}
    for sign in (1, -1):
        cur = block
        for s in range(1, na):
            pairs = []
            for p in range(na):
                if 0 <= p + sign < na and 0 <= p - sign * (s - 1) < na:
                    pairs.extend(along(p, p + sign))
            cur = lax.ppermute(cur, "src", pairs)
            got[(sign, s)] = cur
    col = [block] + [
        jnp.where(ia + k < na, got[(-1, k)], got[(1, na - k)]) for k in range(1, na)
    ]
    col = jnp.stack(col)
    other = lax.ppermute(col, "src", swap)
    first = ib == 0
    planes = jnp.stack([jnp.where(first, col, other), jnp.where(first, other, col)], axis=1)
    return planes.reshape((-1,) + block.shape[1:])


def _sum_over_src(v):
    n = lax.axis_size("src")
    if n & (n - 1):
        return lax.psum(v, "src")
    b = 1
    while b < n:
        v = v + lax.ppermute(v, "src", [(i, i ^ b) for i in range(n)])
        b *= 2
    return v


def _zline(block, na):
    me = lax.axis_index("src")
    ia = me // 2

    def along(p, d):
        return [(p * 2 + o, d * 2 + o) for o in range(2)]

    got = {}
    for sign in (1, -1):
        cur = block
        for s in range(1, na):
            pairs = []
            for p in range(na):
                if 0 <= p + sign < na and 0 <= p - sign * (s - 1) < na:
                    pairs.extend(along(p, p + sign))
            cur = lax.ppermute(cur, "src", pairs)
            got[(sign, s)] = cur
    col = [block] + [
        jnp.where(ia + k < na, got[(-1, k)], got[(1, na - k)]) for k in range(1, na)
    ]
    return jnp.concatenate(col, axis=0)


def _fast(na, forward_voxel_field, adjoint_voxel_field, voxel_input_vector, measurement_weight):
    vox = lax.axis_size("vox")
    me = lax.axis_index("vox")
    m = vox // 2
    par = me % 2
    q = me // 2
    si = lax.axis_index("src")
    ia = si // 2
    first = si % 2 == 0
    sl, vl = forward_voxel_field.shape
    ds = adjoint_voxel_field.shape[0]
    chunks = CHUNKS if ds % (CHUNKS * 8) == 0 else 1
    r = ds // chunks
    swap = [(i, i ^ 1) for i in range(2 * na)]
    pair = [(j, j ^ 1) for j in range(vox)]

    def chip_perm(k):
        return [(g * 2 + p, ((g + k) % m) * 2 + p) for g in range(m) for p in range(2)]

    relays = RELAYS if chunks % RELAYS == 0 else 1
    hr = ds // relays
    per = chunks // relays

    def rows(col, blk):
        return lax.dynamic_slice(col, (((blk - ia) % na) * hr + (c % per) * r, 0), (r, vl))

    fwd = jnp.concatenate(
        [forward_voxel_field, lax.ppermute(forward_voxel_field, "src", swap)], axis=0
    )
    scaled = lax.optimization_barrier(
        (fwd.astype(jnp.float32) * voxel_input_vector[None, :]).astype(jnp.bfloat16)
    )
    weight = measurement_weight.reshape(sl, 2, ds)
    w_mine = jnp.where(first, weight[:, 0], weight[:, 1])
    w_other = jnp.where(first, weight[:, 1], weight[:, 0])
    weight = jnp.concatenate([w_mine, lax.ppermute(w_other, "src", swap)], axis=0)
    back = jnp.zeros((2 * sl, vl), jnp.float32)
    cols = [_zline(adjoint_voxel_field[h * hr:(h + 1) * hr], na) for h in range(relays)]
    for c in range(chunks):
        col = cols[c // per]

        def pblock(blk):
            return lax.dot_general(
                scaled, rows(col, blk), (((1,), (1,)), ((), ())),
                preferred_element_type=jnp.float32,
            )

        keeps = [pblock(2 * ((q + k) % m) + par) for k in range(m)]
        sends = [pblock(2 * ((q + k) % m) + 1 - par) for k in range(m)]
        sends = tuple(x.astype(jnp.bfloat16) for x in sends)
        halves = [
            a + b.astype(jnp.float32) for a, b in zip(keeps, lax.ppermute(sends, "vox", pair))
        ]
        share = halves[0]
        for k in range(1, m):
            share = share + lax.ppermute(
                halves[k].astype(jnp.bfloat16), "vox", chip_perm(k)
            ).astype(jnp.float32)

        piece = (weight[:, c * r:(c + 1) * r] * share).astype(jnp.bfloat16)

        got = [(me, piece)]
        for k in range(1, m):
            got.append((2 * ((q - k) % m) + par, lax.ppermute(piece, "vox", chip_perm(k))))
        mates = lax.ppermute(tuple(w for _, w in got), "vox", pair)
        got = got + [(blk ^ 1, w) for (blk, _), w in zip(got, mates)]
        back = back + jnp.dot(
            jnp.concatenate([w for _, w in got], axis=1),
            jnp.concatenate([rows(col, blk) for blk, _ in got], axis=0),
            preferred_element_type=jnp.float32,
        )

    local_sum = jnp.sum(fwd.astype(jnp.float32) * back, axis=0)
    return _sum_over_src(local_sum)


def per_device(grid, forward_voxel_field, adjoint_voxel_field, voxel_input_vector, measurement_weight):
    nsrc = lax.axis_size("src")
    vox = lax.axis_size("vox")
    me = lax.axis_index("vox")
    m = vox // 2
    par = me % 2
    q = me // 2
    t = nsrc // vox
    sl, vl = forward_voxel_field.shape
    ds = adjoint_voxel_field.shape[0]
    chunks = CHUNKS if ds % CHUNKS == 0 else 1
    r = ds // chunks
    n = t * r
    pair = [(j, j ^ 1) for j in range(vox)]

    def chip_perm(k):
        return [(g * 2 + p, ((g + k) % m) * 2 + p) for g in range(m) for p in range(2)]

    scaled = (forward_voxel_field.astype(jnp.float32) * voxel_input_vector[None, :]).astype(
        jnp.bfloat16
    )
    weight = measurement_weight.reshape(sl, t, ds)
    if grid is not None and grid[0] == t:
        na = grid[1]
        ia = lax.axis_index("src") // t

        def rel(blk):
            return (blk - ia) % na
    else:
        grid = None

        def rel(blk):
            return blk
    def gather(c):
        return _gather_src(adjoint_voxel_field[c * r:(c + 1) * r], grid)

    back = jnp.zeros((sl, vl), jnp.float32)
    nxt = gather(0)
    for c in range(chunks):
        adj = nxt

        def pblock(blk):
            return lax.dot_general(
                scaled, _rows(adj, rel(blk), n), (((1,), (1,)), ((), ())),
                preferred_element_type=jnp.float32,
            )

        keeps = [pblock(2 * ((q + k) % m) + par) for k in range(m)]
        sends = [pblock(2 * ((q + k) % m) + 1 - par) for k in range(m)]
        halves = [a + b for a, b in zip(keeps, lax.ppermute(tuple(sends), "vox", pair))]
        share = halves[0]
        for k in range(1, m):
            share = share + lax.ppermute(
                halves[k].astype(jnp.bfloat16), "vox", chip_perm(k)
            ).astype(jnp.float32)

        w_c = weight[:, :, c * r:(c + 1) * r].reshape(sl, n)
        wt = (w_c * share).astype(jnp.bfloat16)

        got = [(me, wt)]
        for k in range(1, m):
            got.append((2 * ((q - k) % m) + par, lax.ppermute(wt, "vox", chip_perm(k))))
        mine = lax.ppermute(tuple(w for _, w in got), "vox", pair)
        got = got + [(blk ^ 1, w) for (blk, _), w in zip(got, mine)]
        if c + 1 < chunks:
            nxt, ws = lax.optimization_barrier((gather(c + 1), [w for _, w in got]))
            got = [(blk, w) for (blk, _), w in zip(got, ws)]
        for blk, w in got:
            back = back + jnp.dot(w, _rows(adj, rel(blk), n), preferred_element_type=jnp.float32)

    local_sum = jnp.sum(forward_voxel_field.astype(jnp.float32) * back, axis=0)
    return _sum_over_src(local_sum)


def solution(mesh):
    placed = (P("src", "vox"), P("src", "vox"), P("vox"), P("src", "vox"))
    grid = _src_grid(mesh)
    nsrc, vox = mesh.shape["src"], mesh.shape["vox"]
    if grid is not None and grid[0] == 2 and nsrc == 2 * vox and vox % 2 == 0 and grid[1] == vox:
        body = functools.partial(_fast, grid[1])
    else:
        body = functools.partial(per_device, None)
    return jax.shard_map(
        body, mesh=mesh, in_specs=placed, out_specs=P("vox"), check_vma=False
    )
```

```python
import functools

import jax
import jax.numpy as jnp
from jax import lax
from jax.sharding import PartitionSpec as P

CHUNKS = 4
RELAYS = 2


def _rows(a, blk, n):
    return lax.dynamic_slice_in_dim(a, blk * n, n, axis=0)


def _src_grid(mesh):
    devs = mesh.devices
    ax = mesh.axis_names.index("src")
    row = [devs[(i,) + (0,) * (devs.ndim - 1)] if ax == 0 else None for i in range(devs.shape[0])]
    if ax != 0 or any(not hasattr(d, "coords") for d in row):
        return None
    co = [tuple(d.coords) for d in row]
    n = len(co)
    diff = [k for k in range(len(co[0])) if n > 1 and co[1][k] != co[0][k]]
    if len(diff) != 1:
        return None
    nb = 1
    while nb < n and co[nb][diff[0]] != co[0][diff[0]]:
        nb += 1
    if n % nb:
        return None
    na = n // nb

    def near(i, j):
        return sum(abs(a - b) for a, b in zip(co[i], co[j])) == 1

    for i in range(n):
        ia, ib = divmod(i, nb)
        if ib + 1 < nb and not near(i, i + 1):
            return None
        if ia + 1 < na and not near(i, i + nb):
            return None
    if nb != 2 or na < 2:
        return None
    return nb, na


def _gather_src(block, grid):
    if grid is None:
        return lax.all_gather(block, "src", axis=0, tiled=True)
    nb, na = grid
    me = lax.axis_index("src")
    ia, ib = me // nb, me % nb
    swap = [(i, i ^ 1) for i in range(na * nb)]

    def along(p, d):
        return [(p * nb + o, d * nb + o) for o in range(nb)]

    got = {}
    for sign in (1, -1):
        cur = block
        for s in range(1, na):
            pairs = []
            for p in range(na):
                if 0 <= p + sign < na and 0 <= p - sign * (s - 1) < na:
                    pairs.extend(along(p, p + sign))
            cur = lax.ppermute(cur, "src", pairs)
            got[(sign, s)] = cur
    col = [block] + [
        jnp.where(ia + k < na, got[(-1, k)], got[(1, na - k)]) for k in range(1, na)
    ]
    col = jnp.stack(col)
    other = lax.ppermute(col, "src", swap)
    first = ib == 0
    planes = jnp.stack([jnp.where(first, col, other), jnp.where(first, other, col)], axis=1)
    return planes.reshape((-1,) + block.shape[1:])


def _sum_over_src(v):
    n = lax.axis_size("src")
    if n & (n - 1):
        return lax.psum(v, "src")
    b = 1
    while b < n:
        v = v + lax.ppermute(v, "src", [(i, i ^ b) for i in range(n)])
        b *= 2
    return v


def _zline(block, na):
    me = lax.axis_index("src")
    ia = me // 2

    def along(p, d):
        return [(p * 2 + o, d * 2 + o) for o in range(2)]

    got = {}
    for sign in (1, -1):
        cur = block
        for s in range(1, na):
            pairs = []
            for p in range(na):
                if 0 <= p + sign < na and 0 <= p - sign * (s - 1) < na:
                    pairs.extend(along(p, p + sign))
            cur = lax.ppermute(cur, "src", pairs)
            got[(sign, s)] = cur
    col = [block] + [
        jnp.where(ia + k < na, got[(-1, k)], got[(1, na - k)]) for k in range(1, na)
    ]
    return jnp.concatenate(col, axis=0)


def _fast(na, forward_voxel_field, adjoint_voxel_field, voxel_input_vector, measurement_weight):
    vox = lax.axis_size("vox")
    me = lax.axis_index("vox")
    m = vox // 2
    par = me % 2
    q = me // 2
    si = lax.axis_index("src")
    ia = si // 2
    first = si % 2 == 0
    sl, vl = forward_voxel_field.shape
    ds = adjoint_voxel_field.shape[0]
    chunks = CHUNKS if ds % (CHUNKS * 8) == 0 else 1
    r = ds // chunks
    swap = [(i, i ^ 1) for i in range(2 * na)]
    pair = [(j, j ^ 1) for j in range(vox)]

    def chip_perm(k):
        return [(g * 2 + p, ((g + k) % m) * 2 + p) for g in range(m) for p in range(2)]

    relays = RELAYS if chunks % RELAYS == 0 else 1
    hr = ds // relays
    per = chunks // relays

    def rows(col, blk):
        return lax.dynamic_slice(col, (((blk - ia) % na) * hr + (c % per) * r, 0), (r, vl))

    fwd = jnp.concatenate(
        [forward_voxel_field, lax.ppermute(forward_voxel_field, "src", swap)], axis=0
    )
    scaled = lax.optimization_barrier(
        (fwd.astype(jnp.float32) * voxel_input_vector[None, :]).astype(jnp.bfloat16)
    )
    weight = measurement_weight.reshape(sl, 2, ds)
    w_mine = jnp.where(first, weight[:, 0], weight[:, 1])
    w_other = jnp.where(first, weight[:, 1], weight[:, 0])
    weight = jnp.concatenate([w_mine, lax.ppermute(w_other, "src", swap)], axis=0)
    back = jnp.zeros((2 * sl, vl), jnp.float32)
    cols = [_zline(adjoint_voxel_field[h * hr:(h + 1) * hr], na) for h in range(relays)]
    for c in range(chunks):
        col = cols[c // per]

        def pblock(blk):
            return lax.dot_general(
                scaled, rows(col, blk), (((1,), (1,)), ((), ())),
                preferred_element_type=jnp.float32,
            )

        keeps = [pblock(2 * ((q + k) % m) + par) for k in range(m)]
        sends = [pblock(2 * ((q + k) % m) + 1 - par) for k in range(m)]
        halves = [a + b for a, b in zip(keeps, lax.ppermute(tuple(sends), "vox", pair))]
        share = halves[0]
        for k in range(1, m):
            share = share + lax.ppermute(
                halves[k].astype(jnp.bfloat16), "vox", chip_perm(k)
            ).astype(jnp.float32)

        piece = (weight[:, c * r:(c + 1) * r] * share).astype(jnp.bfloat16)

        got = [(me, piece)]
        for k in range(1, m):
            got.append((2 * ((q - k) % m) + par, lax.ppermute(piece, "vox", chip_perm(k))))
        mates = lax.ppermute(jnp.stack([w for _, w in got]), "vox", pair)
        got = got + [(blk ^ 1, mates[i]) for i, (blk, _) in enumerate(got)]
        back = back + jnp.dot(
            jnp.concatenate([w for _, w in got], axis=1),
            jnp.concatenate([rows(col, blk) for blk, _ in got], axis=0),
            preferred_element_type=jnp.float32,
        )

    local_sum = jnp.sum(fwd.astype(jnp.float32) * back, axis=0)
    return _sum_over_src(local_sum)


def per_device(grid, forward_voxel_field, adjoint_voxel_field, voxel_input_vector, measurement_weight):
    nsrc = lax.axis_size("src")
    vox = lax.axis_size("vox")
    me = lax.axis_index("vox")
    m = vox // 2
    par = me % 2
    q = me // 2
    t = nsrc // vox
    sl, vl = forward_voxel_field.shape
    ds = adjoint_voxel_field.shape[0]
    chunks = CHUNKS if ds % CHUNKS == 0 else 1
    r = ds // chunks
    n = t * r
    pair = [(j, j ^ 1) for j in range(vox)]

    def chip_perm(k):
        return [(g * 2 + p, ((g + k) % m) * 2 + p) for g in range(m) for p in range(2)]

    scaled = (forward_voxel_field.astype(jnp.float32) * voxel_input_vector[None, :]).astype(
        jnp.bfloat16
    )
    weight = measurement_weight.reshape(sl, t, ds)
    if grid is not None and grid[0] == t:
        na = grid[1]
        ia = lax.axis_index("src") // t

        def rel(blk):
            return (blk - ia) % na
    else:
        grid = None

        def rel(blk):
            return blk
    def gather(c):
        return _gather_src(adjoint_voxel_field[c * r:(c + 1) * r], grid)

    back = jnp.zeros((sl, vl), jnp.float32)
    nxt = gather(0)
    for c in range(chunks):
        adj = nxt

        def pblock(blk):
            return lax.dot_general(
                scaled, _rows(adj, rel(blk), n), (((1,), (1,)), ((), ())),
                preferred_element_type=jnp.float32,
            )

        keeps = [pblock(2 * ((q + k) % m) + par) for k in range(m)]
        sends = [pblock(2 * ((q + k) % m) + 1 - par) for k in range(m)]
        halves = [a + b for a, b in zip(keeps, lax.ppermute(tuple(sends), "vox", pair))]
        share = halves[0]
        for k in range(1, m):
            share = share + lax.ppermute(
                halves[k].astype(jnp.bfloat16), "vox", chip_perm(k)
            ).astype(jnp.float32)

        w_c = weight[:, :, c * r:(c + 1) * r].reshape(sl, n)
        wt = (w_c * share).astype(jnp.bfloat16)

        got = [(me, wt)]
        for k in range(1, m):
            got.append((2 * ((q - k) % m) + par, lax.ppermute(wt, "vox", chip_perm(k))))
        mine = lax.ppermute(tuple(w for _, w in got), "vox", pair)
        got = got + [(blk ^ 1, w) for (blk, _), w in zip(got, mine)]
        if c + 1 < chunks:
            nxt, ws = lax.optimization_barrier((gather(c + 1), [w for _, w in got]))
            got = [(blk, w) for (blk, _), w in zip(got, ws)]
        for blk, w in got:
            back = back + jnp.dot(w, _rows(adj, rel(blk), n), preferred_element_type=jnp.float32)

    local_sum = jnp.sum(forward_voxel_field.astype(jnp.float32) * back, axis=0)
    return _sum_over_src(local_sum)


def solution(mesh):
    placed = (P("src", "vox"), P("src", "vox"), P("vox"), P("src", "vox"))
    grid = _src_grid(mesh)
    nsrc, vox = mesh.shape["src"], mesh.shape["vox"]
    if grid is not None and grid[0] == 2 and nsrc == 2 * vox and vox % 2 == 0 and grid[1] == vox:
        body = functools.partial(_fast, grid[1])
    else:
        body = functools.partial(per_device, None)
    return jax.shard_map(
        body, mesh=mesh, in_specs=placed, out_specs=P("vox"), check_vma=False
    )
```
